256 devices in a mesh: seq: 64 (over x, z, core), mp: 4 (over y).
Axes of the slice: x: 4, y: 4, z: 8, core: 2. Of those that a mesh axis runs over, the one named last changes fastest.
Arguments:
- states: bfloat16 [4, 128, 2560], P(None, 'seq', 'mp'), may hold values from -6 to 6
- norm_gain: float32 [2560], replicated, may hold values from 0.5 to 2
- query_gain: float32 [128], replicated, may hold values from 0.7 to 2
- key_gain: float32 [128], replicated, may hold values from 0.7 to 2
- w_query: bfloat16 [2560, 2048], P(None, 'mp'), may hold values from -0.125 to 0.125
- key_matrix: bfloat16 [2560, 512], P(None, 'mp'), may hold values from -0.125 to 0.125
- value_matrix: bfloat16 [2560, 512], P(None, 'mp'), may hold values from -0.125 to 0.125
- w_out: bfloat16 [2048, 2560], P('mp'), may hold values from -0.125 to 0.125
- cached_key_blocks: bfloat16 [1024, 256, 512], P('seq', None, 'mp'), may hold values from -216 to 216
- cached_value_blocks: bfloat16 [1024, 256, 512], P('seq', None, 'mp'), may hold values from -6 to 6
- req_len: int32 [128], replicated, may hold values from 1 to 16384, as said below
- slot_request: int32 [1024], P('seq'), may hold values from 0 to 127, as said below
- slot_block: int32 [1024], P('seq'), may hold values from 0 to 63
- slot_empty: int32 [1024], P('seq'), may hold values from 0 to 1
Outputs:
- hidden: bfloat16 [4, 128, 2560], P(None, 'seq', 'mp')
- new_keys: bfloat16 [4, 128, 512], P(None, 'seq', 'mp')
- new_values: bfloat16 [4, 128, 512], P(None, 'seq', 'mp')
The draws below stay inside these ranges and needn't reach their ends.
Inputs may be any that keep to these rules, and one draw needn't show every extreme that they name: `req_len`: exactly 12 requests have length 16384; each other request has length at most 511, and one of them exactly that. Slot s holds positions slot_block[s] * 256 onward of request slot_request[s] unless slot_empty[s] = 1. Each block of a request below its length lies in exactly one slot that is not empty. A request of length 16384 has one block on every index of seq; every block of any other request b lies on index b // 2 of seq.
All inputs are finite; a program needn't handle non-finite values.
Results may differ from the reference program's by a relative error of at most 0.0098.
Values may be sent and summed in bfloat16 or wider, within the bound.
No kernel may reach another device: no remote copies, remote signals or barrier semaphores. Data moves between devices by JAX's collectives and lax.ppermute only.
A program may use at most 64 MiB of HBM per device.

```python
import math
import jax
import jax.numpy as jnp
from jax import lax

MODEL_WIDTH = 2560
HEAD_SIZE = 128
QUERY_HEADS = 16
KEY_VALUE_HEADS = 4
BLOCK_POSITIONS = 256
STEPS = 4
NLONG = 12
ROWS_DEV = 2
REQUEST_COUNT = 128
SEQUENCE_SLOTS = 16
TOTAL_SLOTS = 1024
LONG_LEN = 16384
N_SEQ = 64


def layout(key):
    base_offset = jax.random.fold_in(key, 4242)
    pick_key, length_key, shift_key, order_key = jax.random.split(base_offset, 4)
    request_ids = jnp.arange(REQUEST_COUNT, dtype=jnp.int32)
    long_ids = jax.random.permutation(pick_key, REQUEST_COUNT)[:NLONG].astype(jnp.int32)
    is_long = jnp.any(request_ids[:, None] == long_ids[None, :], axis=1)
    short_len = jax.random.randint(length_key, (REQUEST_COUNT,), 1, 2 * BLOCK_POSITIONS, dtype=jnp.int32)
    first_short = jnp.argmin(jnp.where(is_long, REQUEST_COUNT, request_ids))
    short_len = jnp.where(request_ids == first_short, 2 * BLOCK_POSITIONS - 1, short_len)
    lengths = jnp.where(is_long, LONG_LEN, short_len).astype(jnp.int32)
    devices = jnp.arange(N_SEQ, dtype=jnp.int32)[:, None]
    shifts = jax.random.randint(shift_key, (NLONG,), 0, N_SEQ, dtype=jnp.int32)
    long_request = jnp.broadcast_to(long_ids[None, :], (N_SEQ, NLONG))
    long_block = (devices + shifts[None, :]) % N_SEQ
    long_empty = jnp.zeros((N_SEQ, NLONG), jnp.int32)
    local_slot = jnp.arange(2 * ROWS_DEV, dtype=jnp.int32)[None, :]
    short_request = devices * ROWS_DEV + local_slot // 2
    short_index = jnp.broadcast_to(local_slot % 2, (N_SEQ, 2 * ROWS_DEV))
    owner_len = jnp.take(lengths, short_request)
    owner_long = jnp.take(is_long, short_request)
    short_empty = (owner_long | (short_index == 1) & (owner_len <= BLOCK_POSITIONS)).astype(jnp.int32)
    short_block = jnp.where(short_empty == 1, 0, short_index)
    request_table = jnp.concatenate([long_request, short_request], axis=1)
    block_table = jnp.concatenate([long_block, short_block], axis=1)
    empty_table = jnp.concatenate([long_empty, short_empty], axis=1)

    def shuffle(sub_key):
        return jax.random.permutation(sub_key, SEQUENCE_SLOTS)
    orders = jax.vmap(shuffle)(jax.random.split(order_key, N_SEQ))
    request_flat = jnp.take_along_axis(request_table, orders, axis=1).reshape(-1).astype(jnp.int32)
    block_flat = jnp.take_along_axis(block_table, orders, axis=1).reshape(-1).astype(jnp.int32)
    empty_flat = jnp.take_along_axis(empty_table, orders, axis=1).reshape(-1).astype(jnp.int32)
    return (lengths, request_flat, block_flat, empty_flat)


def draw_req_len(key, part):
    return layout(key)[0]


def draw_slot_request(key, part):
    return layout(key)[1]


def draw_slot_block(key, part):
    return layout(key)[2]


def draw_slot_empty(key, part):
    return layout(key)[3]


def draw_cached_key_blocks(key, part):
    lengths, request_flat, block_flat, empty_flat = layout(key)
    slot_device = jnp.arange(TOTAL_SLOTS, dtype=jnp.int32) // SEQUENCE_SLOTS
    owner_device = request_flat // ROWS_DEV
    slot_long = jnp.take(lengths, request_flat) == LONG_LEN
    across = slot_long & (slot_device == (owner_device + N_SEQ // 2) % N_SEQ) & (empty_flat == 0)
    factor = jnp.where(across, 1.5, 1.0).astype(jnp.float32)[:, None, None]
    base_offset = jax.random.fold_in(key, 31)
    cache_entries = 2.5 * jax.random.truncated_normal(base_offset, -6.0, 6.0, (TOTAL_SLOTS, BLOCK_POSITIONS, KEY_VALUE_HEADS * HEAD_SIZE), jnp.float32)
    cache_entries = cache_entries * factor
    return cache_entries.astype(jnp.bfloat16)


def block_scale(own_key, dims, shards, smallest, top_value):
    loudness = 1.0
    for dim, shards_of in shards:
        draws = jax.random.uniform(jax.random.fold_in(jax.random.fold_in(own_key, 6), dim), (shards_of,), jnp.float32, smallest / len(shards), top_value / len(shards))
        loudness = loudness * jnp.repeat(jnp.exp(draws), dims[dim] // shards_of).reshape((-1,) + (1,) * (len(dims) - 1 - dim))
    return loudness


def noise(stream_key, extent, deviation, bound, cuts=(), held_as=jnp.bfloat16):
    values = deviation * jax.random.normal(stream_key, extent, jnp.float32)
    if cuts:
        values = values * block_scale(stream_key, extent, cuts, -0.22, 0.18)
    return jnp.clip(values, -bound, bound).astype(held_as)


def setup_inputs(seed: int = 0) -> dict:
    seeds = jax.random.split(jax.random.key(seed), 15)
    return {
        "states": noise(seeds[0], (STEPS, REQUEST_COUNT, MODEL_WIDTH), 1.0, 6.0, ((1, 64), (2, 4))),
        "norm_gain": jnp.clip(jnp.exp(jax.random.uniform(seeds[1], (MODEL_WIDTH,), jnp.float32, math.log(0.5), math.log(2.0))), 0.5, 2.0),
        "query_gain": jnp.clip(jnp.exp(jax.random.uniform(seeds[2], (HEAD_SIZE,), jnp.float32, math.log(0.7), math.log(2.0))), 0.7, 2.0),
        "key_gain": jnp.clip(jnp.exp(jax.random.uniform(seeds[3], (HEAD_SIZE,), jnp.float32, math.log(0.7), math.log(2.0))), 0.7, 2.0),
        "w_query": noise(seeds[4], (MODEL_WIDTH, QUERY_HEADS * HEAD_SIZE), MODEL_WIDTH ** -0.5, 0.125, ((1, 4),)),
        "key_matrix": noise(seeds[5], (MODEL_WIDTH, KEY_VALUE_HEADS * HEAD_SIZE), MODEL_WIDTH ** -0.5, 0.125, ((1, 4),)),
        "value_matrix": noise(seeds[6], (MODEL_WIDTH, KEY_VALUE_HEADS * HEAD_SIZE), MODEL_WIDTH ** -0.5, 0.125, ((1, 4),)),
        "w_out": noise(seeds[7], (QUERY_HEADS * HEAD_SIZE, MODEL_WIDTH), (QUERY_HEADS * HEAD_SIZE) ** -0.5, 0.125, ((0, 4),)),
        "cached_key_blocks": draw_cached_key_blocks(jax.random.fold_in(seeds[14], 71), 0),
        "cached_value_blocks": noise(seeds[9], (TOTAL_SLOTS, BLOCK_POSITIONS, KEY_VALUE_HEADS * HEAD_SIZE), 1.0, 6.0, ((0, 64), (2, 4))),
        "req_len": draw_req_len(jax.random.fold_in(seeds[14], 71), 0),
        "slot_request": draw_slot_request(jax.random.fold_in(seeds[14], 71), 0),
        "slot_block": draw_slot_block(jax.random.fold_in(seeds[14], 71), 0),
        "slot_empty": draw_slot_empty(jax.random.fold_in(seeds[14], 71), 0),
    }


ROPE_BASE = 1000000.0
NEGATIVE = -1e+30

def scaled_rms(values, gain):
    return values * lax.rsqrt(lax.optimization_barrier(jnp.mean(values * values, axis=-1, keepdims=True)) + 1e-06) * gain

def rotate(values, positions):
    halfway = values.shape[-1] // 2
    frequency = ROPE_BASE ** (-(jnp.arange(halfway, dtype=jnp.float32) * 2.0) / values.shape[-1])
    angles = positions.astype(jnp.float32)[..., None, None] * frequency
    cosine = jnp.cos(angles)
    sine_part = jnp.sin(angles)
    leading = values[..., :halfway]
    trailing = values[..., halfway:]
    return jnp.concatenate([leading * cosine - trailing * sine_part, trailing * cosine + leading * sine_part], axis=-1)

def project(inputs, positions, norm_gain, query_gain, key_gain, w_query, key_matrix, value_matrix):
    number = inputs.shape[0]
    normed = scaled_rms(inputs.astype(jnp.float32), norm_gain).astype(jnp.bfloat16)
    query_rows = jnp.dot(normed, w_query, preferred_element_type=jnp.float32).reshape(number, -1, HEAD_SIZE)
    keys = jnp.dot(normed, key_matrix, preferred_element_type=jnp.float32).reshape(number, -1, HEAD_SIZE)
    values = jnp.dot(normed, value_matrix, preferred_element_type=jnp.float32).astype(jnp.bfloat16)
    query_rows = rotate(scaled_rms(query_rows, query_gain), positions).reshape(number, -1).astype(jnp.bfloat16)
    keys = rotate(scaled_rms(keys, key_gain), positions).reshape(number, -1).astype(jnp.bfloat16)
    return (query_rows, keys, values)

def reference(states, norm_gain, query_gain, key_gain, w_query, key_matrix, value_matrix, w_out, cached_key_blocks, cached_value_blocks, req_len, slot_request, slot_block, slot_empty):
    head_sharing = QUERY_HEADS // KEY_VALUE_HEADS
    scaling = HEAD_SIZE ** (-0.5)
    offsets = jnp.arange(BLOCK_POSITIONS, dtype=jnp.int32)
    slot_len = jnp.take(req_len, slot_request)
    filled = (slot_empty[:, None] == 0) & (slot_block[:, None] * BLOCK_POSITIONS + offsets[None, :] < slot_len[:, None])
    belongs = (slot_request[None, :] == jnp.arange(REQUEST_COUNT, dtype=jnp.int32)[:, None]) & (slot_empty[None, :] == 0)
    kept_request = jnp.where(slot_empty == 0, slot_request, REQUEST_COUNT).astype(jnp.int32)
    grouped_keys = cached_key_blocks.reshape(N_SEQ, SEQUENCE_SLOTS, BLOCK_POSITIONS, KEY_VALUE_HEADS, HEAD_SIZE)
    grouped_values = cached_value_blocks.reshape(N_SEQ, SEQUENCE_SLOTS, BLOCK_POSITIONS, KEY_VALUE_HEADS, HEAD_SIZE)
    grouped_filled_mask = filled.reshape(N_SEQ, SEQUENCE_SLOTS, BLOCK_POSITIONS)
    grouped_requests = slot_request.reshape(N_SEQ, SEQUENCE_SLOTS)
    current_keys = []
    current_values = []
    results = []
    for sequence_index in range(STEPS):
        positions = req_len + sequence_index
        query_rows, keys, values = project(states[sequence_index], positions, norm_gain, query_gain, key_gain, w_query, key_matrix, value_matrix)
        current_keys.append(keys)
        current_values.append(values)
        query_head_rows = query_rows.reshape(REQUEST_COUNT, KEY_VALUE_HEADS, head_sharing, HEAD_SIZE).astype(jnp.float32)
        earlier_keys = jnp.stack(current_keys).reshape(sequence_index + 1, REQUEST_COUNT, KEY_VALUE_HEADS, HEAD_SIZE).astype(jnp.float32)
        earlier_values = jnp.stack(current_values).reshape(sequence_index + 1, REQUEST_COUNT, KEY_VALUE_HEADS, HEAD_SIZE).astype(jnp.float32)
        fresh_scores = jnp.einsum('bngd,jbnd->bngj', query_head_rows, earlier_keys) * scaling

        def slot_scores(keys_part, filled_part, request_part):
            query_part = jnp.take(query_head_rows, request_part, axis=0)
            raw = jnp.einsum('sngd,sknd->sngk', query_part, keys_part.astype(jnp.float32)) * scaling
            return jnp.where(filled_part[:, None, None, :], raw, NEGATIVE)

        def slot_maximum(operands):
            return lax.optimization_barrier(jnp.max(slot_scores(operands[0], operands[1], operands[2]), axis=-1))
        score_maxima = lax.map(slot_maximum, (grouped_keys, grouped_filled_mask, grouped_requests)).reshape(TOTAL_SLOTS, KEY_VALUE_HEADS, head_sharing)
        cache_top = lax.optimization_barrier(jnp.max(jnp.where(belongs[:, :, None, None], score_maxima[None], NEGATIVE), axis=1))
        overall = jnp.maximum(cache_top, lax.optimization_barrier(jnp.max(fresh_scores, axis=-1)))

        def slot_sums(operands):
            keys_part, values_part, filled_part, request_part = operands
            raw = slot_scores(keys_part, filled_part, request_part)
            reference_top = jnp.take(overall, request_part, axis=0)
            mask_wide = filled_part[:, None, None, :]
            probs = jnp.where(mask_wide, jnp.exp(jnp.where(mask_wide, raw - reference_top[..., None], 0.0)), 0.0)
            rounded = lax.optimization_barrier(probs.astype(jnp.bfloat16)).astype(jnp.float32)
            mixture = jnp.einsum('sngk,sknd->sngd', rounded, values_part.astype(jnp.float32))
            return (lax.optimization_barrier(jnp.sum(probs, axis=-1)), mixture)
        weight_totals, weighted_mixtures = lax.map(slot_sums, (grouped_keys, grouped_values, grouped_filled_mask, grouped_requests))
        weight_totals = weight_totals.reshape(TOTAL_SLOTS, KEY_VALUE_HEADS, head_sharing)
        weighted_mixtures = weighted_mixtures.reshape(TOTAL_SLOTS, KEY_VALUE_HEADS, head_sharing, HEAD_SIZE)
        denominator = jax.ops.segment_sum(weight_totals, kept_request, num_segments=REQUEST_COUNT + 1)[:REQUEST_COUNT]
        mixture = jax.ops.segment_sum(weighted_mixtures, kept_request, num_segments=REQUEST_COUNT + 1)[:REQUEST_COUNT]
        fresh_probs = jnp.exp(fresh_scores - overall[..., None])
        fresh_rounded = lax.optimization_barrier(fresh_probs.astype(jnp.bfloat16)).astype(jnp.float32)
        denominator = denominator + lax.optimization_barrier(jnp.sum(fresh_probs, axis=-1))
        mixture = mixture + jnp.einsum('bngj,jbnd->bngd', fresh_rounded, earlier_values)
        attended = (mixture / denominator[..., None]).astype(jnp.bfloat16).reshape(REQUEST_COUNT, QUERY_HEADS * HEAD_SIZE)
        output = states[sequence_index].astype(jnp.float32) + jnp.dot(attended, w_out, preferred_element_type=jnp.float32)
        results.append(output.astype(jnp.bfloat16))
    return (jnp.stack(results), jnp.stack(current_keys), jnp.stack(current_values))
```

```python
import jax
import jax.numpy as jnp
from jax import lax
from jax.sharding import PartitionSpec as P

HEAD_SIZE = 128
LONG_COUNT = 12

ROPE_BASE = 1000000.0
NEGATIVE = -1e30
HIGHEST = lax.Precision.HIGHEST


def scaled_rms(values, gain):
    return values * lax.rsqrt(jnp.mean(values * values, axis=-1, keepdims=True) + 1e-06) * gain


def rotate(values, positions):
    halfway = values.shape[-1] // 2
    frequency = ROPE_BASE ** (-(jnp.arange(halfway, dtype=jnp.float32) * 2.0) / values.shape[-1])
    angles = positions.astype(jnp.float32)[..., None, None] * frequency
    cosine = jnp.cos(angles)
    sine_part = jnp.sin(angles)
    leading = values[..., :halfway]
    trailing = values[..., halfway:]
    return jnp.concatenate(
        [leading * cosine - trailing * sine_part, trailing * cosine + leading * sine_part], axis=-1
    )


def gather_mp(block, n_mp):
    me = lax.axis_index("mp")
    pieces = [block] + [
        lax.ppermute(block, "mp", [(i, (i + s) % n_mp) for i in range(n_mp)]) for s in range(1, n_mp)
    ]
    stacked = jnp.stack(pieces)
    order = (me - jnp.arange(n_mp, dtype=jnp.int32)) % n_mp
    ordered = jnp.take(stacked, order, axis=0)
    return jnp.concatenate([ordered[c] for c in range(n_mp)], axis=-1)


def reduce_scatter_mp(full, n_mp):
    me = lax.axis_index("mp")
    width = full.shape[-1] // n_mp
    chunks = full.reshape(full.shape[:-1] + (n_mp, width))
    total = jnp.take(chunks, me, axis=-2)
    for s in range(1, n_mp):
        outgoing = jnp.take(chunks, (me + s) % n_mp, axis=-2)
        total = total + lax.ppermute(outgoing, "mp", [(i, (i + s) % n_mp) for i in range(n_mp)])
    return total


def butterfly(value, n_seq, combine):
    stride = 1
    while stride < n_seq:
        partner = lax.ppermute(value, "seq", [(i, i ^ stride) for i in range(n_seq)])
        value = combine(value, partner)
        stride *= 2
    return value


def merge_stats(mine, theirs):
    top_a = mine[..., -1:]
    top_b = theirs[..., -1:]
    top = jnp.maximum(top_a, top_b)
    scaled = mine[..., :-1] * jnp.exp(top_a - top) + theirs[..., :-1] * jnp.exp(top_b - top)
    return jnp.concatenate([scaled, top], axis=-1)


def shards(
    states,
    norm_gain,
    query_gain,
    key_gain,
    w_query,
    key_matrix,
    value_matrix,
    w_out,
    cached_key_blocks,
    cached_value_blocks,
    req_len,
    slot_request,
    slot_block,
    slot_empty,
    n_seq,
    n_mp,
):
    steps, own_rows, _ = states.shape
    me = lax.axis_index("seq")
    first_row = me * own_rows
    kv_heads = key_matrix.shape[1] // HEAD_SIZE
    q_heads = w_query.shape[1] // HEAD_SIZE
    head_sharing = q_heads // kv_heads
    slot_count, block_len, _ = cached_key_blocks.shape
    requests = req_len.shape[0]
    long_len = n_seq * block_len
    scaling = HEAD_SIZE ** (-0.5)

    wide = gather_mp(states, n_mp).reshape(steps * own_rows, -1)
    own_ids = first_row + jnp.arange(own_rows, dtype=jnp.int32)
    own_len = jnp.take(req_len, own_ids)
    positions = (own_len[None, :] + jnp.arange(steps, dtype=jnp.int32)[:, None]).reshape(-1)
    normed = scaled_rms(wide.astype(jnp.float32), norm_gain).astype(jnp.bfloat16)
    rows = steps * own_rows
    query = jnp.dot(normed, w_query, preferred_element_type=jnp.float32).reshape(rows, q_heads, HEAD_SIZE)
    keys = jnp.dot(normed, key_matrix, preferred_element_type=jnp.float32).reshape(rows, kv_heads, HEAD_SIZE)
    values = jnp.dot(normed, value_matrix, preferred_element_type=jnp.float32).astype(jnp.bfloat16)
    query = rotate(scaled_rms(query, query_gain), positions).astype(jnp.bfloat16)
    keys = rotate(scaled_rms(keys, key_gain), positions).astype(jnp.bfloat16)
    new_keys = keys.reshape(steps, own_rows, kv_heads * HEAD_SIZE)
    new_values = values.reshape(steps, own_rows, kv_heads * HEAD_SIZE)
    own_query = query.reshape(steps, own_rows, q_heads, HEAD_SIZE).transpose(1, 0, 2, 3)

    request_ids = jnp.arange(requests, dtype=jnp.int32)
    is_long = req_len == long_len
    rank = jnp.cumsum(is_long.astype(jnp.int32)) - 1
    long_ids = jnp.sum(
        jnp.where(
            is_long[None, :] & (rank[None, :] == jnp.arange(LONG_COUNT, dtype=jnp.int32)[:, None]),
            request_ids[None, :],
            0,
        ),
        axis=1,
    )
    own_pick = long_ids[:, None] == own_ids[None, :]
    long_table = jnp.sum(
        jnp.where(own_pick[:, :, None, None, None], own_query[None], jnp.zeros((), jnp.bfloat16)), axis=1
    ).astype(jnp.bfloat16)
    long_table = butterfly(long_table, n_seq, lambda a, b: a + b)

    slot_req_long = jnp.take(is_long, slot_request)
    slot_rank = jnp.take(rank, slot_request)
    local_row = slot_request - first_row
    slot_local = (local_row >= 0) & (local_row < own_rows)
    pick = jnp.where(
        slot_req_long, slot_rank, jnp.where(slot_local, LONG_COUNT + local_row, LONG_COUNT + own_rows)
    )
    candidates = jnp.concatenate(
        [long_table, own_query, jnp.zeros((1,) + own_query.shape[1:], jnp.bfloat16)], axis=0
    )
    slot_query = jnp.take(candidates, pick, axis=0).reshape(
        slot_count, steps, kv_heads, head_sharing, HEAD_SIZE
    )
    keys_split = cached_key_blocks.reshape(slot_count, block_len, kv_heads, HEAD_SIZE)
    values_split = cached_value_blocks.reshape(slot_count, block_len, kv_heads, HEAD_SIZE)
    scores = (
        jnp.einsum("stngd,sknd->stngk", slot_query, keys_split, preferred_element_type=jnp.float32)
        * scaling
    )
    slot_len = jnp.take(req_len, slot_request)
    kept = slot_empty == 0
    filled = kept[:, None] & (
        slot_block[:, None] * block_len + jnp.arange(block_len, dtype=jnp.int32)[None, :] < slot_len[:, None]
    )
    filled_wide = filled[:, None, None, None, :]
    slot_top = jnp.max(jnp.where(filled_wide, scores, NEGATIVE), axis=-1)
    same = (slot_request[:, None] == slot_request[None, :]) & kept[None, :]
    reference_top = jnp.max(
        jnp.where(same[:, :, None, None, None], slot_top[None], NEGATIVE), axis=1
    )
    weights = jnp.where(
        filled_wide, jnp.exp(jnp.where(filled_wide, scores - reference_top[..., None], 0.0)), 0.0
    )
    slot_total = jnp.sum(weights, axis=-1)
    slot_mix = jnp.einsum(
        "stngk,sknd->stngd", weights.astype(jnp.bfloat16), values_split, preferred_element_type=jnp.float32
    )

    group_ids = jnp.concatenate([long_ids, own_ids])
    member = (group_ids[:, None] == slot_request[None, :]) & kept[None, :]
    member_float = member.astype(jnp.float32)
    group_top = jnp.max(jnp.where(member[:, :, None, None, None], reference_top[None], NEGATIVE), axis=1)
    group_total = jnp.einsum("qs,stng->qtng", member_float, slot_total, precision=HIGHEST)
    group_mix = jnp.einsum("qs,stngd->qtngd", member_float, slot_mix, precision=HIGHEST)
    stats = jnp.concatenate([group_mix, group_total[..., None], group_top[..., None]], axis=-1)
    long_stats = butterfly(stats[:LONG_COUNT], n_seq, merge_stats)
    own_rank = jnp.take(rank, own_ids)
    own_is_long = jnp.take(is_long, own_ids)
    from_long = jnp.take(long_stats, jnp.clip(own_rank, 0, LONG_COUNT - 1), axis=0)
    cache_stats = jnp.where(own_is_long[:, None, None, None, None], from_long, stats[LONG_COUNT:])
    cache_mix = cache_stats[..., :HEAD_SIZE]
    cache_total = cache_stats[..., HEAD_SIZE]
    cache_top = cache_stats[..., HEAD_SIZE + 1]

    heads = own_query.reshape(own_rows, steps, kv_heads, head_sharing, HEAD_SIZE)
    fresh_keys = keys.reshape(steps, own_rows, kv_heads, HEAD_SIZE).transpose(1, 0, 2, 3)
    fresh_values = values.reshape(steps, own_rows, kv_heads, HEAD_SIZE).transpose(1, 0, 2, 3)
    fresh_scores = (
        jnp.einsum("rtngd,rjnd->rtngj", heads, fresh_keys, preferred_element_type=jnp.float32) * scaling
    )
    allowed = (jnp.arange(steps, dtype=jnp.int32)[None, :] <= jnp.arange(steps, dtype=jnp.int32)[:, None])[
        None, :, None, None, :
    ]
    fresh_top = jnp.max(jnp.where(allowed, fresh_scores, NEGATIVE), axis=-1)
    overall = jnp.maximum(cache_top, fresh_top)
    retained = jnp.exp(cache_top - overall)
    fresh_weights = jnp.where(
        allowed, jnp.exp(jnp.where(allowed, fresh_scores - overall[..., None], 0.0)), 0.0
    )
    denominator = cache_total * retained + jnp.sum(fresh_weights, axis=-1)
    mixture = cache_mix * retained[..., None] + jnp.einsum(
        "rtngj,rjnd->rtngd",
        fresh_weights.astype(jnp.bfloat16),
        fresh_values,
        preferred_element_type=jnp.float32,
    )
    attended = (mixture / denominator[..., None]).astype(jnp.bfloat16)
    attended = attended.transpose(1, 0, 2, 3, 4).reshape(steps * own_rows, q_heads * HEAD_SIZE)
    projected = jnp.dot(attended, w_out, preferred_element_type=jnp.float32).reshape(steps, own_rows, -1)
    summed = reduce_scatter_mp(projected, n_mp)
    hidden = (states.astype(jnp.float32) + summed).astype(jnp.bfloat16)
    return hidden, new_keys, new_values


def solution(mesh):
    n_seq = mesh.shape["seq"]
    n_mp = mesh.shape["mp"]
    placed = (
        P(None, "seq", "mp"),
        P(),
        P(),
        P(),
        P(None, "mp"),
        P(None, "mp"),
        P(None, "mp"),
        P("mp", None),
        P("seq", None, "mp"),
        P("seq", None, "mp"),
        P(),
        P("seq"),
        P("seq"),
        P("seq"),
    )

    def body(*args):
        return shards(*args, n_seq=n_seq, n_mp=n_mp)

    return jax.shard_map(
        body,
        mesh=mesh,
        in_specs=placed,
        out_specs=(P(None, "seq", "mp"), P(None, "seq", "mp"), P(None, "seq", "mp")),
        check_vma=False,
    )
```

```python
import jax
import jax.numpy as jnp
from jax import lax
from jax.experimental import pallas as pl
from jax.sharding import PartitionSpec as P

HEAD_SIZE = 128
LONG_COUNT = 12

ROPE_BASE = 1000000.0
NEGATIVE = -1e30
HIGHEST = lax.Precision.HIGHEST


def scaled_rms(values, gain):
    return values * lax.rsqrt(jnp.mean(values * values, axis=-1, keepdims=True) + 1e-06) * gain


def rotate(values, positions):
    halfway = values.shape[-1] // 2
    frequency = ROPE_BASE ** (-(jnp.arange(halfway, dtype=jnp.float32) * 2.0) / values.shape[-1])
    angles = positions.astype(jnp.float32)[..., None, None] * frequency
    cosine = jnp.cos(angles)
    sine_part = jnp.sin(angles)
    leading = values[..., :halfway]
    trailing = values[..., halfway:]
    return jnp.concatenate(
        [leading * cosine - trailing * sine_part, trailing * cosine + leading * sine_part], axis=-1
    )


def _matmul_kernel(x_ref, *refs):
    count = len(refs) // 2
    x = x_ref[...]
    for w_ref, o_ref in zip(refs[:count], refs[count:]):
        o_ref[...] = jnp.dot(x, w_ref[...], preferred_element_type=jnp.float32)


def small_matmul(x, *weights):
    m, k = x.shape
    widths = [w.shape[1] for w in weights]
    return pl.pallas_call(
        _matmul_kernel,
        out_shape=[jax.ShapeDtypeStruct((m, n), jnp.float32) for n in widths],
        cost_estimate=pl.CostEstimate(
            flops=2 * m * k * sum(widths),
            bytes_accessed=2 * (m * k + k * sum(widths)) + 4 * m * sum(widths),
            transcendentals=0,
        ),
    )(x, *weights)


def gather_mp(block, n_mp):
    me = lax.axis_index("mp")
    pieces = [block] + [
        lax.ppermute(block, "mp", [(i, (i + s) % n_mp) for i in range(n_mp)]) for s in range(1, n_mp)
    ]
    stacked = jnp.stack(pieces)
    order = (me - jnp.arange(n_mp, dtype=jnp.int32)) % n_mp
    ordered = jnp.take(stacked, order, axis=0)
    return jnp.concatenate([ordered[c] for c in range(n_mp)], axis=-1)


def reduce_scatter_mp(full, n_mp):
    me = lax.axis_index("mp")
    width = full.shape[-1] // n_mp
    chunks = full.reshape(full.shape[:-1] + (n_mp, width))
    total = jnp.take(chunks, me, axis=-2)
    for s in range(1, n_mp):
        outgoing = jnp.take(chunks, (me + s) % n_mp, axis=-2)
        total = total + lax.ppermute(outgoing, "mp", [(i, (i + s) % n_mp) for i in range(n_mp)])
    return total


def butterfly(value, n_seq, combine):
    stride = 1
    while stride < n_seq:
        partner = lax.ppermute(value, "seq", [(i, i ^ stride) for i in range(n_seq)])
        value = combine(value, partner)
        stride *= 2
    return value


def merge_stats(mine, theirs):
    top_a = mine[-1:]
    top_b = theirs[-1:]
    top = jnp.maximum(top_a, top_b)
    scaled = mine * jnp.exp(top_a - top) + theirs * jnp.exp(top_b - top)
    last = lax.broadcasted_iota(jnp.int32, mine.shape, 0) == mine.shape[0] - 1
    return jnp.where(last, top, scaled)


def shards(
    states,
    norm_gain,
    query_gain,
    key_gain,
    w_query,
    key_matrix,
    value_matrix,
    w_out,
    cached_key_blocks,
    cached_value_blocks,
    req_len,
    slot_request,
    slot_block,
    slot_empty,
    n_seq,
    n_mp,
):
    steps, own_rows, _ = states.shape
    me = lax.axis_index("seq")
    first_row = me * own_rows
    kv_heads = key_matrix.shape[1] // HEAD_SIZE
    q_heads = w_query.shape[1] // HEAD_SIZE
    head_sharing = q_heads // kv_heads
    slot_count, block_len, _ = cached_key_blocks.shape
    requests = req_len.shape[0]
    long_len = n_seq * block_len
    scaling = HEAD_SIZE ** (-0.5)

    wide = gather_mp(states, n_mp).reshape(steps * own_rows, -1)
    own_ids = first_row + jnp.arange(own_rows, dtype=jnp.int32)
    own_len = jnp.take(req_len, own_ids)
    positions = (own_len[None, :] + jnp.arange(steps, dtype=jnp.int32)[:, None]).reshape(-1)
    normed = scaled_rms(wide.astype(jnp.float32), norm_gain).astype(jnp.bfloat16)
    rows = steps * own_rows
    query, keys, values = small_matmul(normed, w_query, key_matrix, value_matrix)
    query = query.reshape(rows, q_heads, HEAD_SIZE)
    keys = keys.reshape(rows, kv_heads, HEAD_SIZE)
    values = values.astype(jnp.bfloat16)
    query = rotate(scaled_rms(query, query_gain), positions).astype(jnp.bfloat16)
    keys = rotate(scaled_rms(keys, key_gain), positions).astype(jnp.bfloat16)
    new_keys = keys.reshape(steps, own_rows, kv_heads * HEAD_SIZE)
    new_values = values.reshape(steps, own_rows, kv_heads * HEAD_SIZE)
    own_query = query.reshape(steps, own_rows, q_heads, HEAD_SIZE).transpose(1, 0, 2, 3)

    request_ids = jnp.arange(requests, dtype=jnp.int32)
    is_long = req_len == long_len
    rank = jnp.cumsum(is_long.astype(jnp.int32)) - 1
    long_ids = jnp.sum(
        jnp.where(
            is_long[None, :] & (rank[None, :] == jnp.arange(LONG_COUNT, dtype=jnp.int32)[:, None]),
            request_ids[None, :],
            0,
        ),
        axis=1,
    )
    own_pick = long_ids[:, None] == own_ids[None, :]
    long_table = jnp.sum(
        jnp.where(own_pick[:, :, None, None, None], own_query[None], jnp.zeros((), jnp.bfloat16)), axis=1
    ).astype(jnp.bfloat16)
    long_table = butterfly(long_table, n_seq, lambda a, b: a + b)

    slot_req_long = jnp.take(is_long, slot_request)
    slot_rank = jnp.take(rank, slot_request)
    local_row = slot_request - first_row
    slot_local = (local_row >= 0) & (local_row < own_rows)
    pick = jnp.where(
        slot_req_long, slot_rank, jnp.where(slot_local, LONG_COUNT + local_row, LONG_COUNT + own_rows)
    )
    candidates = jnp.concatenate(
        [long_table, own_query, jnp.zeros((1,) + own_query.shape[1:], jnp.bfloat16)], axis=0
    )
    slot_query = jnp.take(candidates, pick, axis=0).reshape(
        slot_count, steps, kv_heads, head_sharing, HEAD_SIZE
    )
    keys_split = cached_key_blocks.reshape(slot_count, block_len, kv_heads, HEAD_SIZE)
    values_split = cached_value_blocks.reshape(slot_count, block_len, kv_heads, HEAD_SIZE)
    scores = (
        jnp.einsum("stngd,sknd->stngk", slot_query, keys_split, preferred_element_type=jnp.float32)
        * scaling
    )
    slot_len = jnp.take(req_len, slot_request)
    kept = slot_empty == 0
    filled = kept[:, None] & (
        slot_block[:, None] * block_len + jnp.arange(block_len, dtype=jnp.int32)[None, :] < slot_len[:, None]
    )
    filled_wide = filled[:, None, None, None, :]
    slot_top = jnp.max(jnp.where(filled_wide, scores, NEGATIVE), axis=-1)
    same = (slot_request[:, None] == slot_request[None, :]) & kept[None, :]
    reference_top = jnp.max(
        jnp.where(same[:, :, None, None, None], slot_top[None], NEGATIVE), axis=1
    )
    weights = jnp.where(
        filled_wide, jnp.exp(jnp.where(filled_wide, scores - reference_top[..., None], 0.0)), 0.0
    )
    slot_total = jnp.sum(weights, axis=-1)
    slot_mix = jnp.einsum(
        "stngk,sknd->stngd", weights.astype(jnp.bfloat16), values_split, preferred_element_type=jnp.float32
    )

    group_ids = jnp.concatenate([long_ids, own_ids])
    member = (group_ids[:, None] == slot_request[None, :]) & kept[None, :]
    member_float = member.astype(jnp.float32)
    group_top = jnp.max(jnp.where(member[:, :, None, None, None], reference_top[None], NEGATIVE), axis=1)
    group_total = jnp.einsum("qs,stng->qtng", member_float, slot_total, precision=HIGHEST)
    group_mix = jnp.einsum("qs,stngd->qtngd", member_float, slot_mix, precision=HIGHEST)
    stats = jnp.concatenate(
        [group_mix, group_total[..., None], group_top[..., None]], axis=-1
    )
    long_stats = stats[:LONG_COUNT].reshape(-1, HEAD_SIZE + 2).T
    long_stats = butterfly(long_stats, n_seq, merge_stats)
    long_stats = long_stats.T.reshape((LONG_COUNT,) + stats.shape[1:])
    own_rank = jnp.take(rank, own_ids)
    own_is_long = jnp.take(is_long, own_ids)
    from_long = jnp.take(long_stats, jnp.clip(own_rank, 0, LONG_COUNT - 1), axis=0)
    cache_stats = jnp.where(own_is_long[:, None, None, None, None], from_long, stats[LONG_COUNT:])
    cache_mix = cache_stats[..., :HEAD_SIZE]
    cache_total = cache_stats[..., HEAD_SIZE]
    cache_top = cache_stats[..., HEAD_SIZE + 1]

    heads = own_query.reshape(own_rows, steps, kv_heads, head_sharing, HEAD_SIZE)
    fresh_keys = keys.reshape(steps, own_rows, kv_heads, HEAD_SIZE).transpose(1, 0, 2, 3)
    fresh_values = values.reshape(steps, own_rows, kv_heads, HEAD_SIZE).transpose(1, 0, 2, 3)
    fresh_scores = (
        jnp.einsum("rtngd,rjnd->rtngj", heads, fresh_keys, preferred_element_type=jnp.float32) * scaling
    )
    allowed = (jnp.arange(steps, dtype=jnp.int32)[None, :] <= jnp.arange(steps, dtype=jnp.int32)[:, None])[
        None, :, None, None, :
    ]
    fresh_top = jnp.max(jnp.where(allowed, fresh_scores, NEGATIVE), axis=-1)
    overall = jnp.maximum(cache_top, fresh_top)
    retained = jnp.exp(cache_top - overall)
    fresh_weights = jnp.where(
        allowed, jnp.exp(jnp.where(allowed, fresh_scores - overall[..., None], 0.0)), 0.0
    )
    denominator = cache_total * retained + jnp.sum(fresh_weights, axis=-1)
    mixture = cache_mix * retained[..., None] + jnp.einsum(
        "rtngj,rjnd->rtngd",
        fresh_weights.astype(jnp.bfloat16),
        fresh_values,
        preferred_element_type=jnp.float32,
    )
    attended = (mixture / denominator[..., None]).astype(jnp.bfloat16)
    attended = attended.transpose(1, 0, 2, 3, 4).reshape(steps * own_rows, q_heads * HEAD_SIZE)
    (projected,) = small_matmul(attended, w_out)
    projected = projected.reshape(steps, own_rows, -1)
    summed = reduce_scatter_mp(projected, n_mp)
    hidden = (states.astype(jnp.float32) + summed).astype(jnp.bfloat16)
    return hidden, new_keys, new_values


def solution(mesh):
    n_seq = mesh.shape["seq"]
    n_mp = mesh.shape["mp"]
    placed = (
        P(None, "seq", "mp"),
        P(),
        P(),
        P(),
        P(None, "mp"),
        P(None, "mp"),
        P(None, "mp"),
        P("mp", None),
        P("seq", None, "mp"),
        P("seq", None, "mp"),
        P(),
        P("seq"),
        P("seq"),
        P("seq"),
    )

    def body(*args):
        return shards(*args, n_seq=n_seq, n_mp=n_mp)

    return jax.shard_map(
        body,
        mesh=mesh,
        in_specs=placed,
        out_specs=(P(None, "seq", "mp"), P(None, "seq", "mp"), P(None, "seq", "mp")),
        check_vma=False,
    )
```

```python
import jax
import jax.numpy as jnp
from jax import lax
from jax.experimental import pallas as pl
from jax.sharding import PartitionSpec as P

HEAD_SIZE = 128
LONG_COUNT = 12

ROPE_BASE = 1000000.0
NEGATIVE = -1e30
HIGHEST = lax.Precision.HIGHEST


def scaled_rms(values, gain):
    return values * lax.rsqrt(jnp.mean(values * values, axis=-1, keepdims=True) + 1e-06) * gain


def rotate(values, positions):
    halfway = values.shape[-1] // 2
    frequency = ROPE_BASE ** (-(jnp.arange(halfway, dtype=jnp.float32) * 2.0) / values.shape[-1])
    angles = positions.astype(jnp.float32)[..., None, None] * frequency
    cosine = jnp.cos(angles)
    sine_part = jnp.sin(angles)
    leading = values[..., :halfway]
    trailing = values[..., halfway:]
    return jnp.concatenate(
        [leading * cosine - trailing * sine_part, trailing * cosine + leading * sine_part], axis=-1
    )


def _matmul_kernel(x_ref, *refs):
    count = len(refs) // 2
    x = x_ref[...]
    for w_ref, o_ref in zip(refs[:count], refs[count:]):
        o_ref[...] = jnp.dot(x, w_ref[...], preferred_element_type=jnp.float32)


def small_matmul(x, *weights):
    m, k = x.shape
    widths = [w.shape[1] for w in weights]
    return pl.pallas_call(
        _matmul_kernel,
        out_shape=[jax.ShapeDtypeStruct((m, n), jnp.float32) for n in widths],
        cost_estimate=pl.CostEstimate(
            flops=2 * m * k * sum(widths),
            bytes_accessed=2 * (m * k + k * sum(widths)) + 4 * m * sum(widths),
            transcendentals=0,
        ),
    )(x, *weights)


def gather_mp(block, n_mp):
    me = lax.axis_index("mp")
    pieces = [block] + [
        lax.ppermute(block, "mp", [(i, (i + s) % n_mp) for i in range(n_mp)]) for s in range(1, n_mp)
    ]
    stacked = jnp.stack(pieces)
    order = (me - jnp.arange(n_mp, dtype=jnp.int32)) % n_mp
    ordered = jnp.take(stacked, order, axis=0)
    return jnp.concatenate([ordered[c] for c in range(n_mp)], axis=-1)


def reduce_scatter_mp(full, n_mp):
    me = lax.axis_index("mp")
    width = full.shape[-1] // n_mp
    chunks = full.reshape(full.shape[:-1] + (n_mp, width))
    total = jnp.take(chunks, me, axis=-2)
    for s in range(1, n_mp):
        outgoing = jnp.take(chunks, (me + s) % n_mp, axis=-2)
        total = total + lax.ppermute(outgoing, "mp", [(i, (i + s) % n_mp) for i in range(n_mp)])
    return total


def butterfly(value, n_seq, combine):
    stride = 1
    while stride < n_seq:
        partner = lax.ppermute(value, "seq", [(i, i ^ stride) for i in range(n_seq)])
        value = combine(value, partner)
        stride *= 2
    return value


def merge_stats(mine, theirs):
    mix_a, stats_a = mine
    mix_b, stats_b = theirs
    top_a = stats_a[1:]
    top_b = stats_b[1:]
    top = jnp.maximum(top_a, top_b)
    scale_a = jnp.exp(top_a - top)
    scale_b = jnp.exp(top_b - top)
    mix = mix_a * scale_a + mix_b.astype(jnp.float32) * scale_b
    total = stats_a[:1] * scale_a + stats_b[:1] * scale_b
    return mix, jnp.concatenate([total, top], axis=0)


def split_exact(x):
    hi = lax.reduce_precision(x, exponent_bits=8, mantissa_bits=7)
    rest = x - hi
    mid = lax.reduce_precision(rest, exponent_bits=8, mantissa_bits=7)
    lo = rest - mid
    return jnp.concatenate([hi, mid, lo], axis=0).astype(jnp.bfloat16)


def join_exact(parts):
    parts = parts.astype(jnp.float32)
    return parts[0:1] + parts[1:2] + parts[2:3]


def stats_butterfly(mix, stats, n_seq):
    width = mix.shape[0]
    stride = 1
    while stride < n_seq:
        pairs = [(i, i ^ stride) for i in range(n_seq)]
        packed = jnp.concatenate(
            [mix.astype(jnp.bfloat16), split_exact(stats[:1]), split_exact(stats[1:])], axis=0
        )
        arrived = lax.ppermute(packed, "seq", pairs)
        theirs = (
            arrived[:width],
            jnp.concatenate(
                [join_exact(arrived[width : width + 3]), join_exact(arrived[width + 3 : width + 6])], axis=0
            ),
        )
        mix, stats = merge_stats((mix, stats), theirs)
        stride *= 2
    return mix, stats


def shards(
    states,
    norm_gain,
    query_gain,
    key_gain,
    w_query,
    key_matrix,
    value_matrix,
    w_out,
    cached_key_blocks,
    cached_value_blocks,
    req_len,
    slot_request,
    slot_block,
    slot_empty,
    n_seq,
    n_mp,
):
    steps, own_rows, _ = states.shape
    me = lax.axis_index("seq")
    first_row = me * own_rows
    kv_heads = key_matrix.shape[1] // HEAD_SIZE
    q_heads = w_query.shape[1] // HEAD_SIZE
    head_sharing = q_heads // kv_heads
    slot_count, block_len, _ = cached_key_blocks.shape
    requests = req_len.shape[0]
    long_len = n_seq * block_len
    scaling = HEAD_SIZE ** (-0.5)

    wide = gather_mp(states, n_mp).reshape(steps * own_rows, -1)
    own_ids = first_row + jnp.arange(own_rows, dtype=jnp.int32)
    own_len = jnp.take(req_len, own_ids)
    positions = (own_len[None, :] + jnp.arange(steps, dtype=jnp.int32)[:, None]).reshape(-1)
    normed = scaled_rms(wide.astype(jnp.float32), norm_gain).astype(jnp.bfloat16)
    rows = steps * own_rows
    query, keys, values = small_matmul(normed, w_query, key_matrix, value_matrix)
    query = query.reshape(rows, q_heads, HEAD_SIZE)
    keys = keys.reshape(rows, kv_heads, HEAD_SIZE)
    values = values.astype(jnp.bfloat16)
    query = rotate(scaled_rms(query, query_gain), positions).astype(jnp.bfloat16)
    keys = rotate(scaled_rms(keys, key_gain), positions).astype(jnp.bfloat16)
    new_keys = keys.reshape(steps, own_rows, kv_heads * HEAD_SIZE)
    new_values = values.reshape(steps, own_rows, kv_heads * HEAD_SIZE)
    own_query = query.reshape(steps, own_rows, q_heads, HEAD_SIZE).transpose(1, 0, 2, 3)

    request_ids = jnp.arange(requests, dtype=jnp.int32)
    is_long = req_len == long_len
    rank = jnp.cumsum(is_long.astype(jnp.int32)) - 1
    long_ids = jnp.sum(
        jnp.where(
            is_long[None, :] & (rank[None, :] == jnp.arange(LONG_COUNT, dtype=jnp.int32)[:, None]),
            request_ids[None, :],
            0,
        ),
        axis=1,
    )
    own_pick = long_ids[:, None] == own_ids[None, :]
    long_table = jnp.sum(
        jnp.where(own_pick[:, :, None, None, None], own_query[None], jnp.zeros((), jnp.bfloat16)), axis=1
    ).astype(jnp.bfloat16)
    long_table = butterfly(long_table, n_seq, lambda a, b: a + b)

    slot_req_long = jnp.take(is_long, slot_request)
    slot_rank = jnp.take(rank, slot_request)
    local_row = slot_request - first_row
    slot_local = (local_row >= 0) & (local_row < own_rows)
    pick = jnp.where(
        slot_req_long, slot_rank, jnp.where(slot_local, LONG_COUNT + local_row, LONG_COUNT + own_rows)
    )
    candidates = jnp.concatenate(
        [long_table, own_query, jnp.zeros((1,) + own_query.shape[1:], jnp.bfloat16)], axis=0
    )
    slot_query = jnp.take(candidates, pick, axis=0).reshape(
        slot_count, steps, kv_heads, head_sharing, HEAD_SIZE
    )
    keys_split = cached_key_blocks.reshape(slot_count, block_len, kv_heads, HEAD_SIZE)
    values_split = cached_value_blocks.reshape(slot_count, block_len, kv_heads, HEAD_SIZE)
    scores = (
        jnp.einsum("stngd,sknd->stngk", slot_query, keys_split, preferred_element_type=jnp.float32)
        * scaling
    )
    slot_len = jnp.take(req_len, slot_request)
    kept = slot_empty == 0
    filled = kept[:, None] & (
        slot_block[:, None] * block_len + jnp.arange(block_len, dtype=jnp.int32)[None, :] < slot_len[:, None]
    )
    filled_wide = filled[:, None, None, None, :]
    slot_top = jnp.max(jnp.where(filled_wide, scores, NEGATIVE), axis=-1)
    same = (slot_request[:, None] == slot_request[None, :]) & kept[None, :]
    reference_top = jnp.max(
        jnp.where(same[:, :, None, None, None], slot_top[None], NEGATIVE), axis=1
    )
    weights = jnp.where(
        filled_wide, jnp.exp(jnp.where(filled_wide, scores - reference_top[..., None], 0.0)), 0.0
    )
    slot_total = jnp.sum(weights, axis=-1)
    slot_mix = jnp.einsum(
        "stngk,sknd->stngd", weights.astype(jnp.bfloat16), values_split, preferred_element_type=jnp.float32
    )

    group_ids = jnp.concatenate([long_ids, own_ids])
    member = (group_ids[:, None] == slot_request[None, :]) & kept[None, :]
    member_float = member.astype(jnp.float32)
    group_top = jnp.max(jnp.where(member[:, :, None, None, None], reference_top[None], NEGATIVE), axis=1)
    group_total = jnp.einsum("qs,stng->qtng", member_float, slot_total, precision=HIGHEST)
    group_mix = jnp.einsum("qs,stngd->qtngd", member_float, slot_mix, precision=HIGHEST)
    stats = jnp.concatenate(
        [group_mix, group_total[..., None], group_top[..., None]], axis=-1
    )
    long_stats = stats[:LONG_COUNT].reshape(-1, HEAD_SIZE + 2).T
    long_mix, long_small = stats_butterfly(long_stats[:HEAD_SIZE], long_stats[HEAD_SIZE:], n_seq)
    long_stats = jnp.concatenate([long_mix, long_small], axis=0)
    long_stats = long_stats.T.reshape((LONG_COUNT,) + stats.shape[1:])
    own_rank = jnp.take(rank, own_ids)
    own_is_long = jnp.take(is_long, own_ids)
    from_long = jnp.take(long_stats, jnp.clip(own_rank, 0, LONG_COUNT - 1), axis=0)
    cache_stats = jnp.where(own_is_long[:, None, None, None, None], from_long, stats[LONG_COUNT:])
    cache_mix = cache_stats[..., :HEAD_SIZE]
    cache_total = cache_stats[..., HEAD_SIZE]
    cache_top = cache_stats[..., HEAD_SIZE + 1]

    heads = own_query.reshape(own_rows, steps, kv_heads, head_sharing, HEAD_SIZE)
    fresh_keys = keys.reshape(steps, own_rows, kv_heads, HEAD_SIZE).transpose(1, 0, 2, 3)
    fresh_values = values.reshape(steps, own_rows, kv_heads, HEAD_SIZE).transpose(1, 0, 2, 3)
    fresh_scores = (
        jnp.einsum("rtngd,rjnd->rtngj", heads, fresh_keys, preferred_element_type=jnp.float32) * scaling
    )
    allowed = (jnp.arange(steps, dtype=jnp.int32)[None, :] <= jnp.arange(steps, dtype=jnp.int32)[:, None])[
        None, :, None, None, :
    ]
    fresh_top = jnp.max(jnp.where(allowed, fresh_scores, NEGATIVE), axis=-1)
    overall = jnp.maximum(cache_top, fresh_top)
    retained = jnp.exp(cache_top - overall)
    fresh_weights = jnp.where(
        allowed, jnp.exp(jnp.where(allowed, fresh_scores - overall[..., None], 0.0)), 0.0
    )
    denominator = cache_total * retained + jnp.sum(fresh_weights, axis=-1)
    mixture = cache_mix * retained[..., None] + jnp.einsum(
        "rtngj,rjnd->rtngd",
        fresh_weights.astype(jnp.bfloat16),
        fresh_values,
        preferred_element_type=jnp.float32,
    )
    attended = (mixture / denominator[..., None]).astype(jnp.bfloat16)
    attended = attended.transpose(1, 0, 2, 3, 4).reshape(steps * own_rows, q_heads * HEAD_SIZE)
    (projected,) = small_matmul(attended, w_out)
    projected = projected.reshape(steps, own_rows, -1)
    summed = reduce_scatter_mp(projected, n_mp)
    hidden = (states.astype(jnp.float32) + summed).astype(jnp.bfloat16)
    return hidden, new_keys, new_values


def solution(mesh):
    n_seq = mesh.shape["seq"]
    n_mp = mesh.shape["mp"]
    placed = (
        P(None, "seq", "mp"),
        P(),
        P(),
        P(),
        P(None, "mp"),
        P(None, "mp"),
        P(None, "mp"),
        P("mp", None),
        P("seq", None, "mp"),
        P("seq", None, "mp"),
        P(),
        P("seq"),
        P("seq"),
        P("seq"),
    )

    def body(*args):
        return shards(*args, n_seq=n_seq, n_mp=n_mp)

    return jax.shard_map(
        body,
        mesh=mesh,
        in_specs=placed,
        out_specs=(P(None, "seq", "mp"), P(None, "seq", "mp"), P(None, "seq", "mp")),
        check_vma=False,
    )
```

```python
import jax
import jax.numpy as jnp
from jax import lax
from jax.experimental import pallas as pl
from jax.sharding import PartitionSpec as P

HEAD_SIZE = 128
LONG_COUNT = 12

ROPE_BASE = 1000000.0
NEGATIVE = -1e30
HIGHEST = lax.Precision.HIGHEST


def scaled_rms(values, gain):
    return values * lax.rsqrt(jnp.mean(values * values, axis=-1, keepdims=True) + 1e-06) * gain


def rotate(values, positions):
    halfway = values.shape[-1] // 2
    frequency = ROPE_BASE ** (-(jnp.arange(halfway, dtype=jnp.float32) * 2.0) / values.shape[-1])
    angles = positions.astype(jnp.float32)[..., None, None] * frequency
    cosine = jnp.cos(angles)
    sine_part = jnp.sin(angles)
    leading = values[..., :halfway]
    trailing = values[..., halfway:]
    return jnp.concatenate(
        [leading * cosine - trailing * sine_part, trailing * cosine + leading * sine_part], axis=-1
    )


def _matmul_kernel(x_ref, *refs):
    count = len(refs) // 2
    x = x_ref[...]
    for w_ref, o_ref in zip(refs[:count], refs[count:]):
        o_ref[...] = jnp.dot(x, w_ref[...], preferred_element_type=jnp.float32)


def small_matmul(x, *weights):
    m, k = x.shape
    widths = [w.shape[1] for w in weights]
    return pl.pallas_call(
        _matmul_kernel,
        out_shape=[jax.ShapeDtypeStruct((m, n), jnp.float32) for n in widths],
        cost_estimate=pl.CostEstimate(
            flops=2 * m * k * sum(widths),
            bytes_accessed=2 * (m * k + k * sum(widths)) + 4 * m * sum(widths),
            transcendentals=0,
        ),
    )(x, *weights)


def gather_mp(block, n_mp):
    me = lax.axis_index("mp")
    pieces = [block] + [
        lax.ppermute(block, "mp", [(i, (i + s) % n_mp) for i in range(n_mp)]) for s in range(1, n_mp)
    ]
    ordered = []
    for c in range(n_mp):
        shift = (me - c) % n_mp
        chosen = pieces[0]
        for s in range(1, n_mp):
            chosen = jnp.where(shift == s, pieces[s], chosen)
        ordered.append(chosen)
    return jnp.concatenate(ordered, axis=-1)


def reduce_scatter_mp(full, n_mp):
    me = lax.axis_index("mp")
    width = full.shape[-1] // n_mp
    chunks = full.reshape(full.shape[:-1] + (n_mp, width))
    total = lax.dynamic_index_in_dim(chunks, me, axis=chunks.ndim - 2, keepdims=False)
    for s in range(1, n_mp):
        outgoing = lax.dynamic_index_in_dim(chunks, (me + s) % n_mp, axis=chunks.ndim - 2, keepdims=False)
        total = total + lax.ppermute(outgoing, "mp", [(i, (i + s) % n_mp) for i in range(n_mp)])
    return total


def butterfly(value, n_seq, combine):
    stride = 1
    while stride < n_seq:
        partner = lax.ppermute(value, "seq", [(i, i ^ stride) for i in range(n_seq)])
        value = combine(value, partner)
        stride *= 2
    return value


def merge_stats(mine, theirs):
    mix_a, stats_a = mine
    mix_b, stats_b = theirs
    top_a = stats_a[1:]
    top_b = stats_b[1:]
    top = jnp.maximum(top_a, top_b)
    scale_a = jnp.exp(top_a - top)
    scale_b = jnp.exp(top_b - top)
    mix = mix_a * scale_a + mix_b.astype(jnp.float32) * scale_b
    total = stats_a[:1] * scale_a + stats_b[:1] * scale_b
    return mix, jnp.concatenate([total, top], axis=0)


def split_exact(x):
    hi = lax.reduce_precision(x, exponent_bits=8, mantissa_bits=7)
    rest = x - hi
    mid = lax.reduce_precision(rest, exponent_bits=8, mantissa_bits=7)
    lo = rest - mid
    return jnp.concatenate([hi, mid, lo], axis=0).astype(jnp.bfloat16)


def join_exact(parts):
    parts = parts.astype(jnp.float32)
    return parts[0:1] + parts[1:2] + parts[2:3]


def stats_butterfly(mix, stats, n_seq):
    width = mix.shape[0]
    stride = 1
    while stride < n_seq:
        pairs = [(i, i ^ stride) for i in range(n_seq)]
        packed = jnp.concatenate(
            [mix.astype(jnp.bfloat16), split_exact(stats[:1]), split_exact(stats[1:])], axis=0
        )
        arrived = lax.ppermute(packed, "seq", pairs)
        theirs = (
            arrived[:width],
            jnp.concatenate(
                [join_exact(arrived[width : width + 3]), join_exact(arrived[width + 3 : width + 6])], axis=0
            ),
        )
        mix, stats = merge_stats((mix, stats), theirs)
        stride *= 2
    return mix, stats


def shards(
    states,
    norm_gain,
    query_gain,
    key_gain,
    w_query,
    key_matrix,
    value_matrix,
    w_out,
    cached_key_blocks,
    cached_value_blocks,
    req_len,
    slot_request,
    slot_block,
    slot_empty,
    n_seq,
    n_mp,
):
    steps, own_rows, _ = states.shape
    me = lax.axis_index("seq")
    first_row = me * own_rows
    kv_heads = key_matrix.shape[1] // HEAD_SIZE
    q_heads = w_query.shape[1] // HEAD_SIZE
    head_sharing = q_heads // kv_heads
    slot_count, block_len, _ = cached_key_blocks.shape
    requests = req_len.shape[0]
    long_len = n_seq * block_len
    scaling = HEAD_SIZE ** (-0.5)

    wide = gather_mp(states, n_mp).reshape(steps * own_rows, -1)
    own_ids = first_row + jnp.arange(own_rows, dtype=jnp.int32)
    own_len = lax.dynamic_slice_in_dim(req_len, first_row, own_rows)
    positions = (own_len[None, :] + jnp.arange(steps, dtype=jnp.int32)[:, None]).reshape(-1)
    normed = scaled_rms(wide.astype(jnp.float32), norm_gain).astype(jnp.bfloat16)
    rows = steps * own_rows
    query, keys, values = small_matmul(normed, w_query, key_matrix, value_matrix)
    query = query.reshape(rows, q_heads, HEAD_SIZE)
    keys = keys.reshape(rows, kv_heads, HEAD_SIZE)
    values = values.astype(jnp.bfloat16)
    query = rotate(scaled_rms(query, query_gain), positions).astype(jnp.bfloat16)
    keys = rotate(scaled_rms(keys, key_gain), positions).astype(jnp.bfloat16)
    new_keys = keys.reshape(steps, own_rows, kv_heads * HEAD_SIZE)
    new_values = values.reshape(steps, own_rows, kv_heads * HEAD_SIZE)
    own_query = query.reshape(steps, own_rows, q_heads, HEAD_SIZE).transpose(1, 0, 2, 3)

    request_ids = jnp.arange(requests, dtype=jnp.int32)
    is_long = req_len == long_len
    long_count = is_long.astype(jnp.int32)
    rank = jnp.sum(
        jnp.where(request_ids[None, :] < request_ids[:, None], long_count[None, :], 0), axis=1
    )
    long_ids = jnp.sum(
        jnp.where(
            is_long[None, :] & (rank[None, :] == jnp.arange(LONG_COUNT, dtype=jnp.int32)[:, None]),
            request_ids[None, :],
            0,
        ),
        axis=1,
    )
    own_pick = long_ids[:, None] == own_ids[None, :]
    long_table = jnp.sum(
        jnp.where(own_pick[:, :, None, None, None], own_query[None], jnp.zeros((), jnp.bfloat16)), axis=1
    ).astype(jnp.bfloat16)
    long_table = butterfly(long_table, n_seq, lambda a, b: a + b)

    hit = slot_request[:, None] == request_ids[None, :]
    slot_req_long = jnp.any(hit & is_long[None, :], axis=1)
    slot_rank = jnp.sum(jnp.where(hit, rank[None, :], 0), axis=1)
    slot_len = jnp.sum(jnp.where(hit, req_len[None, :], 0), axis=1)
    local_row = slot_request - first_row
    slot_local = (local_row >= 0) & (local_row < own_rows)
    pick = jnp.where(
        slot_req_long, slot_rank, jnp.where(slot_local, LONG_COUNT + local_row, LONG_COUNT + own_rows)
    )
    candidates = jnp.concatenate(
        [long_table, own_query, jnp.zeros((1,) + own_query.shape[1:], jnp.bfloat16)], axis=0
    )
    slot_query = jnp.take(candidates, pick, axis=0).reshape(
        slot_count, steps, kv_heads, head_sharing, HEAD_SIZE
    )
    keys_split = cached_key_blocks.reshape(slot_count, block_len, kv_heads, HEAD_SIZE)
    values_split = cached_value_blocks.reshape(slot_count, block_len, kv_heads, HEAD_SIZE)
    scores = (
        jnp.einsum("stngd,sknd->stngk", slot_query, keys_split, preferred_element_type=jnp.float32)
        * scaling
    )
    kept = slot_empty == 0
    filled = kept[:, None] & (
        slot_block[:, None] * block_len + jnp.arange(block_len, dtype=jnp.int32)[None, :] < slot_len[:, None]
    )
    filled_wide = filled[:, None, None, None, :]
    slot_top = jnp.max(jnp.where(filled_wide, scores, NEGATIVE), axis=-1)
    same = (slot_request[:, None] == slot_request[None, :]) & kept[None, :]
    reference_top = jnp.max(
        jnp.where(same[:, :, None, None, None], slot_top[None], NEGATIVE), axis=1
    )
    weights = jnp.where(
        filled_wide, jnp.exp(jnp.where(filled_wide, scores - reference_top[..., None], 0.0)), 0.0
    )
    slot_total = jnp.sum(weights, axis=-1)
    slot_mix = jnp.einsum(
        "stngk,sknd->stngd", weights.astype(jnp.bfloat16), values_split, preferred_element_type=jnp.float32
    )

    group_ids = jnp.concatenate([long_ids, own_ids])
    member = (group_ids[:, None] == slot_request[None, :]) & kept[None, :]
    member_float = member.astype(jnp.float32)
    group_top = jnp.max(jnp.where(member[:, :, None, None, None], reference_top[None], NEGATIVE), axis=1)
    group_total = jnp.einsum("qs,stng->qtng", member_float, slot_total, precision=HIGHEST)
    group_mix = jnp.einsum("qs,stngd->qtngd", member_float, slot_mix, precision=HIGHEST)
    stats = jnp.concatenate(
        [group_mix, group_total[..., None], group_top[..., None]], axis=-1
    )
    long_stats = stats[:LONG_COUNT].reshape(-1, HEAD_SIZE + 2).T
    long_mix, long_small = stats_butterfly(long_stats[:HEAD_SIZE], long_stats[HEAD_SIZE:], n_seq)
    long_stats = jnp.concatenate([long_mix, long_small], axis=0)
    long_stats = long_stats.T.reshape((LONG_COUNT,) + stats.shape[1:])
    own_rank = lax.dynamic_slice_in_dim(rank, first_row, own_rows)
    own_is_long = lax.dynamic_slice_in_dim(is_long, first_row, own_rows)
    rank_hit = own_rank[:, None] == jnp.arange(LONG_COUNT, dtype=jnp.int32)[None, :]
    from_long = jnp.sum(
        jnp.where(rank_hit[:, :, None, None, None, None], long_stats[None], 0.0), axis=1
    )
    cache_stats = jnp.where(own_is_long[:, None, None, None, None], from_long, stats[LONG_COUNT:])
    cache_mix = cache_stats[..., :HEAD_SIZE]
    cache_total = cache_stats[..., HEAD_SIZE]
    cache_top = cache_stats[..., HEAD_SIZE + 1]

    heads = own_query.reshape(own_rows, steps, kv_heads, head_sharing, HEAD_SIZE)
    fresh_keys = keys.reshape(steps, own_rows, kv_heads, HEAD_SIZE).transpose(1, 0, 2, 3)
    fresh_values = values.reshape(steps, own_rows, kv_heads, HEAD_SIZE).transpose(1, 0, 2, 3)
    fresh_scores = (
        jnp.einsum("rtngd,rjnd->rtngj", heads, fresh_keys, preferred_element_type=jnp.float32) * scaling
    )
    allowed = (jnp.arange(steps, dtype=jnp.int32)[None, :] <= jnp.arange(steps, dtype=jnp.int32)[:, None])[
        None, :, None, None, :
    ]
    fresh_top = jnp.max(jnp.where(allowed, fresh_scores, NEGATIVE), axis=-1)
    overall = jnp.maximum(cache_top, fresh_top)
    retained = jnp.exp(cache_top - overall)
    fresh_weights = jnp.where(
        allowed, jnp.exp(jnp.where(allowed, fresh_scores - overall[..., None], 0.0)), 0.0
    )
    denominator = cache_total * retained + jnp.sum(fresh_weights, axis=-1)
    mixture = cache_mix * retained[..., None] + jnp.einsum(
        "rtngj,rjnd->rtngd",
        fresh_weights.astype(jnp.bfloat16),
        fresh_values,
        preferred_element_type=jnp.float32,
    )
    attended = (mixture / denominator[..., None]).astype(jnp.bfloat16)
    attended = attended.transpose(1, 0, 2, 3, 4).reshape(steps * own_rows, q_heads * HEAD_SIZE)
    (projected,) = small_matmul(attended, w_out)
    projected = projected.reshape(steps, own_rows, -1)
    summed = reduce_scatter_mp(projected, n_mp)
    hidden = (states.astype(jnp.float32) + summed).astype(jnp.bfloat16)
    return hidden, new_keys, new_values


def solution(mesh):
    n_seq = mesh.shape["seq"]
    n_mp = mesh.shape["mp"]
    placed = (
        P(None, "seq", "mp"),
        P(),
        P(),
        P(),
        P(None, "mp"),
        P(None, "mp"),
        P(None, "mp"),
        P("mp", None),
        P("seq", None, "mp"),
        P("seq", None, "mp"),
        P(),
        P("seq"),
        P("seq"),
        P("seq"),
    )

    def body(*args):
        return shards(*args, n_seq=n_seq, n_mp=n_mp)

    return jax.shard_map(
        body,
        mesh=mesh,
        in_specs=placed,
        out_specs=(P(None, "seq", "mp"), P(None, "seq", "mp"), P(None, "seq", "mp")),
        check_vma=False,
    )
```

```python
import jax
import jax.numpy as jnp
from jax import lax
from jax.experimental import pallas as pl
from jax.experimental.pallas import tpu as pltpu
from jax.sharding import PartitionSpec as P

HEAD_SIZE = 128
LONG_COUNT = 12

ROPE_BASE = 1000000.0
NEGATIVE = -1e30
HIGHEST = lax.Precision.HIGHEST


def scaled_rms(values, gain):
    return values * lax.rsqrt(jnp.mean(values * values, axis=-1, keepdims=True) + 1e-06) * gain


def rotate(values, positions):
    halfway = values.shape[-1] // 2
    frequency = ROPE_BASE ** (-(jnp.arange(halfway, dtype=jnp.float32) * 2.0) / values.shape[-1])
    angles = positions.astype(jnp.float32)[..., None, None] * frequency
    cosine = jnp.cos(angles)
    sine_part = jnp.sin(angles)
    leading = values[..., :halfway]
    trailing = values[..., halfway:]
    return jnp.concatenate(
        [leading * cosine - trailing * sine_part, trailing * cosine + leading * sine_part], axis=-1
    )


def _matmul_kernel(x_ref, *refs):
    count = len(refs) // 2
    x = x_ref[...]
    for w_ref, o_ref in zip(refs[:count], refs[count:]):
        o_ref[...] = jnp.dot(x, w_ref[...], preferred_element_type=jnp.float32)


def _vmem():
    return pl.BlockSpec(memory_space=pltpu.VMEM)


def small_matmul(x, *weights):
    m, k = x.shape
    widths = [w.shape[1] for w in weights]
    return pl.pallas_call(
        _matmul_kernel,
        out_shape=[jax.ShapeDtypeStruct((m, n), jnp.float32) for n in widths],
        in_specs=[_vmem() for _ in range(1 + len(weights))],
        out_specs=[_vmem() for _ in widths],
        cost_estimate=pl.CostEstimate(
            flops=2 * m * k * sum(widths),
            bytes_accessed=2 * (m * k + k * sum(widths)) + 4 * m * sum(widths),
            transcendentals=0,
        ),
    )(x, *weights)


def _chunked_kernel(x_ref, w_ref, o_ref):
    chunks, _, width = o_ref.shape
    x = x_ref[...]
    for c in range(chunks):
        o_ref[c] = jnp.dot(x, w_ref[:, c * width : (c + 1) * width], preferred_element_type=jnp.float32)


def chunked_matmul(x, w, chunks):
    m, k = x.shape
    n = w.shape[1]
    return pl.pallas_call(
        _chunked_kernel,
        out_shape=jax.ShapeDtypeStruct((chunks, m, n // chunks), jnp.float32),
        in_specs=[_vmem(), _vmem()],
        out_specs=_vmem(),
        cost_estimate=pl.CostEstimate(
            flops=2 * m * k * n, bytes_accessed=2 * (m * k + k * n) + 4 * m * n, transcendentals=0
        ),
    )(x, w)


def gather_mp(block, n_mp):
    me = lax.axis_index("mp")
    pieces = [block] + [
        lax.ppermute(block, "mp", [(i, (i + s) % n_mp) for i in range(n_mp)]) for s in range(1, n_mp)
    ]
    ordered = []
    for c in range(n_mp):
        shift = (me - c) % n_mp
        chosen = pieces[0]
        for s in range(1, n_mp):
            chosen = jnp.where(shift == s, pieces[s], chosen)
        ordered.append(chosen)
    return jnp.concatenate(ordered, axis=-1)


def reduce_scatter_mp(chunks, n_mp):
    me = lax.axis_index("mp")
    total = lax.dynamic_index_in_dim(chunks, me, axis=0, keepdims=False)
    for s in range(1, n_mp):
        outgoing = lax.dynamic_index_in_dim(chunks, (me + s) % n_mp, axis=0, keepdims=False)
        total = total + lax.ppermute(outgoing, "mp", [(i, (i + s) % n_mp) for i in range(n_mp)])
    return total


def seq_masks(n_seq):
    if n_seq == 64:
        return [1, 2, 4, 12, 16, 48]
    return [1 << b for b in range(n_seq.bit_length() - 1)]


def butterfly(value, n_seq, combine):
    for stride in seq_masks(n_seq):
        partner = lax.ppermute(value, "seq", [(i, i ^ stride) for i in range(n_seq)])
        value = combine(value, partner)
    return value


def merge_stats(mine, theirs):
    mix_a, stats_a = mine
    mix_b, stats_b = theirs
    top_a = stats_a[1:]
    top_b = stats_b[1:]
    top = jnp.maximum(top_a, top_b)
    scale_a = jnp.exp(top_a - top)
    scale_b = jnp.exp(top_b - top)
    mix = mix_a * scale_a + mix_b.astype(jnp.float32) * scale_b
    total = stats_a[:1] * scale_a + stats_b[:1] * scale_b
    return mix, jnp.concatenate([total, top], axis=0)


def split_exact(x):
    hi = lax.reduce_precision(x, exponent_bits=8, mantissa_bits=7)
    rest = x - hi
    mid = lax.reduce_precision(rest, exponent_bits=8, mantissa_bits=7)
    lo = rest - mid
    return jnp.concatenate([hi, mid, lo], axis=0).astype(jnp.bfloat16)


def join_exact(parts):
    parts = parts.astype(jnp.float32)
    return parts[0:1] + parts[1:2] + parts[2:3]


def stats_butterfly(mix, stats, n_seq):
    width = mix.shape[0]
    for stride in seq_masks(n_seq):
        pairs = [(i, i ^ stride) for i in range(n_seq)]
        packed = jnp.concatenate(
            [mix.astype(jnp.bfloat16), split_exact(stats[:1]), split_exact(stats[1:])], axis=0
        )
        arrived = lax.ppermute(packed, "seq", pairs)
        theirs = (
            arrived[:width],
            jnp.concatenate(
                [join_exact(arrived[width : width + 3]), join_exact(arrived[width + 3 : width + 6])], axis=0
            ),
        )
        mix, stats = merge_stats((mix, stats), theirs)
    return mix, stats


def shards(
    states,
    norm_gain,
    query_gain,
    key_gain,
    w_query,
    key_matrix,
    value_matrix,
    w_out,
    cached_key_blocks,
    cached_value_blocks,
    req_len,
    slot_request,
    slot_block,
    slot_empty,
    n_seq,
    n_mp,
):
    steps, own_rows, _ = states.shape
    me = lax.axis_index("seq")
    first_row = me * own_rows
    kv_heads = key_matrix.shape[1] // HEAD_SIZE
    q_heads = w_query.shape[1] // HEAD_SIZE
    head_sharing = q_heads // kv_heads
    slot_count, block_len, _ = cached_key_blocks.shape
    requests = req_len.shape[0]
    long_len = n_seq * block_len
    scaling = HEAD_SIZE ** (-0.5)

    wide = gather_mp(states, n_mp).reshape(steps * own_rows, -1)
    own_ids = first_row + jnp.arange(own_rows, dtype=jnp.int32)
    own_len = lax.dynamic_slice_in_dim(req_len, first_row, own_rows)
    positions = (own_len[None, :] + jnp.arange(steps, dtype=jnp.int32)[:, None]).reshape(-1)
    normed = scaled_rms(wide.astype(jnp.float32), norm_gain).astype(jnp.bfloat16)
    rows = steps * own_rows
    query, keys, values = small_matmul(normed, w_query, key_matrix, value_matrix)
    query = query.reshape(rows, q_heads, HEAD_SIZE)
    keys = keys.reshape(rows, kv_heads, HEAD_SIZE)
    values = values.astype(jnp.bfloat16)
    query = rotate(scaled_rms(query, query_gain), positions).astype(jnp.bfloat16)
    keys = rotate(scaled_rms(keys, key_gain), positions).astype(jnp.bfloat16)
    new_keys = keys.reshape(steps, own_rows, kv_heads * HEAD_SIZE)
    new_values = values.reshape(steps, own_rows, kv_heads * HEAD_SIZE)
    own_query = query.reshape(steps, own_rows, q_heads, HEAD_SIZE).transpose(1, 0, 2, 3)

    request_ids = jnp.arange(requests, dtype=jnp.int32)
    is_long = req_len == long_len
    long_count = is_long.astype(jnp.int32)
    rank = jnp.sum(
        jnp.where(request_ids[None, :] < request_ids[:, None], long_count[None, :], 0), axis=1
    )
    long_ids = jnp.sum(
        jnp.where(
            is_long[None, :] & (rank[None, :] == jnp.arange(LONG_COUNT, dtype=jnp.int32)[:, None]),
            request_ids[None, :],
            0,
        ),
        axis=1,
    )
    own_pick = long_ids[:, None] == own_ids[None, :]
    long_table = jnp.sum(
        jnp.where(own_pick[:, :, None, None, None], own_query[None], jnp.zeros((), jnp.bfloat16)), axis=1
    ).astype(jnp.bfloat16)
    long_table = butterfly(long_table, n_seq, lambda a, b: a + b)

    hit = slot_request[:, None] == request_ids[None, :]
    slot_req_long = jnp.any(hit & is_long[None, :], axis=1)
    slot_rank = jnp.sum(jnp.where(hit, rank[None, :], 0), axis=1)
    slot_len = jnp.sum(jnp.where(hit, req_len[None, :], 0), axis=1)
    local_row = slot_request - first_row
    slot_local = (local_row >= 0) & (local_row < own_rows)
    pick = jnp.where(
        slot_req_long, slot_rank, jnp.where(slot_local, LONG_COUNT + local_row, LONG_COUNT + own_rows)
    )
    candidates = jnp.concatenate(
        [long_table, own_query, jnp.zeros((1,) + own_query.shape[1:], jnp.bfloat16)], axis=0
    )
    slot_query = jnp.take(candidates, pick, axis=0).reshape(
        slot_count, steps, kv_heads, head_sharing, HEAD_SIZE
    )
    keys_split = cached_key_blocks.reshape(slot_count, block_len, kv_heads, HEAD_SIZE)
    values_split = cached_value_blocks.reshape(slot_count, block_len, kv_heads, HEAD_SIZE)
    scores = (
        jnp.einsum("stngd,sknd->stngk", slot_query, keys_split, preferred_element_type=jnp.float32)
        * scaling
    )
    kept = slot_empty == 0
    filled = kept[:, None] & (
        slot_block[:, None] * block_len + jnp.arange(block_len, dtype=jnp.int32)[None, :] < slot_len[:, None]
    )
    filled_wide = filled[:, None, None, None, :]
    slot_top = jnp.max(jnp.where(filled_wide, scores, NEGATIVE), axis=-1)
    same = (slot_request[:, None] == slot_request[None, :]) & kept[None, :]
    reference_top = jnp.max(
        jnp.where(same[:, :, None, None, None], slot_top[None], NEGATIVE), axis=1
    )
    weights = jnp.where(
        filled_wide, jnp.exp(jnp.where(filled_wide, scores - reference_top[..., None], 0.0)), 0.0
    )
    slot_total = jnp.sum(weights, axis=-1)
    slot_mix = jnp.einsum(
        "stngk,sknd->stngd", weights.astype(jnp.bfloat16), values_split, preferred_element_type=jnp.float32
    )

    group_ids = jnp.concatenate([long_ids, own_ids])
    member = (group_ids[:, None] == slot_request[None, :]) & kept[None, :]
    member_float = member.astype(jnp.float32)
    group_top = jnp.max(jnp.where(member[:, :, None, None, None], reference_top[None], NEGATIVE), axis=1)
    group_total = jnp.einsum("qs,stng->qtng", member_float, slot_total, precision=HIGHEST)
    group_mix = jnp.einsum("qs,stngd->qtngd", member_float, slot_mix, precision=HIGHEST)
    stats = jnp.concatenate(
        [group_mix, group_total[..., None], group_top[..., None]], axis=-1
    )
    long_stats = stats[:LONG_COUNT].reshape(-1, HEAD_SIZE + 2).T
    long_mix, long_small = stats_butterfly(long_stats[:HEAD_SIZE], long_stats[HEAD_SIZE:], n_seq)
    long_stats = jnp.concatenate([long_mix, long_small], axis=0)
    long_stats = long_stats.T.reshape((LONG_COUNT,) + stats.shape[1:])
    own_rank = lax.dynamic_slice_in_dim(rank, first_row, own_rows)
    own_is_long = lax.dynamic_slice_in_dim(is_long, first_row, own_rows)
    rank_hit = own_rank[:, None] == jnp.arange(LONG_COUNT, dtype=jnp.int32)[None, :]
    from_long = jnp.sum(
        jnp.where(rank_hit[:, :, None, None, None, None], long_stats[None], 0.0), axis=1
    )
    cache_stats = jnp.where(own_is_long[:, None, None, None, None], from_long, stats[LONG_COUNT:])
    cache_mix = cache_stats[..., :HEAD_SIZE]
    cache_total = cache_stats[..., HEAD_SIZE]
    cache_top = cache_stats[..., HEAD_SIZE + 1]

    heads = own_query.reshape(own_rows, steps, kv_heads, head_sharing, HEAD_SIZE)
    fresh_keys = keys.reshape(steps, own_rows, kv_heads, HEAD_SIZE).transpose(1, 0, 2, 3)
    fresh_values = values.reshape(steps, own_rows, kv_heads, HEAD_SIZE).transpose(1, 0, 2, 3)
    fresh_scores = (
        jnp.einsum("rtngd,rjnd->rtngj", heads, fresh_keys, preferred_element_type=jnp.float32) * scaling
    )
    allowed = (jnp.arange(steps, dtype=jnp.int32)[None, :] <= jnp.arange(steps, dtype=jnp.int32)[:, None])[
        None, :, None, None, :
    ]
    fresh_top = jnp.max(jnp.where(allowed, fresh_scores, NEGATIVE), axis=-1)
    overall = jnp.maximum(cache_top, fresh_top)
    retained = jnp.exp(cache_top - overall)
    fresh_weights = jnp.where(
        allowed, jnp.exp(jnp.where(allowed, fresh_scores - overall[..., None], 0.0)), 0.0
    )
    denominator = cache_total * retained + jnp.sum(fresh_weights, axis=-1)
    mixture = cache_mix * retained[..., None] + jnp.einsum(
        "rtngj,rjnd->rtngd",
        fresh_weights.astype(jnp.bfloat16),
        fresh_values,
        preferred_element_type=jnp.float32,
    )
    attended = (mixture / denominator[..., None]).astype(jnp.bfloat16)
    attended = attended.transpose(1, 0, 2, 3, 4).reshape(steps * own_rows, q_heads * HEAD_SIZE)
    projected = chunked_matmul(attended, w_out, n_mp)
    summed = reduce_scatter_mp(projected, n_mp).reshape(steps, own_rows, -1)
    hidden = (states.astype(jnp.float32) + summed).astype(jnp.bfloat16)
    return hidden, new_keys, new_values


def solution(mesh):
    n_seq = mesh.shape["seq"]
    n_mp = mesh.shape["mp"]
    placed = (
        P(None, "seq", "mp"),
        P(),
        P(),
        P(),
        P(None, "mp"),
        P(None, "mp"),
        P(None, "mp"),
        P("mp", None),
        P("seq", None, "mp"),
        P("seq", None, "mp"),
        P(),
        P("seq"),
        P("seq"),
        P("seq"),
    )

    def body(*args):
        return shards(*args, n_seq=n_seq, n_mp=n_mp)

    return jax.shard_map(
        body,
        mesh=mesh,
        in_specs=placed,
        out_specs=(P(None, "seq", "mp"), P(None, "seq", "mp"), P(None, "seq", "mp")),
        check_vma=False,
    )
```

```python
import jax
import jax.numpy as jnp
from jax import lax
from jax.experimental import pallas as pl
from jax.experimental.pallas import tpu as pltpu
from jax.sharding import PartitionSpec as P

HEAD_SIZE = 128
LONG_COUNT = 12

ROPE_BASE = 1000000.0
NEGATIVE = -1e30
HIGHEST = lax.Precision.HIGHEST


def scaled_rms(values, gain):
    return values * lax.rsqrt(jnp.mean(values * values, axis=-1, keepdims=True) + 1e-06) * gain


def rotate(values, positions):
    halfway = values.shape[-1] // 2
    frequency = ROPE_BASE ** (-(jnp.arange(halfway, dtype=jnp.float32) * 2.0) / values.shape[-1])
    angles = positions.astype(jnp.float32)[..., None, None] * frequency
    cosine = jnp.cos(angles)
    sine_part = jnp.sin(angles)
    leading = values[..., :halfway]
    trailing = values[..., halfway:]
    return jnp.concatenate(
        [leading * cosine - trailing * sine_part, trailing * cosine + leading * sine_part], axis=-1
    )


def _matmul_kernel(x_ref, *refs):
    count = len(refs) // 2
    x = x_ref[...]
    for w_ref, o_ref in zip(refs[:count], refs[count:]):
        o_ref[...] = jnp.dot(x, w_ref[...], preferred_element_type=jnp.float32)


def _vmem():
    return pl.BlockSpec(memory_space=pltpu.VMEM)


def small_matmul(x, *weights):
    m, k = x.shape
    widths = [w.shape[1] for w in weights]
    return pl.pallas_call(
        _matmul_kernel,
        out_shape=[jax.ShapeDtypeStruct((m, n), jnp.float32) for n in widths],
        in_specs=[_vmem() for _ in range(1 + len(weights))],
        out_specs=[_vmem() for _ in widths],
        cost_estimate=pl.CostEstimate(
            flops=2 * m * k * sum(widths),
            bytes_accessed=2 * (m * k + k * sum(widths)) + 4 * m * sum(widths),
            transcendentals=0,
        ),
    )(x, *weights)


def _chunked_kernel(x_ref, w_ref, o_ref):
    chunks, _, width = o_ref.shape
    x = x_ref[...]
    for c in range(chunks):
        o_ref[c] = jnp.dot(x, w_ref[:, c * width : (c + 1) * width], preferred_element_type=jnp.float32)


def chunked_matmul(x, w, chunks):
    m, k = x.shape
    n = w.shape[1]
    return pl.pallas_call(
        _chunked_kernel,
        out_shape=jax.ShapeDtypeStruct((chunks, m, n // chunks), jnp.float32),
        in_specs=[_vmem(), _vmem()],
        out_specs=_vmem(),
        cost_estimate=pl.CostEstimate(
            flops=2 * m * k * n, bytes_accessed=2 * (m * k + k * n) + 4 * m * n, transcendentals=0
        ),
    )(x, w)


def gather_mp(block, n_mp):
    me = lax.axis_index("mp")
    pieces = [block] + [
        lax.ppermute(block, "mp", [(i, (i + s) % n_mp) for i in range(n_mp)]) for s in range(1, n_mp)
    ]
    ordered = []
    for c in range(n_mp):
        shift = (me - c) % n_mp
        chosen = pieces[0]
        for s in range(1, n_mp):
            chosen = jnp.where(shift == s, pieces[s], chosen)
        ordered.append(chosen)
    return jnp.concatenate(ordered, axis=-1)


def reduce_scatter_mp(chunks, n_mp):
    me = lax.axis_index("mp")

    def chunk(index):
        return lax.dynamic_index_in_dim(chunks, index, axis=0, keepdims=False)

    if n_mp == 4:
        first = [(i, i ^ 1) for i in range(n_mp)]
        second = [(i, i ^ 3) for i in range(n_mp)]
        sent = lax.ppermute(jnp.stack([chunk(me ^ 1), chunk(me ^ 2)]), "mp", first)
        mine = chunk(me) + sent[0]
        other = chunk(me ^ 3) + sent[1]
        return mine + lax.ppermute(other, "mp", second)
    total = chunk(me)
    for s in range(1, n_mp):
        outgoing = chunk((me + s) % n_mp)
        total = total + lax.ppermute(outgoing, "mp", [(i, (i + s) % n_mp) for i in range(n_mp)])
    return total


def seq_masks(n_seq):
    if n_seq == 64:
        return [1, 2, 4, 12, 16, 48]
    return [1 << b for b in range(n_seq.bit_length() - 1)]


def butterfly(value, n_seq, combine):
    for stride in seq_masks(n_seq):
        partner = lax.ppermute(value, "seq", [(i, i ^ stride) for i in range(n_seq)])
        value = combine(value, partner)
    return value


def merge_stats(mine, theirs):
    mix_a, stats_a = mine
    mix_b, stats_b = theirs
    top_a = stats_a[1:]
    top_b = stats_b[1:]
    top = jnp.maximum(top_a, top_b)
    scale_a = jnp.exp(top_a - top)
    scale_b = jnp.exp(top_b - top)
    mix = mix_a * scale_a + mix_b.astype(jnp.float32) * scale_b
    total = stats_a[:1] * scale_a + stats_b[:1] * scale_b
    return mix, jnp.concatenate([total, top], axis=0)


def split_exact(x):
    hi = lax.reduce_precision(x, exponent_bits=8, mantissa_bits=7)
    rest = x - hi
    mid = lax.reduce_precision(rest, exponent_bits=8, mantissa_bits=7)
    lo = rest - mid
    return jnp.concatenate([hi, mid, lo], axis=0).astype(jnp.bfloat16)


def join_exact(parts):
    parts = parts.astype(jnp.float32)
    return parts[0:1] + parts[1:2] + parts[2:3]


def stats_butterfly(mix, stats, n_seq):
    width = mix.shape[0]
    for stride in seq_masks(n_seq):
        pairs = [(i, i ^ stride) for i in range(n_seq)]
        packed = jnp.concatenate(
            [mix.astype(jnp.bfloat16), split_exact(stats[:1]), split_exact(stats[1:])], axis=0
        )
        arrived = lax.ppermute(packed, "seq", pairs)
        theirs = (
            arrived[:width],
            jnp.concatenate(
                [join_exact(arrived[width : width + 3]), join_exact(arrived[width + 3 : width + 6])], axis=0
            ),
        )
        mix, stats = merge_stats((mix, stats), theirs)
    return mix, stats


def shards(
    states,
    norm_gain,
    query_gain,
    key_gain,
    w_query,
    key_matrix,
    value_matrix,
    w_out,
    cached_key_blocks,
    cached_value_blocks,
    req_len,
    slot_request,
    slot_block,
    slot_empty,
    n_seq,
    n_mp,
):
    steps, own_rows, _ = states.shape
    me = lax.axis_index("seq")
    first_row = me * own_rows
    kv_heads = key_matrix.shape[1] // HEAD_SIZE
    q_heads = w_query.shape[1] // HEAD_SIZE
    head_sharing = q_heads // kv_heads
    slot_count, block_len, _ = cached_key_blocks.shape
    requests = req_len.shape[0]
    long_len = n_seq * block_len
    scaling = HEAD_SIZE ** (-0.5)

    wide = gather_mp(states, n_mp).reshape(steps * own_rows, -1)
    own_ids = first_row + jnp.arange(own_rows, dtype=jnp.int32)
    own_len = lax.dynamic_slice_in_dim(req_len, first_row, own_rows)
    positions = (own_len[None, :] + jnp.arange(steps, dtype=jnp.int32)[:, None]).reshape(-1)
    normed = scaled_rms(wide.astype(jnp.float32), norm_gain).astype(jnp.bfloat16)
    rows = steps * own_rows
    query, keys, values = small_matmul(normed, w_query, key_matrix, value_matrix)
    query = query.reshape(rows, q_heads, HEAD_SIZE)
    keys = keys.reshape(rows, kv_heads, HEAD_SIZE)
    values = values.astype(jnp.bfloat16)
    query = rotate(scaled_rms(query, query_gain), positions).astype(jnp.bfloat16)
    keys = rotate(scaled_rms(keys, key_gain), positions).astype(jnp.bfloat16)
    new_keys = keys.reshape(steps, own_rows, kv_heads * HEAD_SIZE)
    new_values = values.reshape(steps, own_rows, kv_heads * HEAD_SIZE)
    own_query = query.reshape(steps, own_rows, q_heads, HEAD_SIZE).transpose(1, 0, 2, 3)

    request_ids = jnp.arange(requests, dtype=jnp.int32)
    is_long = req_len == long_len
    long_count = is_long.astype(jnp.int32)
    rank = jnp.sum(
        jnp.where(request_ids[None, :] < request_ids[:, None], long_count[None, :], 0), axis=1
    )
    long_ids = jnp.sum(
        jnp.where(
            is_long[None, :] & (rank[None, :] == jnp.arange(LONG_COUNT, dtype=jnp.int32)[:, None]),
            request_ids[None, :],
            0,
        ),
        axis=1,
    )
    own_pick = long_ids[:, None] == own_ids[None, :]
    long_table = jnp.sum(
        jnp.where(own_pick[:, :, None, None, None], own_query[None], jnp.zeros((), jnp.bfloat16)), axis=1
    ).astype(jnp.bfloat16)
    long_table = butterfly(long_table, n_seq, lambda a, b: a + b)

    hit = slot_request[:, None] == request_ids[None, :]
    slot_req_long = jnp.any(hit & is_long[None, :], axis=1)
    slot_rank = jnp.sum(jnp.where(hit, rank[None, :], 0), axis=1)
    slot_len = jnp.sum(jnp.where(hit, req_len[None, :], 0), axis=1)
    local_row = slot_request - first_row
    slot_local = (local_row >= 0) & (local_row < own_rows)
    pick = jnp.where(
        slot_req_long, slot_rank, jnp.where(slot_local, LONG_COUNT + local_row, LONG_COUNT + own_rows)
    )
    candidates = jnp.concatenate(
        [long_table, own_query, jnp.zeros((1,) + own_query.shape[1:], jnp.bfloat16)], axis=0
    )
    slot_query = jnp.take(candidates, pick, axis=0).reshape(
        slot_count, steps, kv_heads, head_sharing, HEAD_SIZE
    )
    keys_split = cached_key_blocks.reshape(slot_count, block_len, kv_heads, HEAD_SIZE)
    values_split = cached_value_blocks.reshape(slot_count, block_len, kv_heads, HEAD_SIZE)
    scores = (
        jnp.einsum("stngd,sknd->stngk", slot_query, keys_split, preferred_element_type=jnp.float32)
        * scaling
    )
    kept = slot_empty == 0
    filled = kept[:, None] & (
        slot_block[:, None] * block_len + jnp.arange(block_len, dtype=jnp.int32)[None, :] < slot_len[:, None]
    )
    filled_wide = filled[:, None, None, None, :]
    slot_top = jnp.max(jnp.where(filled_wide, scores, NEGATIVE), axis=-1)
    same = (slot_request[:, None] == slot_request[None, :]) & kept[None, :]
    reference_top = jnp.max(
        jnp.where(same[:, :, None, None, None], slot_top[None], NEGATIVE), axis=1
    )
    weights = jnp.where(
        filled_wide, jnp.exp(jnp.where(filled_wide, scores - reference_top[..., None], 0.0)), 0.0
    )
    slot_total = jnp.sum(weights, axis=-1)
    slot_mix = jnp.einsum(
        "stngk,sknd->stngd", weights.astype(jnp.bfloat16), values_split, preferred_element_type=jnp.float32
    )

    group_ids = jnp.concatenate([long_ids, own_ids])
    member = (group_ids[:, None] == slot_request[None, :]) & kept[None, :]
    member_float = member.astype(jnp.float32)
    group_top = jnp.max(jnp.where(member[:, :, None, None, None], reference_top[None], NEGATIVE), axis=1)
    group_total = jnp.einsum("qs,stng->qtng", member_float, slot_total, precision=HIGHEST)
    group_mix = jnp.einsum("qs,stngd->qtngd", member_float, slot_mix, precision=HIGHEST)
    stats = jnp.concatenate(
        [group_mix, group_total[..., None], group_top[..., None]], axis=-1
    )
    long_stats = stats[:LONG_COUNT].reshape(-1, HEAD_SIZE + 2).T
    long_mix, long_small = stats_butterfly(long_stats[:HEAD_SIZE], long_stats[HEAD_SIZE:], n_seq)
    long_stats = jnp.concatenate([long_mix, long_small], axis=0)
    long_stats = long_stats.T.reshape((LONG_COUNT,) + stats.shape[1:])
    own_rank = lax.dynamic_slice_in_dim(rank, first_row, own_rows)
    own_is_long = lax.dynamic_slice_in_dim(is_long, first_row, own_rows)
    rank_hit = own_rank[:, None] == jnp.arange(LONG_COUNT, dtype=jnp.int32)[None, :]
    from_long = jnp.sum(
        jnp.where(rank_hit[:, :, None, None, None, None], long_stats[None], 0.0), axis=1
    )
    cache_stats = jnp.where(own_is_long[:, None, None, None, None], from_long, stats[LONG_COUNT:])
    cache_mix = cache_stats[..., :HEAD_SIZE]
    cache_total = cache_stats[..., HEAD_SIZE]
    cache_top = cache_stats[..., HEAD_SIZE + 1]

    heads = own_query.reshape(own_rows, steps, kv_heads, head_sharing, HEAD_SIZE)
    fresh_keys = keys.reshape(steps, own_rows, kv_heads, HEAD_SIZE).transpose(1, 0, 2, 3)
    fresh_values = values.reshape(steps, own_rows, kv_heads, HEAD_SIZE).transpose(1, 0, 2, 3)
    fresh_scores = (
        jnp.einsum("rtngd,rjnd->rtngj", heads, fresh_keys, preferred_element_type=jnp.float32) * scaling
    )
    allowed = (jnp.arange(steps, dtype=jnp.int32)[None, :] <= jnp.arange(steps, dtype=jnp.int32)[:, None])[
        None, :, None, None, :
    ]
    fresh_top = jnp.max(jnp.where(allowed, fresh_scores, NEGATIVE), axis=-1)
    overall = jnp.maximum(cache_top, fresh_top)
    retained = jnp.exp(cache_top - overall)
    fresh_weights = jnp.where(
        allowed, jnp.exp(jnp.where(allowed, fresh_scores - overall[..., None], 0.0)), 0.0
    )
    denominator = cache_total * retained + jnp.sum(fresh_weights, axis=-1)
    mixture = cache_mix * retained[..., None] + jnp.einsum(
        "rtngj,rjnd->rtngd",
        fresh_weights.astype(jnp.bfloat16),
        fresh_values,
        preferred_element_type=jnp.float32,
    )
    attended = (mixture / denominator[..., None]).astype(jnp.bfloat16)
    attended = attended.transpose(1, 0, 2, 3, 4).reshape(steps * own_rows, q_heads * HEAD_SIZE)
    projected = chunked_matmul(attended, w_out, n_mp)
    summed = reduce_scatter_mp(projected, n_mp).reshape(steps, own_rows, -1)
    hidden = (states.astype(jnp.float32) + summed).astype(jnp.bfloat16)
    return hidden, new_keys, new_values


def solution(mesh):
    n_seq = mesh.shape["seq"]
    n_mp = mesh.shape["mp"]
    placed = (
        P(None, "seq", "mp"),
        P(),
        P(),
        P(),
        P(None, "mp"),
        P(None, "mp"),
        P(None, "mp"),
        P("mp", None),
        P("seq", None, "mp"),
        P("seq", None, "mp"),
        P(),
        P("seq"),
        P("seq"),
        P("seq"),
    )

    def body(*args):
        return shards(*args, n_seq=n_seq, n_mp=n_mp)

    return jax.shard_map(
        body,
        mesh=mesh,
        in_specs=placed,
        out_specs=(P(None, "seq", "mp"), P(None, "seq", "mp"), P(None, "seq", "mp")),
        check_vma=False,
    )
```

```python
import jax
import jax.numpy as jnp
from jax import lax
from jax.experimental import pallas as pl
from jax.experimental.pallas import tpu as pltpu
from jax.sharding import PartitionSpec as P

HEAD_SIZE = 128
LONG_COUNT = 12

ROPE_BASE = 1000000.0
NEGATIVE = -1e30
HIGHEST = lax.Precision.HIGHEST


def scaled_rms(values, gain):
    return values * lax.rsqrt(jnp.mean(values * values, axis=-1, keepdims=True) + 1e-06) * gain


def rotate(values, positions):
    halfway = values.shape[-1] // 2
    frequency = ROPE_BASE ** (-(jnp.arange(halfway, dtype=jnp.float32) * 2.0) / values.shape[-1])
    angles = positions.astype(jnp.float32)[..., None, None] * frequency
    cosine = jnp.cos(angles)
    sine_part = jnp.sin(angles)
    leading = values[..., :halfway]
    trailing = values[..., halfway:]
    return jnp.concatenate(
        [leading * cosine - trailing * sine_part, trailing * cosine + leading * sine_part], axis=-1
    )


def _matmul_kernel(x_ref, *refs):
    count = len(refs) // 2
    x = x_ref[...]
    for w_ref, o_ref in zip(refs[:count], refs[count:]):
        o_ref[...] = jnp.dot(x, w_ref[...], preferred_element_type=jnp.float32)


def _vmem():
    return pl.BlockSpec(memory_space=pltpu.VMEM)


def small_matmul(x, *weights):
    m, k = x.shape
    widths = [w.shape[1] for w in weights]
    return pl.pallas_call(
        _matmul_kernel,
        out_shape=[jax.ShapeDtypeStruct((m, n), jnp.float32) for n in widths],
        in_specs=[_vmem() for _ in range(1 + len(weights))],
        out_specs=[_vmem() for _ in widths],
        cost_estimate=pl.CostEstimate(
            flops=2 * m * k * sum(widths),
            bytes_accessed=2 * (m * k + k * sum(widths)) + 4 * m * sum(widths),
            transcendentals=0,
        ),
    )(x, *weights)


def _chunked_kernel(x_ref, w_ref, o_ref):
    chunks, _, width = o_ref.shape
    x = x_ref[...]
    for c in range(chunks):
        o_ref[c] = jnp.dot(x, w_ref[:, c * width : (c + 1) * width], preferred_element_type=jnp.float32)


def chunked_matmul(x, w, chunks):
    m, k = x.shape
    n = w.shape[1]
    return pl.pallas_call(
        _chunked_kernel,
        out_shape=jax.ShapeDtypeStruct((chunks, m, n // chunks), jnp.float32),
        in_specs=[_vmem(), _vmem()],
        out_specs=_vmem(),
        cost_estimate=pl.CostEstimate(
            flops=2 * m * k * n, bytes_accessed=2 * (m * k + k * n) + 4 * m * n, transcendentals=0
        ),
    )(x, w)


def gather_mp(block, n_mp):
    me = lax.axis_index("mp")
    pieces = [block] + [
        lax.ppermute(block, "mp", [(i, (i + s) % n_mp) for i in range(n_mp)]) for s in range(1, n_mp)
    ]
    ordered = []
    for c in range(n_mp):
        shift = (me - c) % n_mp
        chosen = pieces[0]
        for s in range(1, n_mp):
            chosen = jnp.where(shift == s, pieces[s], chosen)
        ordered.append(chosen)
    return jnp.concatenate(ordered, axis=-1)


def reduce_scatter_mp(full, n_mp):
    me = lax.axis_index("mp")
    width = full.shape[-1] // n_mp
    pieces = [full[:, c * width : (c + 1) * width] for c in range(n_mp)]

    def chunk(index):
        chosen = pieces[0]
        for c in range(1, n_mp):
            chosen = jnp.where(index == c, pieces[c], chosen)
        return chosen

    total = chunk(me)
    for s in range(1, n_mp):
        outgoing = chunk((me + s) % n_mp)
        total = total + lax.ppermute(outgoing, "mp", [(i, (i + s) % n_mp) for i in range(n_mp)])
    return total


def seq_masks(n_seq):
    if n_seq == 64:
        return [1, 2, 4, 12, 16, 48]
    return [1 << b for b in range(n_seq.bit_length() - 1)]


def butterfly(value, n_seq, combine):
    for stride in seq_masks(n_seq):
        partner = lax.ppermute(value, "seq", [(i, i ^ stride) for i in range(n_seq)])
        value = combine(value, partner)
    return value


def merge_stats(mine, theirs):
    mix_a, stats_a = mine
    mix_b, stats_b = theirs
    top_a = stats_a[1:]
    top_b = stats_b[1:]
    top = jnp.maximum(top_a, top_b)
    scale_a = jnp.exp(top_a - top)
    scale_b = jnp.exp(top_b - top)
    mix = mix_a * scale_a + mix_b.astype(jnp.float32) * scale_b
    total = stats_a[:1] * scale_a + stats_b[:1] * scale_b
    return mix, jnp.concatenate([total, top], axis=0)


def split_exact(x):
    hi = lax.reduce_precision(x, exponent_bits=8, mantissa_bits=7)
    rest = x - hi
    mid = lax.reduce_precision(rest, exponent_bits=8, mantissa_bits=7)
    lo = rest - mid
    return jnp.concatenate([hi, mid, lo], axis=0).astype(jnp.bfloat16)


def join_exact(parts):
    parts = parts.astype(jnp.float32)
    return parts[0:1] + parts[1:2] + parts[2:3]


def stats_butterfly(mix, stats, n_seq):
    width = mix.shape[0]
    for stride in seq_masks(n_seq):
        pairs = [(i, i ^ stride) for i in range(n_seq)]
        packed = jnp.concatenate(
            [mix.astype(jnp.bfloat16), split_exact(stats[:1]), split_exact(stats[1:])], axis=0
        )
        arrived = lax.ppermute(packed, "seq", pairs)
        theirs = (
            arrived[:width],
            jnp.concatenate(
                [join_exact(arrived[width : width + 3]), join_exact(arrived[width + 3 : width + 6])], axis=0
            ),
        )
        mix, stats = merge_stats((mix, stats), theirs)
    return mix, stats


def shards(
    states,
    norm_gain,
    query_gain,
    key_gain,
    w_query,
    key_matrix,
    value_matrix,
    w_out,
    cached_key_blocks,
    cached_value_blocks,
    req_len,
    slot_request,
    slot_block,
    slot_empty,
    n_seq,
    n_mp,
):
    steps, own_rows, _ = states.shape
    me = lax.axis_index("seq")
    first_row = me * own_rows
    kv_heads = key_matrix.shape[1] // HEAD_SIZE
    q_heads = w_query.shape[1] // HEAD_SIZE
    head_sharing = q_heads // kv_heads
    slot_count, block_len, _ = cached_key_blocks.shape
    requests = req_len.shape[0]
    long_len = n_seq * block_len
    scaling = HEAD_SIZE ** (-0.5)

    wide = gather_mp(states, n_mp).reshape(steps * own_rows, -1)
    own_ids = first_row + jnp.arange(own_rows, dtype=jnp.int32)
    own_len = lax.dynamic_slice_in_dim(req_len, first_row, own_rows)
    positions = (own_len[None, :] + jnp.arange(steps, dtype=jnp.int32)[:, None]).reshape(-1)
    normed = scaled_rms(wide.astype(jnp.float32), norm_gain).astype(jnp.bfloat16)
    rows = steps * own_rows
    query, keys, values = small_matmul(normed, w_query, key_matrix, value_matrix)
    query = query.reshape(rows, q_heads, HEAD_SIZE)
    keys = keys.reshape(rows, kv_heads, HEAD_SIZE)
    values = values.astype(jnp.bfloat16)
    query = rotate(scaled_rms(query, query_gain), positions).astype(jnp.bfloat16)
    keys = rotate(scaled_rms(keys, key_gain), positions).astype(jnp.bfloat16)
    new_keys = keys.reshape(steps, own_rows, kv_heads * HEAD_SIZE)
    new_values = values.reshape(steps, own_rows, kv_heads * HEAD_SIZE)
    own_query = query.reshape(steps, own_rows, q_heads, HEAD_SIZE).transpose(1, 0, 2, 3)

    request_ids = jnp.arange(requests, dtype=jnp.int32)
    is_long = req_len == long_len
    long_count = is_long.astype(jnp.int32)
    rank = jnp.sum(
        jnp.where(request_ids[None, :] < request_ids[:, None], long_count[None, :], 0), axis=1
    )
    long_ids = jnp.sum(
        jnp.where(
            is_long[None, :] & (rank[None, :] == jnp.arange(LONG_COUNT, dtype=jnp.int32)[:, None]),
            request_ids[None, :],
            0,
        ),
        axis=1,
    )
    own_pick = long_ids[:, None] == own_ids[None, :]
    long_table = jnp.sum(
        jnp.where(own_pick[:, :, None, None, None], own_query[None], jnp.zeros((), jnp.bfloat16)), axis=1
    ).astype(jnp.bfloat16)
    long_table = butterfly(long_table, n_seq, lambda a, b: a + b)

    hit = slot_request[:, None] == request_ids[None, :]
    slot_req_long = jnp.any(hit & is_long[None, :], axis=1)
    slot_rank = jnp.sum(jnp.where(hit, rank[None, :], 0), axis=1)
    slot_len = jnp.sum(jnp.where(hit, req_len[None, :], 0), axis=1)
    local_row = slot_request - first_row
    slot_local = (local_row >= 0) & (local_row < own_rows)
    pick = jnp.where(
        slot_req_long, slot_rank, jnp.where(slot_local, LONG_COUNT + local_row, LONG_COUNT + own_rows)
    )
    candidates = jnp.concatenate(
        [long_table, own_query, jnp.zeros((1,) + own_query.shape[1:], jnp.bfloat16)], axis=0
    )
    slot_query = jnp.take(candidates, pick, axis=0).reshape(
        slot_count, steps, kv_heads, head_sharing, HEAD_SIZE
    )
    keys_split = cached_key_blocks.reshape(slot_count, block_len, kv_heads, HEAD_SIZE)
    values_split = cached_value_blocks.reshape(slot_count, block_len, kv_heads, HEAD_SIZE)
    scores = (
        jnp.einsum("stngd,sknd->stngk", slot_query, keys_split, preferred_element_type=jnp.float32)
        * scaling
    )
    kept = slot_empty == 0
    filled = kept[:, None] & (
        slot_block[:, None] * block_len + jnp.arange(block_len, dtype=jnp.int32)[None, :] < slot_len[:, None]
    )
    filled_wide = filled[:, None, None, None, :]
    slot_top = jnp.max(jnp.where(filled_wide, scores, NEGATIVE), axis=-1)
    same = (slot_request[:, None] == slot_request[None, :]) & kept[None, :]
    reference_top = jnp.max(
        jnp.where(same[:, :, None, None, None], slot_top[None], NEGATIVE), axis=1
    )
    weights = jnp.where(
        filled_wide, jnp.exp(jnp.where(filled_wide, scores - reference_top[..., None], 0.0)), 0.0
    )
    slot_total = jnp.sum(weights, axis=-1)
    slot_mix = jnp.einsum(
        "stngk,sknd->stngd", weights.astype(jnp.bfloat16), values_split, preferred_element_type=jnp.float32
    )

    group_ids = jnp.concatenate([long_ids, own_ids])
    member = (group_ids[:, None] == slot_request[None, :]) & kept[None, :]
    member_float = member.astype(jnp.float32)
    group_top = jnp.max(jnp.where(member[:, :, None, None, None], reference_top[None], NEGATIVE), axis=1)
    group_total = jnp.einsum("qs,stng->qtng", member_float, slot_total, precision=HIGHEST)
    group_mix = jnp.einsum("qs,stngd->qtngd", member_float, slot_mix, precision=HIGHEST)
    stats = jnp.concatenate(
        [group_mix, group_total[..., None], group_top[..., None]], axis=-1
    )
    long_stats = stats[:LONG_COUNT].reshape(-1, HEAD_SIZE + 2).T
    long_mix, long_small = stats_butterfly(long_stats[:HEAD_SIZE], long_stats[HEAD_SIZE:], n_seq)
    long_stats = jnp.concatenate([long_mix, long_small], axis=0)
    long_stats = long_stats.T.reshape((LONG_COUNT,) + stats.shape[1:])
    own_rank = lax.dynamic_slice_in_dim(rank, first_row, own_rows)
    own_is_long = lax.dynamic_slice_in_dim(is_long, first_row, own_rows)
    rank_hit = own_rank[:, None] == jnp.arange(LONG_COUNT, dtype=jnp.int32)[None, :]
    from_long = jnp.sum(
        jnp.where(rank_hit[:, :, None, None, None, None], long_stats[None], 0.0), axis=1
    )
    cache_stats = jnp.where(own_is_long[:, None, None, None, None], from_long, stats[LONG_COUNT:])
    cache_mix = cache_stats[..., :HEAD_SIZE]
    cache_total = cache_stats[..., HEAD_SIZE]
    cache_top = cache_stats[..., HEAD_SIZE + 1]

    heads = own_query.reshape(own_rows, steps, kv_heads, head_sharing, HEAD_SIZE)
    fresh_keys = keys.reshape(steps, own_rows, kv_heads, HEAD_SIZE).transpose(1, 0, 2, 3)
    fresh_values = values.reshape(steps, own_rows, kv_heads, HEAD_SIZE).transpose(1, 0, 2, 3)
    fresh_scores = (
        jnp.einsum("rtngd,rjnd->rtngj", heads, fresh_keys, preferred_element_type=jnp.float32) * scaling
    )
    allowed = (jnp.arange(steps, dtype=jnp.int32)[None, :] <= jnp.arange(steps, dtype=jnp.int32)[:, None])[
        None, :, None, None, :
    ]
    fresh_top = jnp.max(jnp.where(allowed, fresh_scores, NEGATIVE), axis=-1)
    overall = jnp.maximum(cache_top, fresh_top)
    retained = jnp.exp(cache_top - overall)
    fresh_weights = jnp.where(
        allowed, jnp.exp(jnp.where(allowed, fresh_scores - overall[..., None], 0.0)), 0.0
    )
    denominator = cache_total * retained + jnp.sum(fresh_weights, axis=-1)
    mixture = cache_mix * retained[..., None] + jnp.einsum(
        "rtngj,rjnd->rtngd",
        fresh_weights.astype(jnp.bfloat16),
        fresh_values,
        preferred_element_type=jnp.float32,
    )
    attended = (mixture / denominator[..., None]).astype(jnp.bfloat16)
    attended = attended.transpose(1, 0, 2, 3, 4).reshape(steps * own_rows, q_heads * HEAD_SIZE)
    projected = jnp.dot(attended, w_out, preferred_element_type=jnp.float32)
    summed = reduce_scatter_mp(projected, n_mp).reshape(steps, own_rows, -1)
    hidden = (states.astype(jnp.float32) + summed).astype(jnp.bfloat16)
    return hidden, new_keys, new_values


def solution(mesh):
    n_seq = mesh.shape["seq"]
    n_mp = mesh.shape["mp"]
    placed = (
        P(None, "seq", "mp"),
        P(),
        P(),
        P(),
        P(None, "mp"),
        P(None, "mp"),
        P(None, "mp"),
        P("mp", None),
        P("seq", None, "mp"),
        P("seq", None, "mp"),
        P(),
        P("seq"),
        P("seq"),
        P("seq"),
    )

    def body(*args):
        return shards(*args, n_seq=n_seq, n_mp=n_mp)

    return jax.shard_map(
        body,
        mesh=mesh,
        in_specs=placed,
        out_specs=(P(None, "seq", "mp"), P(None, "seq", "mp"), P(None, "seq", "mp")),
        check_vma=False,
    )
```

```python
import jax
import jax.numpy as jnp
from jax import lax
from jax.experimental import pallas as pl
from jax.experimental.pallas import tpu as pltpu
from jax.sharding import PartitionSpec as P

HEAD_SIZE = 128
LONG_COUNT = 12

ROPE_BASE = 1000000.0
NEGATIVE = -1e30
HIGHEST = lax.Precision.HIGHEST


def scaled_rms(values, gain):
    return values * lax.rsqrt(jnp.mean(values * values, axis=-1, keepdims=True) + 1e-06) * gain


def rotate(values, positions):
    halfway = values.shape[-1] // 2
    frequency = ROPE_BASE ** (-(jnp.arange(halfway, dtype=jnp.float32) * 2.0) / values.shape[-1])
    angles = positions.astype(jnp.float32)[..., None, None] * frequency
    cosine = jnp.cos(angles)
    sine_part = jnp.sin(angles)
    leading = values[..., :halfway]
    trailing = values[..., halfway:]
    return jnp.concatenate(
        [leading * cosine - trailing * sine_part, trailing * cosine + leading * sine_part], axis=-1
    )


def _matmul_kernel(x_ref, *refs):
    count = len(refs) // 2
    x = x_ref[...]
    for w_ref, o_ref in zip(refs[:count], refs[count:]):
        o_ref[...] = jnp.dot(x, w_ref[...], preferred_element_type=jnp.float32)


def _vmem():
    return pl.BlockSpec(memory_space=pltpu.VMEM)


def small_matmul(x, *weights):
    m, k = x.shape
    widths = [w.shape[1] for w in weights]
    return pl.pallas_call(
        _matmul_kernel,
        out_shape=[jax.ShapeDtypeStruct((m, n), jnp.float32) for n in widths],
        in_specs=[_vmem() for _ in range(1 + len(weights))],
        out_specs=[_vmem() for _ in widths],
        cost_estimate=pl.CostEstimate(
            flops=2 * m * k * sum(widths),
            bytes_accessed=2 * (m * k + k * sum(widths)) + 4 * m * sum(widths),
            transcendentals=0,
        ),
    )(x, *weights)


def _chunked_kernel(x_ref, w_ref, o_ref):
    chunks, _, width = o_ref.shape
    x = x_ref[...]
    for c in range(chunks):
        o_ref[c] = jnp.dot(x, w_ref[:, c * width : (c + 1) * width], preferred_element_type=jnp.float32)


def chunked_matmul(x, w, chunks):
    m, k = x.shape
    n = w.shape[1]
    return pl.pallas_call(
        _chunked_kernel,
        out_shape=jax.ShapeDtypeStruct((chunks, m, n // chunks), jnp.float32),
        in_specs=[_vmem(), _vmem()],
        out_specs=_vmem(),
        cost_estimate=pl.CostEstimate(
            flops=2 * m * k * n, bytes_accessed=2 * (m * k + k * n) + 4 * m * n, transcendentals=0
        ),
    )(x, w)


def gather_mp(block, n_mp):
    me = lax.axis_index("mp")
    pieces = [block] + [
        lax.ppermute(block, "mp", [(i, (i + s) % n_mp) for i in range(n_mp)]) for s in range(1, n_mp)
    ]
    ordered = []
    for c in range(n_mp):
        shift = (me - c) % n_mp
        chosen = pieces[0]
        for s in range(1, n_mp):
            chosen = jnp.where(shift == s, pieces[s], chosen)
        ordered.append(chosen)
    return jnp.concatenate(ordered, axis=-1)


def reduce_scatter_mp(chunks, n_mp):
    me = lax.axis_index("mp")
    total = lax.dynamic_index_in_dim(chunks, me, axis=0, keepdims=False)
    for s in range(1, n_mp):
        outgoing = lax.dynamic_index_in_dim(chunks, (me + s) % n_mp, axis=0, keepdims=False)
        total = total + lax.ppermute(outgoing, "mp", [(i, (i + s) % n_mp) for i in range(n_mp)])
    return total


def seq_masks(n_seq):
    if n_seq == 64:
        return [1, 2, 4, 12, 16, 48]
    return [1 << b for b in range(n_seq.bit_length() - 1)]


def butterfly(value, n_seq, combine, extras=None):
    for index, stride in enumerate(seq_masks(n_seq)):
        partner = lax.ppermute(value, "seq", [(i, i ^ stride) for i in range(n_seq)])
        value = combine(value, partner)
        if index == 0 and extras is not None:
            value, extras = lax.optimization_barrier((value, extras))
    return value, extras


def merge_stats(mine, theirs):
    mix_a, stats_a = mine
    mix_b, stats_b = theirs
    top_a = stats_a[1:]
    top_b = stats_b[1:]
    top = jnp.maximum(top_a, top_b)
    scale_a = jnp.exp(top_a - top)
    scale_b = jnp.exp(top_b - top)
    mix = mix_a * scale_a + mix_b.astype(jnp.float32) * scale_b
    total = stats_a[:1] * scale_a + stats_b[:1] * scale_b
    return mix, jnp.concatenate([total, top], axis=0)


def split_exact(x):
    hi = lax.reduce_precision(x, exponent_bits=8, mantissa_bits=7)
    rest = x - hi
    mid = lax.reduce_precision(rest, exponent_bits=8, mantissa_bits=7)
    lo = rest - mid
    return jnp.concatenate([hi, mid, lo], axis=0).astype(jnp.bfloat16)


def join_exact(parts):
    parts = parts.astype(jnp.float32)
    return parts[0:1] + parts[1:2] + parts[2:3]


def stats_butterfly(mix, stats, n_seq):
    width = mix.shape[0]
    for stride in seq_masks(n_seq):
        pairs = [(i, i ^ stride) for i in range(n_seq)]
        packed = jnp.concatenate(
            [mix.astype(jnp.bfloat16), split_exact(stats[:1]), split_exact(stats[1:])], axis=0
        )
        arrived = lax.ppermute(packed, "seq", pairs)
        theirs = (
            arrived[:width],
            jnp.concatenate(
                [join_exact(arrived[width : width + 3]), join_exact(arrived[width + 3 : width + 6])], axis=0
            ),
        )
        mix, stats = merge_stats((mix, stats), theirs)
    return mix, stats


def shards(
    states,
    norm_gain,
    query_gain,
    key_gain,
    w_query,
    key_matrix,
    value_matrix,
    w_out,
    cached_key_blocks,
    cached_value_blocks,
    req_len,
    slot_request,
    slot_block,
    slot_empty,
    n_seq,
    n_mp,
):
    steps, own_rows, _ = states.shape
    me = lax.axis_index("seq")
    first_row = me * own_rows
    kv_heads = key_matrix.shape[1] // HEAD_SIZE
    q_heads = w_query.shape[1] // HEAD_SIZE
    head_sharing = q_heads // kv_heads
    slot_count, block_len, _ = cached_key_blocks.shape
    requests = req_len.shape[0]
    long_len = n_seq * block_len
    scaling = HEAD_SIZE ** (-0.5)

    wide = gather_mp(states, n_mp).reshape(steps * own_rows, -1)
    own_ids = first_row + jnp.arange(own_rows, dtype=jnp.int32)
    own_len = lax.dynamic_slice_in_dim(req_len, first_row, own_rows)
    positions = (own_len[None, :] + jnp.arange(steps, dtype=jnp.int32)[:, None]).reshape(-1)
    normed = scaled_rms(wide.astype(jnp.float32), norm_gain).astype(jnp.bfloat16)
    rows = steps * own_rows
    query, keys, values = small_matmul(normed, w_query, key_matrix, value_matrix)
    query = query.reshape(rows, q_heads, HEAD_SIZE)
    keys = keys.reshape(rows, kv_heads, HEAD_SIZE)
    values = values.astype(jnp.bfloat16)
    query = rotate(scaled_rms(query, query_gain), positions).astype(jnp.bfloat16)
    keys = rotate(scaled_rms(keys, key_gain), positions).astype(jnp.bfloat16)
    new_keys = keys.reshape(steps, own_rows, kv_heads * HEAD_SIZE)
    new_values = values.reshape(steps, own_rows, kv_heads * HEAD_SIZE)
    own_query = query.reshape(steps, own_rows, q_heads, HEAD_SIZE).transpose(1, 0, 2, 3)

    request_ids = jnp.arange(requests, dtype=jnp.int32)
    is_long = req_len == long_len
    long_count = is_long.astype(jnp.int32)
    rank = jnp.sum(
        jnp.where(request_ids[None, :] < request_ids[:, None], long_count[None, :], 0), axis=1
    )
    long_ids = jnp.sum(
        jnp.where(
            is_long[None, :] & (rank[None, :] == jnp.arange(LONG_COUNT, dtype=jnp.int32)[:, None]),
            request_ids[None, :],
            0,
        ),
        axis=1,
    )
    own_pick = long_ids[:, None] == own_ids[None, :]
    long_table = jnp.sum(
        jnp.where(own_pick[:, :, None, None, None], own_query[None], jnp.zeros((), jnp.bfloat16)), axis=1
    ).astype(jnp.bfloat16)
    long_table, (slot_request, slot_block, slot_empty, slot_lengths) = butterfly(
        long_table, n_seq, lambda a, b: a + b, (slot_request, slot_block, slot_empty, req_len)
    )

    hit = slot_request[:, None] == request_ids[None, :]
    slot_req_long = jnp.any(hit & is_long[None, :], axis=1)
    slot_rank = jnp.sum(jnp.where(hit, rank[None, :], 0), axis=1)
    slot_len = jnp.sum(jnp.where(hit, slot_lengths[None, :], 0), axis=1)
    local_row = slot_request - first_row
    slot_local = (local_row >= 0) & (local_row < own_rows)
    pick = jnp.where(
        slot_req_long, slot_rank, jnp.where(slot_local, LONG_COUNT + local_row, LONG_COUNT + own_rows)
    )
    candidates = jnp.concatenate(
        [long_table, own_query, jnp.zeros((1,) + own_query.shape[1:], jnp.bfloat16)], axis=0
    )
    slot_query = jnp.take(candidates, pick, axis=0).reshape(
        slot_count, steps, kv_heads, head_sharing, HEAD_SIZE
    )
    keys_split = cached_key_blocks.reshape(slot_count, block_len, kv_heads, HEAD_SIZE)
    values_split = cached_value_blocks.reshape(slot_count, block_len, kv_heads, HEAD_SIZE)
    scores = (
        jnp.einsum("stngd,sknd->stngk", slot_query, keys_split, preferred_element_type=jnp.float32)
        * scaling
    )
    kept = slot_empty == 0
    filled = kept[:, None] & (
        slot_block[:, None] * block_len + jnp.arange(block_len, dtype=jnp.int32)[None, :] < slot_len[:, None]
    )
    filled_wide = filled[:, None, None, None, :]
    slot_top = jnp.max(jnp.where(filled_wide, scores, NEGATIVE), axis=-1)
    same = (slot_request[:, None] == slot_request[None, :]) & kept[None, :]
    reference_top = jnp.max(
        jnp.where(same[:, :, None, None, None], slot_top[None], NEGATIVE), axis=1
    )
    weights = jnp.where(
        filled_wide, jnp.exp(jnp.where(filled_wide, scores - reference_top[..., None], 0.0)), 0.0
    )
    slot_total = jnp.sum(weights, axis=-1)
    slot_mix = jnp.einsum(
        "stngk,sknd->stngd", weights.astype(jnp.bfloat16), values_split, preferred_element_type=jnp.float32
    )

    group_ids = jnp.concatenate([long_ids, own_ids])
    member = (group_ids[:, None] == slot_request[None, :]) & kept[None, :]
    member_float = member.astype(jnp.float32)
    group_top = jnp.max(jnp.where(member[:, :, None, None, None], reference_top[None], NEGATIVE), axis=1)
    group_total = jnp.einsum("qs,stng->qtng", member_float, slot_total, precision=HIGHEST)
    group_mix = jnp.einsum("qs,stngd->qtngd", member_float, slot_mix, precision=HIGHEST)
    stats = jnp.concatenate(
        [group_mix, group_total[..., None], group_top[..., None]], axis=-1
    )
    long_stats = stats[:LONG_COUNT].reshape(-1, HEAD_SIZE + 2).T
    long_mix, long_small = stats_butterfly(long_stats[:HEAD_SIZE], long_stats[HEAD_SIZE:], n_seq)
    long_stats = jnp.concatenate([long_mix, long_small], axis=0)
    long_stats = long_stats.T.reshape((LONG_COUNT,) + stats.shape[1:])
    own_rank = lax.dynamic_slice_in_dim(rank, first_row, own_rows)
    own_is_long = lax.dynamic_slice_in_dim(is_long, first_row, own_rows)
    rank_hit = own_rank[:, None] == jnp.arange(LONG_COUNT, dtype=jnp.int32)[None, :]
    from_long = jnp.sum(
        jnp.where(rank_hit[:, :, None, None, None, None], long_stats[None], 0.0), axis=1
    )
    cache_stats = jnp.where(own_is_long[:, None, None, None, None], from_long, stats[LONG_COUNT:])
    cache_mix = cache_stats[..., :HEAD_SIZE]
    cache_total = cache_stats[..., HEAD_SIZE]
    cache_top = cache_stats[..., HEAD_SIZE + 1]

    heads = own_query.reshape(own_rows, steps, kv_heads, head_sharing, HEAD_SIZE)
    fresh_keys = keys.reshape(steps, own_rows, kv_heads, HEAD_SIZE).transpose(1, 0, 2, 3)
    fresh_values = values.reshape(steps, own_rows, kv_heads, HEAD_SIZE).transpose(1, 0, 2, 3)
    fresh_scores = (
        jnp.einsum("rtngd,rjnd->rtngj", heads, fresh_keys, preferred_element_type=jnp.float32) * scaling
    )
    allowed = (jnp.arange(steps, dtype=jnp.int32)[None, :] <= jnp.arange(steps, dtype=jnp.int32)[:, None])[
        None, :, None, None, :
    ]
    fresh_top = jnp.max(jnp.where(allowed, fresh_scores, NEGATIVE), axis=-1)
    fresh_weights = jnp.where(
        allowed, jnp.exp(jnp.where(allowed, fresh_scores - fresh_top[..., None], 0.0)), 0.0
    )
    fresh_total = jnp.sum(fresh_weights, axis=-1)
    fresh_mix = jnp.einsum(
        "rtngj,rjnd->rtngd",
        fresh_weights.astype(jnp.bfloat16),
        fresh_values,
        preferred_element_type=jnp.float32,
    )
    overall = jnp.maximum(cache_top, fresh_top)
    retained = jnp.exp(cache_top - overall)
    fresh_scale = jnp.exp(fresh_top - overall)
    denominator = cache_total * retained + fresh_total * fresh_scale
    mixture = cache_mix * retained[..., None] + fresh_mix * fresh_scale[..., None]
    attended = (mixture / denominator[..., None]).astype(jnp.bfloat16)
    attended = attended.transpose(1, 0, 2, 3, 4).reshape(steps * own_rows, q_heads * HEAD_SIZE)
    projected = chunked_matmul(attended, w_out, n_mp)
    summed = reduce_scatter_mp(projected, n_mp).reshape(steps, own_rows, -1)
    hidden = (states.astype(jnp.float32) + summed).astype(jnp.bfloat16)
    return hidden, new_keys, new_values


def solution(mesh):
    n_seq = mesh.shape["seq"]
    n_mp = mesh.shape["mp"]
    placed = (
        P(None, "seq", "mp"),
        P(),
        P(),
        P(),
        P(None, "mp"),
        P(None, "mp"),
        P(None, "mp"),
        P("mp", None),
        P("seq", None, "mp"),
        P("seq", None, "mp"),
        P(),
        P("seq"),
        P("seq"),
        P("seq"),
    )

    def body(*args):
        return shards(*args, n_seq=n_seq, n_mp=n_mp)

    return jax.shard_map(
        body,
        mesh=mesh,
        in_specs=placed,
        out_specs=(P(None, "seq", "mp"), P(None, "seq", "mp"), P(None, "seq", "mp")),
        check_vma=False,
    )
```

```python
import jax
import jax.numpy as jnp
from jax import lax
from jax.experimental import pallas as pl
from jax.experimental.pallas import tpu as pltpu
from jax.sharding import PartitionSpec as P

HEAD_SIZE = 128
LONG_COUNT = 12

ROPE_BASE = 1000000.0
NEGATIVE = -1e30
HIGHEST = lax.Precision.HIGHEST


def scaled_rms(values, gain):
    return values * lax.rsqrt(jnp.mean(values * values, axis=-1, keepdims=True) + 1e-06) * gain


def rotate(values, positions):
    halfway = values.shape[-1] // 2
    frequency = ROPE_BASE ** (-(jnp.arange(halfway, dtype=jnp.float32) * 2.0) / values.shape[-1])
    angles = positions.astype(jnp.float32)[..., None, None] * frequency
    cosine = jnp.cos(angles)
    sine_part = jnp.sin(angles)
    leading = values[..., :halfway]
    trailing = values[..., halfway:]
    return jnp.concatenate(
        [leading * cosine - trailing * sine_part, trailing * cosine + leading * sine_part], axis=-1
    )


def _matmul_kernel(x_ref, *refs):
    count = len(refs) // 2
    x = x_ref[...]
    for w_ref, o_ref in zip(refs[:count], refs[count:]):
        o_ref[...] = jnp.dot(x, w_ref[...], preferred_element_type=jnp.float32)


def _norm_matmul_kernel(x_ref, g_ref, *refs):
    count = len(refs) // 2
    x = x_ref[...].astype(jnp.float32)
    scale = lax.rsqrt(jnp.mean(x * x, axis=-1, keepdims=True) + 1e-06)
    normed = (x * scale * g_ref[...]).astype(jnp.bfloat16)
    for w_ref, o_ref in zip(refs[:count], refs[count:]):
        o_ref[...] = jnp.dot(normed, w_ref[...], preferred_element_type=jnp.float32)


def norm_matmul(x, gain, *weights):
    m, k = x.shape
    widths = [w.shape[1] for w in weights]
    return pl.pallas_call(
        _norm_matmul_kernel,
        out_shape=[jax.ShapeDtypeStruct((m, n), jnp.float32) for n in widths],
        cost_estimate=pl.CostEstimate(
            flops=2 * m * k * sum(widths),
            bytes_accessed=2 * (m * k + k * sum(widths)) + 4 * m * sum(widths),
            transcendentals=m,
        ),
    )(x, gain.reshape(1, k), *weights)


def _vmem():
    return pl.BlockSpec(memory_space=pltpu.VMEM)


def small_matmul(x, *weights):
    m, k = x.shape
    widths = [w.shape[1] for w in weights]
    return pl.pallas_call(
        _matmul_kernel,
        out_shape=[jax.ShapeDtypeStruct((m, n), jnp.float32) for n in widths],
        in_specs=[_vmem() for _ in range(1 + len(weights))],
        out_specs=[_vmem() for _ in widths],
        cost_estimate=pl.CostEstimate(
            flops=2 * m * k * sum(widths),
            bytes_accessed=2 * (m * k + k * sum(widths)) + 4 * m * sum(widths),
            transcendentals=0,
        ),
    )(x, *weights)


def _chunked_kernel(x_ref, w_ref, o_ref):
    chunks, _, width = o_ref.shape
    x = x_ref[...]
    for c in range(chunks):
        o_ref[c] = jnp.dot(x, w_ref[:, c * width : (c + 1) * width], preferred_element_type=jnp.float32)


def chunked_matmul(x, w, chunks):
    m, k = x.shape
    n = w.shape[1]
    return pl.pallas_call(
        _chunked_kernel,
        out_shape=jax.ShapeDtypeStruct((chunks, m, n // chunks), jnp.float32),
        in_specs=[_vmem(), _vmem()],
        out_specs=_vmem(),
        cost_estimate=pl.CostEstimate(
            flops=2 * m * k * n, bytes_accessed=2 * (m * k + k * n) + 4 * m * n, transcendentals=0
        ),
    )(x, w)


def gather_mp(block, n_mp):
    me = lax.axis_index("mp")
    pieces = [block] + [
        lax.ppermute(block, "mp", [(i, (i + s) % n_mp) for i in range(n_mp)]) for s in range(1, n_mp)
    ]
    ordered = []
    for c in range(n_mp):
        shift = (me - c) % n_mp
        chosen = pieces[0]
        for s in range(1, n_mp):
            chosen = jnp.where(shift == s, pieces[s], chosen)
        ordered.append(chosen)
    return jnp.concatenate(ordered, axis=-1)


def reduce_scatter_mp(chunks, n_mp):
    me = lax.axis_index("mp")
    total = lax.dynamic_index_in_dim(chunks, me, axis=0, keepdims=False)
    for s in range(1, n_mp):
        outgoing = lax.dynamic_index_in_dim(chunks, (me + s) % n_mp, axis=0, keepdims=False)
        total = total + lax.ppermute(outgoing, "mp", [(i, (i + s) % n_mp) for i in range(n_mp)])
    return total


def seq_masks(n_seq):
    if n_seq == 64:
        return [1, 2, 4, 12, 16, 48]
    return [1 << b for b in range(n_seq.bit_length() - 1)]


def butterfly(value, n_seq, combine, extras=None):
    for index, stride in enumerate(seq_masks(n_seq)):
        partner = lax.ppermute(value, "seq", [(i, i ^ stride) for i in range(n_seq)])
        value = combine(value, partner)
        if index == 0 and extras is not None:
            value, extras = lax.optimization_barrier((value, extras))
    return value, extras


def merge_stats(mine, theirs):
    mix_a, stats_a = mine
    mix_b, stats_b = theirs
    top_a = stats_a[1:]
    top_b = stats_b[1:]
    top = jnp.maximum(top_a, top_b)
    scale_a = jnp.exp(top_a - top)
    scale_b = jnp.exp(top_b - top)
    mix = mix_a * scale_a + mix_b.astype(jnp.float32) * scale_b
    total = stats_a[:1] * scale_a + stats_b[:1] * scale_b
    return mix, jnp.concatenate([total, top], axis=0)


def split_exact(x):
    hi = lax.reduce_precision(x, exponent_bits=8, mantissa_bits=7)
    rest = x - hi
    mid = lax.reduce_precision(rest, exponent_bits=8, mantissa_bits=7)
    lo = rest - mid
    return jnp.concatenate([hi, mid, lo], axis=0).astype(jnp.bfloat16)


def join_exact(parts):
    parts = parts.astype(jnp.float32)
    return parts[0:1] + parts[1:2] + parts[2:3]


def stats_butterfly(mix, stats, n_seq):
    width = mix.shape[0]
    for stride in seq_masks(n_seq):
        pairs = [(i, i ^ stride) for i in range(n_seq)]
        packed = jnp.concatenate(
            [mix.astype(jnp.bfloat16), split_exact(stats[:1]), split_exact(stats[1:])], axis=0
        )
        arrived = lax.ppermute(packed, "seq", pairs)
        theirs = (
            arrived[:width],
            jnp.concatenate(
                [join_exact(arrived[width : width + 3]), join_exact(arrived[width + 3 : width + 6])], axis=0
            ),
        )
        mix, stats = merge_stats((mix, stats), theirs)
    return mix, stats


def shards(
    states,
    norm_gain,
    query_gain,
    key_gain,
    w_query,
    key_matrix,
    value_matrix,
    w_out,
    cached_key_blocks,
    cached_value_blocks,
    req_len,
    slot_request,
    slot_block,
    slot_empty,
    n_seq,
    n_mp,
):
    steps, own_rows, _ = states.shape
    me = lax.axis_index("seq")
    first_row = me * own_rows
    kv_heads = key_matrix.shape[1] // HEAD_SIZE
    q_heads = w_query.shape[1] // HEAD_SIZE
    head_sharing = q_heads // kv_heads
    slot_count, block_len, _ = cached_key_blocks.shape
    requests = req_len.shape[0]
    long_len = n_seq * block_len
    scaling = HEAD_SIZE ** (-0.5)

    wide = gather_mp(states, n_mp).reshape(steps * own_rows, -1)
    own_ids = first_row + jnp.arange(own_rows, dtype=jnp.int32)
    own_len = lax.dynamic_slice_in_dim(req_len, first_row, own_rows)
    positions = (own_len[None, :] + jnp.arange(steps, dtype=jnp.int32)[:, None]).reshape(-1)
    rows = steps * own_rows
    query, keys, values = norm_matmul(wide, norm_gain, w_query, key_matrix, value_matrix)
    query = query.reshape(rows, q_heads, HEAD_SIZE)
    keys = keys.reshape(rows, kv_heads, HEAD_SIZE)
    values = values.astype(jnp.bfloat16)
    query = rotate(scaled_rms(query, query_gain), positions).astype(jnp.bfloat16)
    keys = rotate(scaled_rms(keys, key_gain), positions).astype(jnp.bfloat16)
    new_keys = keys.reshape(steps, own_rows, kv_heads * HEAD_SIZE)
    new_values = values.reshape(steps, own_rows, kv_heads * HEAD_SIZE)
    own_query = query.reshape(steps, own_rows, q_heads, HEAD_SIZE).transpose(1, 0, 2, 3)

    request_ids = jnp.arange(requests, dtype=jnp.int32)
    is_long = req_len == long_len
    long_count = is_long.astype(jnp.int32)
    rank = jnp.sum(
        jnp.where(request_ids[None, :] < request_ids[:, None], long_count[None, :], 0), axis=1
    )
    long_ids = jnp.sum(
        jnp.where(
            is_long[None, :] & (rank[None, :] == jnp.arange(LONG_COUNT, dtype=jnp.int32)[:, None]),
            request_ids[None, :],
            0,
        ),
        axis=1,
    )
    own_pick = long_ids[:, None] == own_ids[None, :]
    long_table = jnp.sum(
        jnp.where(own_pick[:, :, None, None, None], own_query[None], jnp.zeros((), jnp.bfloat16)), axis=1
    ).astype(jnp.bfloat16)
    long_table, (slot_request, slot_block, slot_empty, slot_lengths) = butterfly(
        long_table, n_seq, lambda a, b: a + b, (slot_request, slot_block, slot_empty, req_len)
    )

    hit = slot_request[:, None] == request_ids[None, :]
    slot_req_long = jnp.any(hit & is_long[None, :], axis=1)
    slot_rank = jnp.sum(jnp.where(hit, rank[None, :], 0), axis=1)
    slot_len = jnp.sum(jnp.where(hit, slot_lengths[None, :], 0), axis=1)
    local_row = slot_request - first_row
    slot_local = (local_row >= 0) & (local_row < own_rows)
    pick = jnp.where(
        slot_req_long, slot_rank, jnp.where(slot_local, LONG_COUNT + local_row, LONG_COUNT + own_rows)
    )
    candidates = jnp.concatenate(
        [long_table, own_query, jnp.zeros((1,) + own_query.shape[1:], jnp.bfloat16)], axis=0
    )
    slot_query = jnp.take(candidates, pick, axis=0).reshape(
        slot_count, steps, kv_heads, head_sharing, HEAD_SIZE
    )
    keys_split = cached_key_blocks.reshape(slot_count, block_len, kv_heads, HEAD_SIZE)
    values_split = cached_value_blocks.reshape(slot_count, block_len, kv_heads, HEAD_SIZE)
    scores = (
        jnp.einsum("stngd,sknd->stngk", slot_query, keys_split, preferred_element_type=jnp.float32)
        * scaling
    )
    kept = slot_empty == 0
    filled = kept[:, None] & (
        slot_block[:, None] * block_len + jnp.arange(block_len, dtype=jnp.int32)[None, :] < slot_len[:, None]
    )
    filled_wide = filled[:, None, None, None, :]
    slot_top = jnp.max(jnp.where(filled_wide, scores, NEGATIVE), axis=-1)
    same = (slot_request[:, None] == slot_request[None, :]) & kept[None, :]
    reference_top = jnp.max(
        jnp.where(same[:, :, None, None, None], slot_top[None], NEGATIVE), axis=1
    )
    weights = jnp.where(
        filled_wide, jnp.exp(jnp.where(filled_wide, scores - reference_top[..., None], 0.0)), 0.0
    )
    slot_total = jnp.sum(weights, axis=-1)
    slot_mix = jnp.einsum(
        "stngk,sknd->stngd", weights.astype(jnp.bfloat16), values_split, preferred_element_type=jnp.float32
    )

    group_ids = jnp.concatenate([long_ids, own_ids])
    member = (group_ids[:, None] == slot_request[None, :]) & kept[None, :]
    member_float = member.astype(jnp.float32)
    group_top = jnp.max(jnp.where(member[:, :, None, None, None], reference_top[None], NEGATIVE), axis=1)
    group_total = jnp.einsum("qs,stng->qtng", member_float, slot_total, precision=HIGHEST)
    group_mix = jnp.einsum("qs,stngd->qtngd", member_float, slot_mix, precision=HIGHEST)
    stats = jnp.concatenate(
        [group_mix, group_total[..., None], group_top[..., None]], axis=-1
    )
    long_stats = stats[:LONG_COUNT].reshape(-1, HEAD_SIZE + 2).T
    long_mix, long_small = stats_butterfly(long_stats[:HEAD_SIZE], long_stats[HEAD_SIZE:], n_seq)
    long_stats = jnp.concatenate([long_mix, long_small], axis=0)
    long_stats = long_stats.T.reshape((LONG_COUNT,) + stats.shape[1:])
    own_rank = lax.dynamic_slice_in_dim(rank, first_row, own_rows)
    own_is_long = lax.dynamic_slice_in_dim(is_long, first_row, own_rows)
    rank_hit = own_rank[:, None] == jnp.arange(LONG_COUNT, dtype=jnp.int32)[None, :]
    from_long = jnp.sum(
        jnp.where(rank_hit[:, :, None, None, None, None], long_stats[None], 0.0), axis=1
    )
    cache_stats = jnp.where(own_is_long[:, None, None, None, None], from_long, stats[LONG_COUNT:])
    cache_mix = cache_stats[..., :HEAD_SIZE]
    cache_total = cache_stats[..., HEAD_SIZE]
    cache_top = cache_stats[..., HEAD_SIZE + 1]

    heads = own_query.reshape(own_rows, steps, kv_heads, head_sharing, HEAD_SIZE)
    fresh_keys = keys.reshape(steps, own_rows, kv_heads, HEAD_SIZE).transpose(1, 0, 2, 3)
    fresh_values = values.reshape(steps, own_rows, kv_heads, HEAD_SIZE).transpose(1, 0, 2, 3)
    fresh_scores = (
        jnp.einsum("rtngd,rjnd->rtngj", heads, fresh_keys, preferred_element_type=jnp.float32) * scaling
    )
    allowed = (jnp.arange(steps, dtype=jnp.int32)[None, :] <= jnp.arange(steps, dtype=jnp.int32)[:, None])[
        None, :, None, None, :
    ]
    fresh_top = jnp.max(jnp.where(allowed, fresh_scores, NEGATIVE), axis=-1)
    fresh_weights = jnp.where(
        allowed, jnp.exp(jnp.where(allowed, fresh_scores - fresh_top[..., None], 0.0)), 0.0
    )
    fresh_total = jnp.sum(fresh_weights, axis=-1)
    fresh_mix = jnp.einsum(
        "rtngj,rjnd->rtngd",
        fresh_weights.astype(jnp.bfloat16),
        fresh_values,
        preferred_element_type=jnp.float32,
    )
    overall = jnp.maximum(cache_top, fresh_top)
    retained = jnp.exp(cache_top - overall)
    fresh_scale = jnp.exp(fresh_top - overall)
    denominator = cache_total * retained + fresh_total * fresh_scale
    mixture = cache_mix * retained[..., None] + fresh_mix * fresh_scale[..., None]
    attended = (mixture / denominator[..., None]).astype(jnp.bfloat16)
    attended = attended.transpose(1, 0, 2, 3, 4).reshape(steps * own_rows, q_heads * HEAD_SIZE)
    projected = chunked_matmul(attended, w_out, n_mp)
    summed = reduce_scatter_mp(projected, n_mp).reshape(steps, own_rows, -1)
    hidden = (states.astype(jnp.float32) + summed).astype(jnp.bfloat16)
    return hidden, new_keys, new_values


def solution(mesh):
    n_seq = mesh.shape["seq"]
    n_mp = mesh.shape["mp"]
    placed = (
        P(None, "seq", "mp"),
        P(),
        P(),
        P(),
        P(None, "mp"),
        P(None, "mp"),
        P(None, "mp"),
        P("mp", None),
        P("seq", None, "mp"),
        P("seq", None, "mp"),
        P(),
        P("seq"),
        P("seq"),
        P("seq"),
    )

    def body(*args):
        return shards(*args, n_seq=n_seq, n_mp=n_mp)

    return jax.shard_map(
        body,
        mesh=mesh,
        in_specs=placed,
        out_specs=(P(None, "seq", "mp"), P(None, "seq", "mp"), P(None, "seq", "mp")),
        check_vma=False,
    )
```

```python
import jax
import jax.numpy as jnp
from jax import lax
from jax.experimental import pallas as pl
from jax.experimental.pallas import tpu as pltpu
from jax.sharding import PartitionSpec as P

HEAD_SIZE = 128
LONG_COUNT = 12

ROPE_BASE = 1000000.0
NEGATIVE = -1e30
HIGHEST = lax.Precision.HIGHEST


def scaled_rms(values, gain):
    return values * lax.rsqrt(jnp.mean(values * values, axis=-1, keepdims=True) + 1e-06) * gain


def rotate(values, positions):
    halfway = values.shape[-1] // 2
    frequency = ROPE_BASE ** (-(jnp.arange(halfway, dtype=jnp.float32) * 2.0) / values.shape[-1])
    angles = positions.astype(jnp.float32)[..., None, None] * frequency
    cosine = jnp.cos(angles)
    sine_part = jnp.sin(angles)
    leading = values[..., :halfway]
    trailing = values[..., halfway:]
    return jnp.concatenate(
        [leading * cosine - trailing * sine_part, trailing * cosine + leading * sine_part], axis=-1
    )


def _matmul_kernel(x_ref, *refs):
    count = len(refs) // 2
    x = x_ref[...]
    for w_ref, o_ref in zip(refs[:count], refs[count:]):
        o_ref[...] = jnp.dot(x, w_ref[...], preferred_element_type=jnp.float32)


def _project_kernel(x_ref, g_ref, qg_ref, kg_ref, cos_ref, sin_ref, wq_ref, wk_ref, wv_ref, q_ref, k_ref, v_ref):
    x = x_ref[...].astype(jnp.float32)
    scale = lax.rsqrt(jnp.mean(x * x, axis=-1, keepdims=True) + 1e-06)
    normed = (x * scale * g_ref[...]).astype(jnp.bfloat16)
    cosine = cos_ref[...]
    sine = sin_ref[...]

    def norm_rotate(y, gain):
        y = y * lax.rsqrt(jnp.mean(y * y, axis=-1, keepdims=True) + 1e-06) * gain
        return y * cosine + pltpu.roll(y, HEAD_SIZE // 2, 1) * sine

    for w_ref, o_ref, gain_ref in ((wq_ref, q_ref, qg_ref), (wk_ref, k_ref, kg_ref)):
        product = jnp.dot(normed, w_ref[...], preferred_element_type=jnp.float32)
        gain = gain_ref[...]
        for h in range(product.shape[1] // HEAD_SIZE):
            o_ref[:, h * HEAD_SIZE : (h + 1) * HEAD_SIZE] = norm_rotate(
                product[:, h * HEAD_SIZE : (h + 1) * HEAD_SIZE], gain
            )
    v_ref[...] = jnp.dot(normed, wv_ref[...], preferred_element_type=jnp.float32)


def project_rows(x, gain, query_gain, key_gain, positions, w_query, key_matrix, value_matrix):
    m, k = x.shape
    halfway = HEAD_SIZE // 2
    frequency = ROPE_BASE ** (-(jnp.arange(halfway, dtype=jnp.float32) * 2.0) / HEAD_SIZE)
    angles = positions.astype(jnp.float32)[:, None] * frequency
    cosine = jnp.cos(angles)
    sine = jnp.sin(angles)
    cos_both = jnp.concatenate([cosine, cosine], axis=-1)
    sin_signed = jnp.concatenate([-sine, sine], axis=-1)
    weights = (w_query, key_matrix, value_matrix)
    widths = [w.shape[1] for w in weights]
    return pl.pallas_call(
        _project_kernel,
        out_shape=[jax.ShapeDtypeStruct((m, n), jnp.float32) for n in widths],
        cost_estimate=pl.CostEstimate(
            flops=2 * m * k * sum(widths),
            bytes_accessed=2 * (m * k + k * sum(widths)) + 4 * m * sum(widths),
            transcendentals=m,
        ),
    )(
        x,
        gain.reshape(1, k),
        query_gain.reshape(1, HEAD_SIZE),
        key_gain.reshape(1, HEAD_SIZE),
        cos_both,
        sin_signed,
        *weights,
    )


def _vmem():
    return pl.BlockSpec(memory_space=pltpu.VMEM)


def small_matmul(x, *weights):
    m, k = x.shape
    widths = [w.shape[1] for w in weights]
    return pl.pallas_call(
        _matmul_kernel,
        out_shape=[jax.ShapeDtypeStruct((m, n), jnp.float32) for n in widths],
        in_specs=[_vmem() for _ in range(1 + len(weights))],
        out_specs=[_vmem() for _ in widths],
        cost_estimate=pl.CostEstimate(
            flops=2 * m * k * sum(widths),
            bytes_accessed=2 * (m * k + k * sum(widths)) + 4 * m * sum(widths),
            transcendentals=0,
        ),
    )(x, *weights)


def _chunked_kernel(x_ref, w_ref, o_ref):
    chunks, _, width = o_ref.shape
    x = x_ref[...]
    for c in range(chunks):
        o_ref[c] = jnp.dot(x, w_ref[:, c * width : (c + 1) * width], preferred_element_type=jnp.float32)


def chunked_matmul(x, w, chunks):
    m, k = x.shape
    n = w.shape[1]
    return pl.pallas_call(
        _chunked_kernel,
        out_shape=jax.ShapeDtypeStruct((chunks, m, n // chunks), jnp.float32),
        in_specs=[_vmem(), _vmem()],
        out_specs=_vmem(),
        cost_estimate=pl.CostEstimate(
            flops=2 * m * k * n, bytes_accessed=2 * (m * k + k * n) + 4 * m * n, transcendentals=0
        ),
    )(x, w)


def gather_mp(block, n_mp):
    me = lax.axis_index("mp")
    pieces = [block] + [
        lax.ppermute(block, "mp", [(i, (i + s) % n_mp) for i in range(n_mp)]) for s in range(1, n_mp)
    ]
    ordered = []
    for c in range(n_mp):
        shift = (me - c) % n_mp
        chosen = pieces[0]
        for s in range(1, n_mp):
            chosen = jnp.where(shift == s, pieces[s], chosen)
        ordered.append(chosen)
    return jnp.concatenate(ordered, axis=-1)


def reduce_scatter_mp(chunks, n_mp):
    me = lax.axis_index("mp")
    total = lax.dynamic_index_in_dim(chunks, me, axis=0, keepdims=False)
    for s in range(1, n_mp):
        outgoing = lax.dynamic_index_in_dim(chunks, (me + s) % n_mp, axis=0, keepdims=False)
        total = total + lax.ppermute(outgoing, "mp", [(i, (i + s) % n_mp) for i in range(n_mp)])
    return total


def seq_masks(n_seq):
    if n_seq == 64:
        return [1, 2, 4, 12, 16, 48]
    return [1 << b for b in range(n_seq.bit_length() - 1)]


def butterfly(value, n_seq, combine, extras=None):
    for index, stride in enumerate(seq_masks(n_seq)):
        partner = lax.ppermute(value, "seq", [(i, i ^ stride) for i in range(n_seq)])
        value = combine(value, partner)
        if index == 0 and extras is not None:
            value, extras = lax.optimization_barrier((value, extras))
    return value, extras


def merge_stats(mine, theirs):
    mix_a, stats_a = mine
    mix_b, stats_b = theirs
    top_a = stats_a[1:]
    top_b = stats_b[1:]
    top = jnp.maximum(top_a, top_b)
    scale_a = jnp.exp(top_a - top)
    scale_b = jnp.exp(top_b - top)
    mix = mix_a * scale_a + mix_b.astype(jnp.float32) * scale_b
    total = stats_a[:1] * scale_a + stats_b[:1] * scale_b
    return mix, jnp.concatenate([total, top], axis=0)


def split_exact(x):
    hi = lax.reduce_precision(x, exponent_bits=8, mantissa_bits=7)
    rest = x - hi
    mid = lax.reduce_precision(rest, exponent_bits=8, mantissa_bits=7)
    lo = rest - mid
    return jnp.concatenate([hi, mid, lo], axis=0).astype(jnp.bfloat16)


def join_exact(parts):
    parts = parts.astype(jnp.float32)
    return parts[0:1] + parts[1:2] + parts[2:3]


def stats_butterfly(mix, stats, n_seq):
    width = mix.shape[0]
    for stride in seq_masks(n_seq):
        pairs = [(i, i ^ stride) for i in range(n_seq)]
        packed = jnp.concatenate(
            [mix.astype(jnp.bfloat16), split_exact(stats[:1]), split_exact(stats[1:])], axis=0
        )
        arrived = lax.ppermute(packed, "seq", pairs)
        theirs = (
            arrived[:width],
            jnp.concatenate(
                [join_exact(arrived[width : width + 3]), join_exact(arrived[width + 3 : width + 6])], axis=0
            ),
        )
        mix, stats = merge_stats((mix, stats), theirs)
    return mix, stats


def shards(
    states,
    norm_gain,
    query_gain,
    key_gain,
    w_query,
    key_matrix,
    value_matrix,
    w_out,
    cached_key_blocks,
    cached_value_blocks,
    req_len,
    slot_request,
    slot_block,
    slot_empty,
    n_seq,
    n_mp,
):
    steps, own_rows, _ = states.shape
    me = lax.axis_index("seq")
    first_row = me * own_rows
    kv_heads = key_matrix.shape[1] // HEAD_SIZE
    q_heads = w_query.shape[1] // HEAD_SIZE
    head_sharing = q_heads // kv_heads
    slot_count, block_len, _ = cached_key_blocks.shape
    requests = req_len.shape[0]
    long_len = n_seq * block_len
    scaling = HEAD_SIZE ** (-0.5)

    wide = gather_mp(states, n_mp).reshape(steps * own_rows, -1)
    own_ids = first_row + jnp.arange(own_rows, dtype=jnp.int32)
    own_len = lax.dynamic_slice_in_dim(req_len, first_row, own_rows)
    positions = (own_len[None, :] + jnp.arange(steps, dtype=jnp.int32)[:, None]).reshape(-1)
    rows = steps * own_rows
    query, keys, values = project_rows(
        wide, norm_gain, query_gain, key_gain, positions, w_query, key_matrix, value_matrix
    )
    query = query.reshape(rows, q_heads, HEAD_SIZE).astype(jnp.bfloat16)
    keys = keys.reshape(rows, kv_heads, HEAD_SIZE).astype(jnp.bfloat16)
    values = values.astype(jnp.bfloat16)
    new_keys = keys.reshape(steps, own_rows, kv_heads * HEAD_SIZE)
    new_values = values.reshape(steps, own_rows, kv_heads * HEAD_SIZE)
    own_query = query.reshape(steps, own_rows, q_heads, HEAD_SIZE).transpose(1, 0, 2, 3)

    request_ids = jnp.arange(requests, dtype=jnp.int32)
    is_long = req_len == long_len
    long_count = is_long.astype(jnp.int32)
    rank = jnp.sum(
        jnp.where(request_ids[None, :] < request_ids[:, None], long_count[None, :], 0), axis=1
    )
    long_ids = jnp.sum(
        jnp.where(
            is_long[None, :] & (rank[None, :] == jnp.arange(LONG_COUNT, dtype=jnp.int32)[:, None]),
            request_ids[None, :],
            0,
        ),
        axis=1,
    )
    own_pick = long_ids[:, None] == own_ids[None, :]
    long_table = jnp.sum(
        jnp.where(own_pick[:, :, None, None, None], own_query[None], jnp.zeros((), jnp.bfloat16)), axis=1
    ).astype(jnp.bfloat16)
    long_table, (slot_request, slot_block, slot_empty, slot_lengths) = butterfly(
        long_table, n_seq, lambda a, b: a + b, (slot_request, slot_block, slot_empty, req_len)
    )

    hit = slot_request[:, None] == request_ids[None, :]
    slot_req_long = jnp.any(hit & is_long[None, :], axis=1)
    slot_rank = jnp.sum(jnp.where(hit, rank[None, :], 0), axis=1)
    slot_len = jnp.sum(jnp.where(hit, slot_lengths[None, :], 0), axis=1)
    local_row = slot_request - first_row
    slot_local = (local_row >= 0) & (local_row < own_rows)
    pick = jnp.where(
        slot_req_long, slot_rank, jnp.where(slot_local, LONG_COUNT + local_row, LONG_COUNT + own_rows)
    )
    candidates = jnp.concatenate(
        [long_table, own_query, jnp.zeros((1,) + own_query.shape[1:], jnp.bfloat16)], axis=0
    )
    slot_query = jnp.take(candidates, pick, axis=0).reshape(
        slot_count, steps, kv_heads, head_sharing, HEAD_SIZE
    )
    keys_split = cached_key_blocks.reshape(slot_count, block_len, kv_heads, HEAD_SIZE)
    values_split = cached_value_blocks.reshape(slot_count, block_len, kv_heads, HEAD_SIZE)
    scores = (
        jnp.einsum("stngd,sknd->stngk", slot_query, keys_split, preferred_element_type=jnp.float32)
        * scaling
    )
    kept = slot_empty == 0
    filled = kept[:, None] & (
        slot_block[:, None] * block_len + jnp.arange(block_len, dtype=jnp.int32)[None, :] < slot_len[:, None]
    )
    filled_wide = filled[:, None, None, None, :]
    slot_top = jnp.max(jnp.where(filled_wide, scores, NEGATIVE), axis=-1)
    same = (slot_request[:, None] == slot_request[None, :]) & kept[None, :]
    reference_top = jnp.max(
        jnp.where(same[:, :, None, None, None], slot_top[None], NEGATIVE), axis=1
    )
    weights = jnp.where(
        filled_wide, jnp.exp(jnp.where(filled_wide, scores - reference_top[..., None], 0.0)), 0.0
    )
    slot_total = jnp.sum(weights, axis=-1)
    slot_mix = jnp.einsum(
        "stngk,sknd->stngd", weights.astype(jnp.bfloat16), values_split, preferred_element_type=jnp.float32
    )

    group_ids = jnp.concatenate([long_ids, own_ids])
    member = (group_ids[:, None] == slot_request[None, :]) & kept[None, :]
    member_float = member.astype(jnp.float32)
    group_top = jnp.max(jnp.where(member[:, :, None, None, None], reference_top[None], NEGATIVE), axis=1)
    group_total = jnp.einsum("qs,stng->qtng", member_float, slot_total, precision=HIGHEST)
    group_mix = jnp.einsum("qs,stngd->qtngd", member_float, slot_mix, precision=HIGHEST)
    stats = jnp.concatenate(
        [group_mix, group_total[..., None], group_top[..., None]], axis=-1
    )
    long_stats = stats[:LONG_COUNT].reshape(-1, HEAD_SIZE + 2).T
    long_mix, long_small = stats_butterfly(long_stats[:HEAD_SIZE], long_stats[HEAD_SIZE:], n_seq)
    long_stats = jnp.concatenate([long_mix, long_small], axis=0)
    long_stats = long_stats.T.reshape((LONG_COUNT,) + stats.shape[1:])
    own_rank = lax.dynamic_slice_in_dim(rank, first_row, own_rows)
    own_is_long = lax.dynamic_slice_in_dim(is_long, first_row, own_rows)
    rank_hit = own_rank[:, None] == jnp.arange(LONG_COUNT, dtype=jnp.int32)[None, :]
    from_long = jnp.sum(
        jnp.where(rank_hit[:, :, None, None, None, None], long_stats[None], 0.0), axis=1
    )
    cache_stats = jnp.where(own_is_long[:, None, None, None, None], from_long, stats[LONG_COUNT:])
    cache_mix = cache_stats[..., :HEAD_SIZE]
    cache_total = cache_stats[..., HEAD_SIZE]
    cache_top = cache_stats[..., HEAD_SIZE + 1]

    heads = own_query.reshape(own_rows, steps, kv_heads, head_sharing, HEAD_SIZE)
    fresh_keys = keys.reshape(steps, own_rows, kv_heads, HEAD_SIZE).transpose(1, 0, 2, 3)
    fresh_values = values.reshape(steps, own_rows, kv_heads, HEAD_SIZE).transpose(1, 0, 2, 3)
    fresh_scores = (
        jnp.einsum("rtngd,rjnd->rtngj", heads, fresh_keys, preferred_element_type=jnp.float32) * scaling
    )
    allowed = (jnp.arange(steps, dtype=jnp.int32)[None, :] <= jnp.arange(steps, dtype=jnp.int32)[:, None])[
        None, :, None, None, :
    ]
    fresh_top = jnp.max(jnp.where(allowed, fresh_scores, NEGATIVE), axis=-1)
    fresh_weights = jnp.where(
        allowed, jnp.exp(jnp.where(allowed, fresh_scores - fresh_top[..., None], 0.0)), 0.0
    )
    fresh_total = jnp.sum(fresh_weights, axis=-1)
    fresh_mix = jnp.einsum(
        "rtngj,rjnd->rtngd",
        fresh_weights.astype(jnp.bfloat16),
        fresh_values,
        preferred_element_type=jnp.float32,
    )
    overall = jnp.maximum(cache_top, fresh_top)
    retained = jnp.exp(cache_top - overall)
    fresh_scale = jnp.exp(fresh_top - overall)
    denominator = cache_total * retained + fresh_total * fresh_scale
    mixture = cache_mix * retained[..., None] + fresh_mix * fresh_scale[..., None]
    attended = (mixture / denominator[..., None]).astype(jnp.bfloat16)
    attended = attended.transpose(1, 0, 2, 3, 4).reshape(steps * own_rows, q_heads * HEAD_SIZE)
    projected = chunked_matmul(attended, w_out, n_mp)
    summed = reduce_scatter_mp(projected, n_mp).reshape(steps, own_rows, -1)
    hidden = (states.astype(jnp.float32) + summed).astype(jnp.bfloat16)
    return hidden, new_keys, new_values


def solution(mesh):
    n_seq = mesh.shape["seq"]
    n_mp = mesh.shape["mp"]
    placed = (
        P(None, "seq", "mp"),
        P(),
        P(),
        P(),
        P(None, "mp"),
        P(None, "mp"),
        P(None, "mp"),
        P("mp", None),
        P("seq", None, "mp"),
        P("seq", None, "mp"),
        P(),
        P("seq"),
        P("seq"),
        P("seq"),
    )

    def body(*args):
        return shards(*args, n_seq=n_seq, n_mp=n_mp)

    return jax.shard_map(
        body,
        mesh=mesh,
        in_specs=placed,
        out_specs=(P(None, "seq", "mp"), P(None, "seq", "mp"), P(None, "seq", "mp")),
        check_vma=False,
    )
```

```python
import jax
import jax.numpy as jnp
from jax import lax
from jax.experimental import pallas as pl
from jax.experimental.pallas import tpu as pltpu
from jax.sharding import PartitionSpec as P

HEAD_SIZE = 128
LONG_COUNT = 12

ROPE_BASE = 1000000.0
NEGATIVE = -1e30
HIGHEST = lax.Precision.HIGHEST


def scaled_rms(values, gain):
    return values * lax.rsqrt(jnp.mean(values * values, axis=-1, keepdims=True) + 1e-06) * gain


def rotate(values, positions):
    halfway = values.shape[-1] // 2
    frequency = ROPE_BASE ** (-(jnp.arange(halfway, dtype=jnp.float32) * 2.0) / values.shape[-1])
    angles = positions.astype(jnp.float32)[..., None, None] * frequency
    cosine = jnp.cos(angles)
    sine_part = jnp.sin(angles)
    leading = values[..., :halfway]
    trailing = values[..., halfway:]
    return jnp.concatenate(
        [leading * cosine - trailing * sine_part, trailing * cosine + leading * sine_part], axis=-1
    )


def _matmul_kernel(x_ref, *refs):
    count = len(refs) // 2
    x = x_ref[...]
    for w_ref, o_ref in zip(refs[:count], refs[count:]):
        o_ref[...] = jnp.dot(x, w_ref[...], preferred_element_type=jnp.float32)


def _project_kernel(x_ref, g_ref, qg_ref, kg_ref, cos_ref, sin_ref, wq_ref, wk_ref, wv_ref, q_ref, k_ref, v_ref):
    x = x_ref[...].astype(jnp.float32)
    scale = lax.rsqrt(jnp.mean(x * x, axis=-1, keepdims=True) + 1e-06)
    normed = (x * scale * g_ref[...]).astype(jnp.bfloat16)
    cosine = cos_ref[...]
    sine = sin_ref[...]

    def norm_rotate(y, gain):
        y = y * lax.rsqrt(jnp.mean(y * y, axis=-1, keepdims=True) + 1e-06) * gain
        return y * cosine + pltpu.roll(y, HEAD_SIZE // 2, 1) * sine

    for w_ref, o_ref, gain_ref in ((wq_ref, q_ref, qg_ref), (wk_ref, k_ref, kg_ref)):
        product = jnp.dot(normed, w_ref[...], preferred_element_type=jnp.float32)
        gain = gain_ref[...]
        for h in range(product.shape[1] // HEAD_SIZE):
            o_ref[:, h * HEAD_SIZE : (h + 1) * HEAD_SIZE] = norm_rotate(
                product[:, h * HEAD_SIZE : (h + 1) * HEAD_SIZE], gain
            )
    v_ref[...] = jnp.dot(normed, wv_ref[...], preferred_element_type=jnp.float32)


def project_rows(x, gain, query_gain, key_gain, positions, w_query, key_matrix, value_matrix):
    m, k = x.shape
    halfway = HEAD_SIZE // 2
    frequency = ROPE_BASE ** (-(jnp.arange(halfway, dtype=jnp.float32) * 2.0) / HEAD_SIZE)
    angles = positions.astype(jnp.float32)[:, None] * frequency
    cosine = jnp.cos(angles)
    sine = jnp.sin(angles)
    cos_both = jnp.concatenate([cosine, cosine], axis=-1)
    sin_signed = jnp.concatenate([-sine, sine], axis=-1)
    weights = (w_query, key_matrix, value_matrix)
    widths = [w.shape[1] for w in weights]
    return pl.pallas_call(
        _project_kernel,
        out_shape=[jax.ShapeDtypeStruct((m, n), jnp.float32) for n in widths],
        cost_estimate=pl.CostEstimate(
            flops=2 * m * k * sum(widths),
            bytes_accessed=2 * (m * k + k * sum(widths)) + 4 * m * sum(widths),
            transcendentals=m,
        ),
    )(
        x,
        gain.reshape(1, k),
        query_gain.reshape(1, HEAD_SIZE),
        key_gain.reshape(1, HEAD_SIZE),
        cos_both,
        sin_signed,
        *weights,
    )


def _vmem():
    return pl.BlockSpec(memory_space=pltpu.VMEM)


def small_matmul(x, *weights):
    m, k = x.shape
    widths = [w.shape[1] for w in weights]
    return pl.pallas_call(
        _matmul_kernel,
        out_shape=[jax.ShapeDtypeStruct((m, n), jnp.float32) for n in widths],
        in_specs=[_vmem() for _ in range(1 + len(weights))],
        out_specs=[_vmem() for _ in widths],
        cost_estimate=pl.CostEstimate(
            flops=2 * m * k * sum(widths),
            bytes_accessed=2 * (m * k + k * sum(widths)) + 4 * m * sum(widths),
            transcendentals=0,
        ),
    )(x, *weights)


def _chunked_kernel(x_ref, w_ref, o_ref):
    chunks, _, width = o_ref.shape
    me = lax.axis_index("mp")
    x = x_ref[...]
    products = [
        jnp.dot(x, w_ref[:, c * width : (c + 1) * width], preferred_element_type=jnp.float32)
        for c in range(chunks)
    ]
    for s in range(chunks):
        index = (me + s) % chunks
        chosen = products[0]
        for c in range(1, chunks):
            chosen = jnp.where(index == c, products[c], chosen)
        o_ref[s] = chosen


def chunked_matmul(x, w, chunks):
    m, k = x.shape
    n = w.shape[1]
    return pl.pallas_call(
        _chunked_kernel,
        out_shape=jax.ShapeDtypeStruct((chunks, m, n // chunks), jnp.float32),
        in_specs=[_vmem(), _vmem()],
        out_specs=_vmem(),
        cost_estimate=pl.CostEstimate(
            flops=2 * m * k * n, bytes_accessed=2 * (m * k + k * n) + 4 * m * n, transcendentals=0
        ),
    )(x, w)


def gather_mp(block, n_mp):
    me = lax.axis_index("mp")
    pieces = [block] + [
        lax.ppermute(block, "mp", [(i, (i + s) % n_mp) for i in range(n_mp)]) for s in range(1, n_mp)
    ]
    ordered = []
    for c in range(n_mp):
        shift = (me - c) % n_mp
        chosen = pieces[0]
        for s in range(1, n_mp):
            chosen = jnp.where(shift == s, pieces[s], chosen)
        ordered.append(chosen)
    return jnp.concatenate(ordered, axis=-1)


def reduce_scatter_mp(chunks, n_mp):
    total = chunks[0]
    for s in range(1, n_mp):
        total = total + lax.ppermute(chunks[s], "mp", [(i, (i + s) % n_mp) for i in range(n_mp)])
    return total


def seq_masks(n_seq):
    if n_seq == 64:
        return [1, 2, 4, 12, 16, 48]
    return [1 << b for b in range(n_seq.bit_length() - 1)]


def butterfly(value, n_seq, combine, extras=None):
    for index, stride in enumerate(seq_masks(n_seq)):
        partner = lax.ppermute(value, "seq", [(i, i ^ stride) for i in range(n_seq)])
        value = combine(value, partner)
        if index == 0 and extras is not None:
            value, extras = lax.optimization_barrier((value, extras))
    return value, extras


def merge_stats(mine, theirs):
    mix_a, stats_a = mine
    mix_b, stats_b = theirs
    top_a = stats_a[1:]
    top_b = stats_b[1:]
    top = jnp.maximum(top_a, top_b)
    scale_a = jnp.exp(top_a - top)
    scale_b = jnp.exp(top_b - top)
    mix = mix_a * scale_a + mix_b.astype(jnp.float32) * scale_b
    total = stats_a[:1] * scale_a + stats_b[:1] * scale_b
    return mix, jnp.concatenate([total, top], axis=0)


def split_exact(x):
    hi = lax.reduce_precision(x, exponent_bits=8, mantissa_bits=7)
    rest = x - hi
    mid = lax.reduce_precision(rest, exponent_bits=8, mantissa_bits=7)
    lo = rest - mid
    return jnp.concatenate([hi, mid, lo], axis=0).astype(jnp.bfloat16)


def join_exact(parts):
    parts = parts.astype(jnp.float32)
    return parts[0:1] + parts[1:2] + parts[2:3]


def stats_butterfly(mix, stats, n_seq):
    width = mix.shape[0]
    for stride in seq_masks(n_seq):
        pairs = [(i, i ^ stride) for i in range(n_seq)]
        packed = jnp.concatenate(
            [mix.astype(jnp.bfloat16), split_exact(stats[:1]), split_exact(stats[1:])], axis=0
        )
        arrived = lax.ppermute(packed, "seq", pairs)
        theirs = (
            arrived[:width],
            jnp.concatenate(
                [join_exact(arrived[width : width + 3]), join_exact(arrived[width + 3 : width + 6])], axis=0
            ),
        )
        mix, stats = merge_stats((mix, stats), theirs)
    return mix, stats


def shards(
    states,
    norm_gain,
    query_gain,
    key_gain,
    w_query,
    key_matrix,
    value_matrix,
    w_out,
    cached_key_blocks,
    cached_value_blocks,
    req_len,
    slot_request,
    slot_block,
    slot_empty,
    n_seq,
    n_mp,
):
    steps, own_rows, _ = states.shape
    me = lax.axis_index("seq")
    first_row = me * own_rows
    kv_heads = key_matrix.shape[1] // HEAD_SIZE
    q_heads = w_query.shape[1] // HEAD_SIZE
    head_sharing = q_heads // kv_heads
    slot_count, block_len, _ = cached_key_blocks.shape
    requests = req_len.shape[0]
    long_len = n_seq * block_len
    scaling = HEAD_SIZE ** (-0.5)

    wide = gather_mp(states, n_mp).reshape(steps * own_rows, -1)
    own_ids = first_row + jnp.arange(own_rows, dtype=jnp.int32)
    own_len = lax.dynamic_slice_in_dim(req_len, first_row, own_rows)
    positions = (own_len[None, :] + jnp.arange(steps, dtype=jnp.int32)[:, None]).reshape(-1)
    rows = steps * own_rows
    query, keys, values = project_rows(
        wide, norm_gain, query_gain, key_gain, positions, w_query, key_matrix, value_matrix
    )
    query = query.reshape(rows, q_heads, HEAD_SIZE).astype(jnp.bfloat16)
    keys = keys.reshape(rows, kv_heads, HEAD_SIZE).astype(jnp.bfloat16)
    values = values.astype(jnp.bfloat16)
    new_keys = keys.reshape(steps, own_rows, kv_heads * HEAD_SIZE)
    new_values = values.reshape(steps, own_rows, kv_heads * HEAD_SIZE)
    own_query = query.reshape(steps, own_rows, q_heads, HEAD_SIZE).transpose(1, 0, 2, 3)

    request_ids = jnp.arange(requests, dtype=jnp.int32)
    is_long = req_len == long_len
    long_count = is_long.astype(jnp.int32)
    rank = jnp.sum(
        jnp.where(request_ids[None, :] < request_ids[:, None], long_count[None, :], 0), axis=1
    )
    long_ids = jnp.sum(
        jnp.where(
            is_long[None, :] & (rank[None, :] == jnp.arange(LONG_COUNT, dtype=jnp.int32)[:, None]),
            request_ids[None, :],
            0,
        ),
        axis=1,
    )
    own_pick = long_ids[:, None] == own_ids[None, :]
    long_table = jnp.sum(
        jnp.where(own_pick[:, :, None, None, None], own_query[None], jnp.zeros((), jnp.bfloat16)), axis=1
    ).astype(jnp.bfloat16)
    long_table, (slot_request, slot_block, slot_empty, slot_lengths) = butterfly(
        long_table, n_seq, lambda a, b: a + b, (slot_request, slot_block, slot_empty, req_len)
    )

    hit = slot_request[:, None] == request_ids[None, :]
    slot_req_long = jnp.any(hit & is_long[None, :], axis=1)
    slot_rank = jnp.sum(jnp.where(hit, rank[None, :], 0), axis=1)
    slot_len = jnp.sum(jnp.where(hit, slot_lengths[None, :], 0), axis=1)
    local_row = slot_request - first_row
    slot_local = (local_row >= 0) & (local_row < own_rows)
    pick = jnp.where(
        slot_req_long, slot_rank, jnp.where(slot_local, LONG_COUNT + local_row, LONG_COUNT + own_rows)
    )
    candidates = jnp.concatenate(
        [long_table, own_query, jnp.zeros((1,) + own_query.shape[1:], jnp.bfloat16)], axis=0
    )
    slot_query = jnp.take(candidates, pick, axis=0).reshape(
        slot_count, steps, kv_heads, head_sharing, HEAD_SIZE
    )
    keys_split = cached_key_blocks.reshape(slot_count, block_len, kv_heads, HEAD_SIZE)
    values_split = cached_value_blocks.reshape(slot_count, block_len, kv_heads, HEAD_SIZE)
    scores = (
        jnp.einsum("stngd,sknd->stngk", slot_query, keys_split, preferred_element_type=jnp.float32)
        * scaling
    )
    kept = slot_empty == 0
    filled = kept[:, None] & (
        slot_block[:, None] * block_len + jnp.arange(block_len, dtype=jnp.int32)[None, :] < slot_len[:, None]
    )
    filled_wide = filled[:, None, None, None, :]
    slot_top = jnp.max(jnp.where(filled_wide, scores, NEGATIVE), axis=-1)
    same = (slot_request[:, None] == slot_request[None, :]) & kept[None, :]
    reference_top = jnp.max(
        jnp.where(same[:, :, None, None, None], slot_top[None], NEGATIVE), axis=1
    )
    weights = jnp.where(
        filled_wide, jnp.exp(jnp.where(filled_wide, scores - reference_top[..., None], 0.0)), 0.0
    )
    slot_total = jnp.sum(weights, axis=-1)
    slot_mix = jnp.einsum(
        "stngk,sknd->stngd", weights.astype(jnp.bfloat16), values_split, preferred_element_type=jnp.float32
    )

    group_ids = jnp.concatenate([long_ids, own_ids])
    member = (group_ids[:, None] == slot_request[None, :]) & kept[None, :]
    member_float = member.astype(jnp.float32)
    group_top = jnp.max(jnp.where(member[:, :, None, None, None], reference_top[None], NEGATIVE), axis=1)
    group_total = jnp.einsum("qs,stng->qtng", member_float, slot_total, precision=HIGHEST)
    group_mix = jnp.einsum("qs,stngd->qtngd", member_float, slot_mix, precision=HIGHEST)
    stats = jnp.concatenate(
        [group_mix, group_total[..., None], group_top[..., None]], axis=-1
    )
    long_stats = stats[:LONG_COUNT].reshape(-1, HEAD_SIZE + 2).T
    long_mix, long_small = stats_butterfly(long_stats[:HEAD_SIZE], long_stats[HEAD_SIZE:], n_seq)
    long_stats = jnp.concatenate([long_mix, long_small], axis=0)
    long_stats = long_stats.T.reshape((LONG_COUNT,) + stats.shape[1:])
    own_rank = lax.dynamic_slice_in_dim(rank, first_row, own_rows)
    own_is_long = lax.dynamic_slice_in_dim(is_long, first_row, own_rows)
    rank_hit = own_rank[:, None] == jnp.arange(LONG_COUNT, dtype=jnp.int32)[None, :]
    from_long = jnp.sum(
        jnp.where(rank_hit[:, :, None, None, None, None], long_stats[None], 0.0), axis=1
    )
    cache_stats = jnp.where(own_is_long[:, None, None, None, None], from_long, stats[LONG_COUNT:])
    cache_mix = cache_stats[..., :HEAD_SIZE]
    cache_total = cache_stats[..., HEAD_SIZE]
    cache_top = cache_stats[..., HEAD_SIZE + 1]

    heads = own_query.reshape(own_rows, steps, kv_heads, head_sharing, HEAD_SIZE)
    fresh_keys = keys.reshape(steps, own_rows, kv_heads, HEAD_SIZE).transpose(1, 0, 2, 3)
    fresh_values = values.reshape(steps, own_rows, kv_heads, HEAD_SIZE).transpose(1, 0, 2, 3)
    fresh_scores = (
        jnp.einsum("rtngd,rjnd->rtngj", heads, fresh_keys, preferred_element_type=jnp.float32) * scaling
    )
    allowed = (jnp.arange(steps, dtype=jnp.int32)[None, :] <= jnp.arange(steps, dtype=jnp.int32)[:, None])[
        None, :, None, None, :
    ]
    fresh_top = jnp.max(jnp.where(allowed, fresh_scores, NEGATIVE), axis=-1)
    fresh_weights = jnp.where(
        allowed, jnp.exp(jnp.where(allowed, fresh_scores - fresh_top[..., None], 0.0)), 0.0
    )
    fresh_total = jnp.sum(fresh_weights, axis=-1)
    fresh_mix = jnp.einsum(
        "rtngj,rjnd->rtngd",
        fresh_weights.astype(jnp.bfloat16),
        fresh_values,
        preferred_element_type=jnp.float32,
    )
    overall = jnp.maximum(cache_top, fresh_top)
    retained = jnp.exp(cache_top - overall)
    fresh_scale = jnp.exp(fresh_top - overall)
    denominator = cache_total * retained + fresh_total * fresh_scale
    mixture = cache_mix * retained[..., None] + fresh_mix * fresh_scale[..., None]
    attended = (mixture / denominator[..., None]).astype(jnp.bfloat16)
    attended = attended.transpose(1, 0, 2, 3, 4).reshape(steps * own_rows, q_heads * HEAD_SIZE)
    projected = chunked_matmul(attended, w_out, n_mp)
    summed = reduce_scatter_mp(projected, n_mp).reshape(steps, own_rows, -1)
    hidden = (states.astype(jnp.float32) + summed).astype(jnp.bfloat16)
    return hidden, new_keys, new_values


def solution(mesh):
    n_seq = mesh.shape["seq"]
    n_mp = mesh.shape["mp"]
    placed = (
        P(None, "seq", "mp"),
        P(),
        P(),
        P(),
        P(None, "mp"),
        P(None, "mp"),
        P(None, "mp"),
        P("mp", None),
        P("seq", None, "mp"),
        P("seq", None, "mp"),
        P(),
        P("seq"),
        P("seq"),
        P("seq"),
    )

    def body(*args):
        return shards(*args, n_seq=n_seq, n_mp=n_mp)

    return jax.shard_map(
        body,
        mesh=mesh,
        in_specs=placed,
        out_specs=(P(None, "seq", "mp"), P(None, "seq", "mp"), P(None, "seq", "mp")),
        check_vma=False,
    )
```

```python
import jax
import jax.numpy as jnp
from jax import lax
from jax.experimental import pallas as pl
from jax.experimental.pallas import tpu as pltpu
from jax.sharding import PartitionSpec as P

HEAD_SIZE = 128
LONG_COUNT = 12

ROPE_BASE = 1000000.0
NEGATIVE = -1e30
HIGHEST = lax.Precision.HIGHEST


def scaled_rms(values, gain):
    return values * lax.rsqrt(jnp.mean(values * values, axis=-1, keepdims=True) + 1e-06) * gain


def rotate(values, positions):
    halfway = values.shape[-1] // 2
    frequency = ROPE_BASE ** (-(jnp.arange(halfway, dtype=jnp.float32) * 2.0) / values.shape[-1])
    angles = positions.astype(jnp.float32)[..., None, None] * frequency
    cosine = jnp.cos(angles)
    sine_part = jnp.sin(angles)
    leading = values[..., :halfway]
    trailing = values[..., halfway:]
    return jnp.concatenate(
        [leading * cosine - trailing * sine_part, trailing * cosine + leading * sine_part], axis=-1
    )


def _matmul_kernel(x_ref, *refs):
    count = len(refs) // 2
    x = x_ref[...]
    for w_ref, o_ref in zip(refs[:count], refs[count:]):
        o_ref[...] = jnp.dot(x, w_ref[...], preferred_element_type=jnp.float32)


def _project_kernel(x_ref, g_ref, qg_ref, kg_ref, cos_ref, sin_ref, wq_ref, wk_ref, wv_ref, q_ref, k_ref, v_ref):
    x = x_ref[...].astype(jnp.float32)
    scale = lax.rsqrt(jnp.mean(x * x, axis=-1, keepdims=True) + 1e-06)
    normed = (x * scale * g_ref[...]).astype(jnp.bfloat16)
    cosine = cos_ref[...]
    sine = sin_ref[...]

    def norm_rotate(y, gain):
        y = y * lax.rsqrt(jnp.mean(y * y, axis=-1, keepdims=True) + 1e-06) * gain
        return y * cosine + pltpu.roll(y, HEAD_SIZE // 2, 1) * sine

    for w_ref, o_ref, gain_ref in ((wq_ref, q_ref, qg_ref), (wk_ref, k_ref, kg_ref)):
        product = jnp.dot(normed, w_ref[...], preferred_element_type=jnp.float32)
        gain = gain_ref[...]
        for h in range(product.shape[1] // HEAD_SIZE):
            o_ref[:, h * HEAD_SIZE : (h + 1) * HEAD_SIZE] = norm_rotate(
                product[:, h * HEAD_SIZE : (h + 1) * HEAD_SIZE], gain
            ).astype(o_ref.dtype)
    v_ref[...] = jnp.dot(normed, wv_ref[...], preferred_element_type=jnp.float32).astype(v_ref.dtype)


def project_rows(x, gain, query_gain, key_gain, positions, w_query, key_matrix, value_matrix):
    m, k = x.shape
    halfway = HEAD_SIZE // 2
    frequency = ROPE_BASE ** (-(jnp.arange(halfway, dtype=jnp.float32) * 2.0) / HEAD_SIZE)
    angles = positions.astype(jnp.float32)[:, None] * frequency
    cosine = jnp.cos(angles)
    sine = jnp.sin(angles)
    cos_both = jnp.concatenate([cosine, cosine], axis=-1)
    sin_signed = jnp.concatenate([-sine, sine], axis=-1)
    weights = (w_query, key_matrix, value_matrix)
    widths = [w.shape[1] for w in weights]
    return pl.pallas_call(
        _project_kernel,
        out_shape=[jax.ShapeDtypeStruct((m, n), jnp.bfloat16) for n in widths],
        cost_estimate=pl.CostEstimate(
            flops=2 * m * k * sum(widths),
            bytes_accessed=2 * (m * k + k * sum(widths)) + 2 * m * sum(widths),
            transcendentals=m,
        ),
    )(
        x,
        gain.reshape(1, k),
        query_gain.reshape(1, HEAD_SIZE),
        key_gain.reshape(1, HEAD_SIZE),
        cos_both,
        sin_signed,
        *weights,
    )


def _vmem():
    return pl.BlockSpec(memory_space=pltpu.VMEM)


def small_matmul(x, *weights):
    m, k = x.shape
    widths = [w.shape[1] for w in weights]
    return pl.pallas_call(
        _matmul_kernel,
        out_shape=[jax.ShapeDtypeStruct((m, n), jnp.float32) for n in widths],
        in_specs=[_vmem() for _ in range(1 + len(weights))],
        out_specs=[_vmem() for _ in widths],
        cost_estimate=pl.CostEstimate(
            flops=2 * m * k * sum(widths),
            bytes_accessed=2 * (m * k + k * sum(widths)) + 4 * m * sum(widths),
            transcendentals=0,
        ),
    )(x, *weights)


def _chunked_kernel(x_ref, w_ref, o_ref):
    chunks, _, width = o_ref.shape
    x = x_ref[...]
    for c in range(chunks):
        o_ref[c] = jnp.dot(x, w_ref[:, c * width : (c + 1) * width], preferred_element_type=jnp.float32)


def chunked_matmul(x, w, chunks):
    m, k = x.shape
    n = w.shape[1]
    return pl.pallas_call(
        _chunked_kernel,
        out_shape=jax.ShapeDtypeStruct((chunks, m, n // chunks), jnp.float32),
        in_specs=[_vmem(), _vmem()],
        out_specs=_vmem(),
        cost_estimate=pl.CostEstimate(
            flops=2 * m * k * n, bytes_accessed=2 * (m * k + k * n) + 4 * m * n, transcendentals=0
        ),
    )(x, w)


def gather_mp(block, n_mp):
    me = lax.axis_index("mp")
    pieces = [block] + [
        lax.ppermute(block, "mp", [(i, (i + s) % n_mp) for i in range(n_mp)]) for s in range(1, n_mp)
    ]
    ordered = []
    for c in range(n_mp):
        shift = (me - c) % n_mp
        chosen = pieces[0]
        for s in range(1, n_mp):
            chosen = jnp.where(shift == s, pieces[s], chosen)
        ordered.append(chosen)
    return jnp.concatenate(ordered, axis=-1)


def reduce_scatter_mp(chunks, n_mp):
    me = lax.axis_index("mp")
    total = lax.dynamic_index_in_dim(chunks, me, axis=0, keepdims=False)
    for s in range(1, n_mp):
        outgoing = lax.dynamic_index_in_dim(chunks, (me + s) % n_mp, axis=0, keepdims=False)
        total = total + lax.ppermute(outgoing, "mp", [(i, (i + s) % n_mp) for i in range(n_mp)])
    return total


def seq_masks(n_seq):
    if n_seq == 64:
        return [1, 2, 4, 12, 16, 48]
    return [1 << b for b in range(n_seq.bit_length() - 1)]


def butterfly(value, n_seq, combine, extras=None):
    for index, stride in enumerate(seq_masks(n_seq)):
        partner = lax.ppermute(value, "seq", [(i, i ^ stride) for i in range(n_seq)])
        value = combine(value, partner)
        if index == 0 and extras is not None:
            value, extras = lax.optimization_barrier((value, extras))
    return value, extras


def merge_stats(mine, theirs):
    mix_a, stats_a = mine
    mix_b, stats_b = theirs
    top_a = stats_a[1:]
    top_b = stats_b[1:]
    top = jnp.maximum(top_a, top_b)
    scale_a = jnp.exp(top_a - top)
    scale_b = jnp.exp(top_b - top)
    mix = mix_a * scale_a + mix_b.astype(jnp.float32) * scale_b
    total = stats_a[:1] * scale_a + stats_b[:1] * scale_b
    return mix, jnp.concatenate([total, top], axis=0)


def split_exact(x):
    hi = lax.reduce_precision(x, exponent_bits=8, mantissa_bits=7)
    rest = x - hi
    mid = lax.reduce_precision(rest, exponent_bits=8, mantissa_bits=7)
    lo = rest - mid
    return jnp.concatenate([hi, mid, lo], axis=0).astype(jnp.bfloat16)


def join_exact(parts):
    parts = parts.astype(jnp.float32)
    return parts[0:1] + parts[1:2] + parts[2:3]


def stats_butterfly(mix, stats, n_seq):
    width = mix.shape[0]
    for stride in seq_masks(n_seq):
        pairs = [(i, i ^ stride) for i in range(n_seq)]
        packed = jnp.concatenate(
            [mix.astype(jnp.bfloat16), split_exact(stats[:1]), split_exact(stats[1:])], axis=0
        )
        arrived = lax.ppermute(packed, "seq", pairs)
        theirs = (
            arrived[:width],
            jnp.concatenate(
                [join_exact(arrived[width : width + 3]), join_exact(arrived[width + 3 : width + 6])], axis=0
            ),
        )
        mix, stats = merge_stats((mix, stats), theirs)
    return mix, stats


def shards(
    states,
    norm_gain,
    query_gain,
    key_gain,
    w_query,
    key_matrix,
    value_matrix,
    w_out,
    cached_key_blocks,
    cached_value_blocks,
    req_len,
    slot_request,
    slot_block,
    slot_empty,
    n_seq,
    n_mp,
):
    steps, own_rows, _ = states.shape
    me = lax.axis_index("seq")
    first_row = me * own_rows
    kv_heads = key_matrix.shape[1] // HEAD_SIZE
    q_heads = w_query.shape[1] // HEAD_SIZE
    head_sharing = q_heads // kv_heads
    slot_count, block_len, _ = cached_key_blocks.shape
    requests = req_len.shape[0]
    long_len = n_seq * block_len
    scaling = HEAD_SIZE ** (-0.5)

    wide = gather_mp(states, n_mp).reshape(steps * own_rows, -1)
    own_ids = first_row + jnp.arange(own_rows, dtype=jnp.int32)
    own_len = lax.dynamic_slice_in_dim(req_len, first_row, own_rows)
    positions = (own_len[None, :] + jnp.arange(steps, dtype=jnp.int32)[:, None]).reshape(-1)
    rows = steps * own_rows
    query, keys, values = project_rows(
        wide, norm_gain, query_gain, key_gain, positions, w_query, key_matrix, value_matrix
    )
    query = query.reshape(rows, q_heads, HEAD_SIZE)
    keys = keys.reshape(rows, kv_heads, HEAD_SIZE)
    new_keys = keys.reshape(steps, own_rows, kv_heads * HEAD_SIZE)
    new_values = values.reshape(steps, own_rows, kv_heads * HEAD_SIZE)
    own_query = query.reshape(steps, own_rows, q_heads, HEAD_SIZE).transpose(1, 0, 2, 3)

    request_ids = jnp.arange(requests, dtype=jnp.int32)
    is_long = req_len == long_len
    long_count = is_long.astype(jnp.int32)
    rank = jnp.sum(
        jnp.where(request_ids[None, :] < request_ids[:, None], long_count[None, :], 0), axis=1
    )
    long_ids = jnp.sum(
        jnp.where(
            is_long[None, :] & (rank[None, :] == jnp.arange(LONG_COUNT, dtype=jnp.int32)[:, None]),
            request_ids[None, :],
            0,
        ),
        axis=1,
    )
    own_pick = long_ids[:, None] == own_ids[None, :]
    long_table = jnp.sum(
        jnp.where(own_pick[:, :, None, None, None], own_query[None], jnp.zeros((), jnp.bfloat16)), axis=1
    ).astype(jnp.bfloat16)
    long_table, (slot_request, slot_block, slot_empty, slot_lengths) = butterfly(
        long_table, n_seq, lambda a, b: a + b, (slot_request, slot_block, slot_empty, req_len)
    )

    hit = slot_request[:, None] == request_ids[None, :]
    slot_req_long = jnp.any(hit & is_long[None, :], axis=1)
    slot_rank = jnp.sum(jnp.where(hit, rank[None, :], 0), axis=1)
    slot_len = jnp.sum(jnp.where(hit, slot_lengths[None, :], 0), axis=1)
    local_row = slot_request - first_row
    slot_local = (local_row >= 0) & (local_row < own_rows)
    pick = jnp.where(
        slot_req_long, slot_rank, jnp.where(slot_local, LONG_COUNT + local_row, LONG_COUNT + own_rows)
    )
    candidates = jnp.concatenate(
        [long_table, own_query, jnp.zeros((1,) + own_query.shape[1:], jnp.bfloat16)], axis=0
    )
    slot_query = jnp.take(candidates, pick, axis=0).reshape(
        slot_count, steps, kv_heads, head_sharing, HEAD_SIZE
    )
    keys_split = cached_key_blocks.reshape(slot_count, block_len, kv_heads, HEAD_SIZE)
    values_split = cached_value_blocks.reshape(slot_count, block_len, kv_heads, HEAD_SIZE)
    scores = (
        jnp.einsum("stngd,sknd->stngk", slot_query, keys_split, preferred_element_type=jnp.float32)
        * scaling
    )
    kept = slot_empty == 0
    filled = kept[:, None] & (
        slot_block[:, None] * block_len + jnp.arange(block_len, dtype=jnp.int32)[None, :] < slot_len[:, None]
    )
    filled_wide = filled[:, None, None, None, :]
    slot_top = jnp.max(jnp.where(filled_wide, scores, NEGATIVE), axis=-1)
    same = (slot_request[:, None] == slot_request[None, :]) & kept[None, :]
    reference_top = jnp.max(
        jnp.where(same[:, :, None, None, None], slot_top[None], NEGATIVE), axis=1
    )
    weights = jnp.where(
        filled_wide, jnp.exp(jnp.where(filled_wide, scores - reference_top[..., None], 0.0)), 0.0
    )
    slot_total = jnp.sum(weights, axis=-1)
    slot_mix = jnp.einsum(
        "stngk,sknd->stngd", weights.astype(jnp.bfloat16), values_split, preferred_element_type=jnp.float32
    )

    group_ids = jnp.concatenate([long_ids, own_ids])
    member = (group_ids[:, None] == slot_request[None, :]) & kept[None, :]
    member_float = member.astype(jnp.float32)
    group_top = jnp.max(jnp.where(member[:, :, None, None, None], reference_top[None], NEGATIVE), axis=1)
    group_total = jnp.einsum("qs,stng->qtng", member_float, slot_total, precision=HIGHEST)
    group_mix = jnp.einsum("qs,stngd->qtngd", member_float, slot_mix, precision=HIGHEST)
    stats = jnp.concatenate(
        [group_mix, group_total[..., None], group_top[..., None]], axis=-1
    )
    long_stats = stats[:LONG_COUNT].reshape(-1, HEAD_SIZE + 2).T
    long_mix, long_small = stats_butterfly(long_stats[:HEAD_SIZE], long_stats[HEAD_SIZE:], n_seq)
    long_stats = jnp.concatenate([long_mix, long_small], axis=0)
    long_stats = long_stats.T.reshape((LONG_COUNT,) + stats.shape[1:])
    own_rank = lax.dynamic_slice_in_dim(rank, first_row, own_rows)
    own_is_long = lax.dynamic_slice_in_dim(is_long, first_row, own_rows)
    rank_hit = own_rank[:, None] == jnp.arange(LONG_COUNT, dtype=jnp.int32)[None, :]
    from_long = jnp.sum(
        jnp.where(rank_hit[:, :, None, None, None, None], long_stats[None], 0.0), axis=1
    )
    cache_stats = jnp.where(own_is_long[:, None, None, None, None], from_long, stats[LONG_COUNT:])
    cache_mix = cache_stats[..., :HEAD_SIZE]
    cache_total = cache_stats[..., HEAD_SIZE]
    cache_top = cache_stats[..., HEAD_SIZE + 1]

    heads = own_query.reshape(own_rows, steps, kv_heads, head_sharing, HEAD_SIZE)
    fresh_keys = keys.reshape(steps, own_rows, kv_heads, HEAD_SIZE).transpose(1, 0, 2, 3)
    fresh_values = values.reshape(steps, own_rows, kv_heads, HEAD_SIZE).transpose(1, 0, 2, 3)
    fresh_scores = (
        jnp.einsum("rtngd,rjnd->rtngj", heads, fresh_keys, preferred_element_type=jnp.float32) * scaling
    )
    allowed = (jnp.arange(steps, dtype=jnp.int32)[None, :] <= jnp.arange(steps, dtype=jnp.int32)[:, None])[
        None, :, None, None, :
    ]
    fresh_top = jnp.max(jnp.where(allowed, fresh_scores, NEGATIVE), axis=-1)
    fresh_weights = jnp.where(
        allowed, jnp.exp(jnp.where(allowed, fresh_scores - fresh_top[..., None], 0.0)), 0.0
    )
    fresh_total = jnp.sum(fresh_weights, axis=-1)
    fresh_mix = jnp.einsum(
        "rtngj,rjnd->rtngd",
        fresh_weights.astype(jnp.bfloat16),
        fresh_values,
        preferred_element_type=jnp.float32,
    )
    overall = jnp.maximum(cache_top, fresh_top)
    retained = jnp.exp(cache_top - overall)
    fresh_scale = jnp.exp(fresh_top - overall)
    denominator = cache_total * retained + fresh_total * fresh_scale
    mixture = cache_mix * retained[..., None] + fresh_mix * fresh_scale[..., None]
    attended = (mixture / denominator[..., None]).astype(jnp.bfloat16)
    attended = attended.transpose(1, 0, 2, 3, 4).reshape(steps * own_rows, q_heads * HEAD_SIZE)
    projected = chunked_matmul(attended, w_out, n_mp)
    summed = reduce_scatter_mp(projected, n_mp).reshape(steps, own_rows, -1)
    hidden = (states.astype(jnp.float32) + summed).astype(jnp.bfloat16)
    return hidden, new_keys, new_values


def solution(mesh):
    n_seq = mesh.shape["seq"]
    n_mp = mesh.shape["mp"]
    placed = (
        P(None, "seq", "mp"),
        P(),
        P(),
        P(),
        P(None, "mp"),
        P(None, "mp"),
        P(None, "mp"),
        P("mp", None),
        P("seq", None, "mp"),
        P("seq", None, "mp"),
        P(),
        P("seq"),
        P("seq"),
        P("seq"),
    )

    def body(*args):
        return shards(*args, n_seq=n_seq, n_mp=n_mp)

    return jax.shard_map(
        body,
        mesh=mesh,
        in_specs=placed,
        out_specs=(P(None, "seq", "mp"), P(None, "seq", "mp"), P(None, "seq", "mp")),
        check_vma=False,
    )
```

```python
import jax
import jax.numpy as jnp
from jax import lax
from jax.experimental import pallas as pl
from jax.experimental.pallas import tpu as pltpu
from jax.sharding import PartitionSpec as P

HEAD_SIZE = 128
LONG_COUNT = 12

ROPE_BASE = 1000000.0
NEGATIVE = -1e30
HIGHEST = lax.Precision.HIGHEST


def scaled_rms(values, gain):
    return values * lax.rsqrt(jnp.mean(values * values, axis=-1, keepdims=True) + 1e-06) * gain


def rotate(values, positions):
    halfway = values.shape[-1] // 2
    frequency = ROPE_BASE ** (-(jnp.arange(halfway, dtype=jnp.float32) * 2.0) / values.shape[-1])
    angles = positions.astype(jnp.float32)[..., None, None] * frequency
    cosine = jnp.cos(angles)
    sine_part = jnp.sin(angles)
    leading = values[..., :halfway]
    trailing = values[..., halfway:]
    return jnp.concatenate(
        [leading * cosine - trailing * sine_part, trailing * cosine + leading * sine_part], axis=-1
    )


def _matmul_kernel(x_ref, *refs):
    count = len(refs) // 2
    x = x_ref[...]
    for w_ref, o_ref in zip(refs[:count], refs[count:]):
        o_ref[...] = jnp.dot(x, w_ref[...], preferred_element_type=jnp.float32)


def _project_kernel(x_ref, g_ref, qg_ref, kg_ref, cos_ref, sin_ref, wq_ref, wk_ref, wv_ref, q_ref, k_ref, v_ref):
    x = x_ref[...].astype(jnp.float32)
    scale = lax.rsqrt(jnp.mean(x * x, axis=-1, keepdims=True) + 1e-06)
    normed = (x * scale * g_ref[...]).astype(jnp.bfloat16)
    cosine = cos_ref[...]
    sine = sin_ref[...]

    def norm_rotate(y, gain):
        y = y * lax.rsqrt(jnp.mean(y * y, axis=-1, keepdims=True) + 1e-06) * gain
        return y * cosine + pltpu.roll(y, HEAD_SIZE // 2, 1) * sine

    for w_ref, o_ref, gain_ref in ((wq_ref, q_ref, qg_ref), (wk_ref, k_ref, kg_ref)):
        product = jnp.dot(normed, w_ref[...], preferred_element_type=jnp.float32)
        gain = gain_ref[...]
        for h in range(product.shape[1] // HEAD_SIZE):
            o_ref[:, h * HEAD_SIZE : (h + 1) * HEAD_SIZE] = norm_rotate(
                product[:, h * HEAD_SIZE : (h + 1) * HEAD_SIZE], gain
            ).astype(o_ref.dtype)
    v_ref[...] = jnp.dot(normed, wv_ref[...], preferred_element_type=jnp.float32).astype(v_ref.dtype)


def project_rows(x, gain, query_gain, key_gain, positions, w_query, key_matrix, value_matrix):
    m, k = x.shape
    halfway = HEAD_SIZE // 2
    frequency = ROPE_BASE ** (-(jnp.arange(halfway, dtype=jnp.float32) * 2.0) / HEAD_SIZE)
    angles = positions.astype(jnp.float32)[:, None] * frequency
    cosine = jnp.cos(angles)
    sine = jnp.sin(angles)
    cos_both = jnp.concatenate([cosine, cosine], axis=-1)
    sin_signed = jnp.concatenate([-sine, sine], axis=-1)
    weights = (w_query, key_matrix, value_matrix)
    widths = [w.shape[1] for w in weights]
    return pl.pallas_call(
        _project_kernel,
        out_shape=[jax.ShapeDtypeStruct((m, n), jnp.bfloat16) for n in widths],
        cost_estimate=pl.CostEstimate(
            flops=2 * m * k * sum(widths),
            bytes_accessed=2 * (m * k + k * sum(widths)) + 2 * m * sum(widths),
            transcendentals=m,
        ),
    )(
        x,
        jnp.broadcast_to(gain[None, :], (m, k)),
        query_gain.reshape(1, HEAD_SIZE),
        key_gain.reshape(1, HEAD_SIZE),
        cos_both,
        sin_signed,
        *weights,
    )


def _vmem():
    return pl.BlockSpec(memory_space=pltpu.VMEM)


def small_matmul(x, *weights):
    m, k = x.shape
    widths = [w.shape[1] for w in weights]
    return pl.pallas_call(
        _matmul_kernel,
        out_shape=[jax.ShapeDtypeStruct((m, n), jnp.float32) for n in widths],
        in_specs=[_vmem() for _ in range(1 + len(weights))],
        out_specs=[_vmem() for _ in widths],
        cost_estimate=pl.CostEstimate(
            flops=2 * m * k * sum(widths),
            bytes_accessed=2 * (m * k + k * sum(widths)) + 4 * m * sum(widths),
            transcendentals=0,
        ),
    )(x, *weights)


def _chunked_kernel(x_ref, w_ref, o_ref):
    chunks, _, width = o_ref.shape
    x = x_ref[...]
    for c in range(chunks):
        o_ref[c] = jnp.dot(x, w_ref[:, c * width : (c + 1) * width], preferred_element_type=jnp.float32)


def chunked_matmul(x, w, chunks):
    m, k = x.shape
    n = w.shape[1]
    return pl.pallas_call(
        _chunked_kernel,
        out_shape=jax.ShapeDtypeStruct((chunks, m, n // chunks), jnp.float32),
        in_specs=[_vmem(), _vmem()],
        out_specs=_vmem(),
        cost_estimate=pl.CostEstimate(
            flops=2 * m * k * n, bytes_accessed=2 * (m * k + k * n) + 4 * m * n, transcendentals=0
        ),
    )(x, w)


def gather_mp(block, n_mp):
    me = lax.axis_index("mp")
    pieces = [block] + [
        lax.ppermute(block, "mp", [(i, (i + s) % n_mp) for i in range(n_mp)]) for s in range(1, n_mp)
    ]
    ordered = []
    for c in range(n_mp):
        shift = (me - c) % n_mp
        chosen = pieces[0]
        for s in range(1, n_mp):
            chosen = jnp.where(shift == s, pieces[s], chosen)
        ordered.append(chosen)
    return jnp.concatenate(ordered, axis=-1)


def reduce_scatter_mp(chunks, n_mp):
    me = lax.axis_index("mp")
    total = lax.dynamic_index_in_dim(chunks, me, axis=0, keepdims=False)
    for s in range(1, n_mp):
        outgoing = lax.dynamic_index_in_dim(chunks, (me + s) % n_mp, axis=0, keepdims=False)
        total = total + lax.ppermute(outgoing, "mp", [(i, (i + s) % n_mp) for i in range(n_mp)])
    return total


def seq_masks(n_seq):
    if n_seq == 64:
        return [1, 2, 4, 12, 16, 48]
    return [1 << b for b in range(n_seq.bit_length() - 1)]


def butterfly(value, n_seq, combine, extras=None):
    for index, stride in enumerate(seq_masks(n_seq)):
        partner = lax.ppermute(value, "seq", [(i, i ^ stride) for i in range(n_seq)])
        value = combine(value, partner)
        if index == 0 and extras is not None:
            value, extras = lax.optimization_barrier((value, extras))
    return value, extras


def merge_stats(mine, theirs):
    mix_a, stats_a = mine
    mix_b, stats_b = theirs
    top_a = stats_a[1:]
    top_b = stats_b[1:]
    top = jnp.maximum(top_a, top_b)
    scale_a = jnp.exp(top_a - top)
    scale_b = jnp.exp(top_b - top)
    mix = mix_a * scale_a + mix_b.astype(jnp.float32) * scale_b
    total = stats_a[:1] * scale_a + stats_b[:1] * scale_b
    return mix, jnp.concatenate([total, top], axis=0)


def split_exact(x):
    hi = lax.reduce_precision(x, exponent_bits=8, mantissa_bits=7)
    rest = x - hi
    mid = lax.reduce_precision(rest, exponent_bits=8, mantissa_bits=7)
    lo = rest - mid
    return jnp.concatenate([hi, mid, lo], axis=0).astype(jnp.bfloat16)


def join_exact(parts):
    parts = parts.astype(jnp.float32)
    return parts[0:1] + parts[1:2] + parts[2:3]


def stats_butterfly(mix, stats, n_seq):
    width = mix.shape[0]
    for stride in seq_masks(n_seq):
        pairs = [(i, i ^ stride) for i in range(n_seq)]
        packed = jnp.concatenate(
            [mix.astype(jnp.bfloat16), split_exact(stats[:1]), split_exact(stats[1:])], axis=0
        )
        arrived = lax.ppermute(packed, "seq", pairs)
        theirs = (
            arrived[:width],
            jnp.concatenate(
                [join_exact(arrived[width : width + 3]), join_exact(arrived[width + 3 : width + 6])], axis=0
            ),
        )
        mix, stats = merge_stats((mix, stats), theirs)
    return mix, stats


def shards(
    states,
    norm_gain,
    query_gain,
    key_gain,
    w_query,
    key_matrix,
    value_matrix,
    w_out,
    cached_key_blocks,
    cached_value_blocks,
    req_len,
    slot_request,
    slot_block,
    slot_empty,
    n_seq,
    n_mp,
):
    steps, own_rows, _ = states.shape
    me = lax.axis_index("seq")
    first_row = me * own_rows
    kv_heads = key_matrix.shape[1] // HEAD_SIZE
    q_heads = w_query.shape[1] // HEAD_SIZE
    head_sharing = q_heads // kv_heads
    slot_count, block_len, _ = cached_key_blocks.shape
    requests = req_len.shape[0]
    long_len = n_seq * block_len
    scaling = HEAD_SIZE ** (-0.5)

    wide = gather_mp(states, n_mp).reshape(steps * own_rows, -1)
    own_ids = first_row + jnp.arange(own_rows, dtype=jnp.int32)
    own_len = lax.dynamic_slice_in_dim(req_len, first_row, own_rows)
    positions = (own_len[None, :] + jnp.arange(steps, dtype=jnp.int32)[:, None]).reshape(-1)
    rows = steps * own_rows
    query, keys, values = project_rows(
        wide, norm_gain, query_gain, key_gain, positions, w_query, key_matrix, value_matrix
    )
    query = query.reshape(rows, q_heads, HEAD_SIZE)
    keys = keys.reshape(rows, kv_heads, HEAD_SIZE)
    new_keys = keys.reshape(steps, own_rows, kv_heads * HEAD_SIZE)
    new_values = values.reshape(steps, own_rows, kv_heads * HEAD_SIZE)
    own_query = query.reshape(steps, own_rows, q_heads, HEAD_SIZE).transpose(1, 0, 2, 3)

    request_ids = jnp.arange(requests, dtype=jnp.int32)
    is_long = req_len == long_len
    long_count = is_long.astype(jnp.int32)
    rank = jnp.sum(
        jnp.where(request_ids[None, :] < request_ids[:, None], long_count[None, :], 0), axis=1
    )
    long_ids = jnp.sum(
        jnp.where(
            is_long[None, :] & (rank[None, :] == jnp.arange(LONG_COUNT, dtype=jnp.int32)[:, None]),
            request_ids[None, :],
            0,
        ),
        axis=1,
    )
    own_pick = long_ids[:, None] == own_ids[None, :]
    long_table = jnp.sum(
        jnp.where(own_pick[:, :, None, None, None], own_query[None], jnp.zeros((), jnp.bfloat16)), axis=1
    ).astype(jnp.bfloat16)
    long_table, (slot_request, slot_block, slot_empty, slot_lengths) = butterfly(
        long_table, n_seq, lambda a, b: a + b, (slot_request, slot_block, slot_empty, req_len)
    )

    hit = slot_request[:, None] == request_ids[None, :]
    slot_req_long = jnp.any(hit & is_long[None, :], axis=1)
    slot_rank = jnp.sum(jnp.where(hit, rank[None, :], 0), axis=1)
    slot_len = jnp.sum(jnp.where(hit, slot_lengths[None, :], 0), axis=1)
    local_row = slot_request - first_row
    slot_local = (local_row >= 0) & (local_row < own_rows)
    pick = jnp.where(
        slot_req_long, slot_rank, jnp.where(slot_local, LONG_COUNT + local_row, LONG_COUNT + own_rows)
    )
    candidates = jnp.concatenate(
        [long_table, own_query, jnp.zeros((1,) + own_query.shape[1:], jnp.bfloat16)], axis=0
    )
    slot_query = jnp.take(candidates, pick, axis=0).reshape(
        slot_count, steps, kv_heads, head_sharing, HEAD_SIZE
    )
    keys_split = cached_key_blocks.reshape(slot_count, block_len, kv_heads, HEAD_SIZE)
    values_split = cached_value_blocks.reshape(slot_count, block_len, kv_heads, HEAD_SIZE)
    scores = (
        jnp.einsum("stngd,sknd->stngk", slot_query, keys_split, preferred_element_type=jnp.float32)
        * scaling
    )
    kept = slot_empty == 0
    filled = kept[:, None] & (
        slot_block[:, None] * block_len + jnp.arange(block_len, dtype=jnp.int32)[None, :] < slot_len[:, None]
    )
    filled_wide = filled[:, None, None, None, :]
    slot_top = jnp.max(jnp.where(filled_wide, scores, NEGATIVE), axis=-1)
    same = (slot_request[:, None] == slot_request[None, :]) & kept[None, :]
    reference_top = jnp.max(
        jnp.where(same[:, :, None, None, None], slot_top[None], NEGATIVE), axis=1
    )
    weights = jnp.where(
        filled_wide, jnp.exp(jnp.where(filled_wide, scores - reference_top[..., None], 0.0)), 0.0
    )
    slot_total = jnp.sum(weights, axis=-1)
    slot_mix = jnp.einsum(
        "stngk,sknd->stngd", weights.astype(jnp.bfloat16), values_split, preferred_element_type=jnp.float32
    )

    group_ids = jnp.concatenate([long_ids, own_ids])
    member = (group_ids[:, None] == slot_request[None, :]) & kept[None, :]
    member_float = member.astype(jnp.float32)
    group_top = jnp.max(jnp.where(member[:, :, None, None, None], reference_top[None], NEGATIVE), axis=1)
    group_total = jnp.einsum("qs,stng->qtng", member_float, slot_total, precision=HIGHEST)
    group_mix = jnp.einsum("qs,stngd->qtngd", member_float, slot_mix, precision=HIGHEST)
    stats = jnp.concatenate(
        [group_mix, group_total[..., None], group_top[..., None]], axis=-1
    )
    long_stats = stats[:LONG_COUNT].reshape(-1, HEAD_SIZE + 2).T
    long_mix, long_small = stats_butterfly(long_stats[:HEAD_SIZE], long_stats[HEAD_SIZE:], n_seq)
    long_stats = jnp.concatenate([long_mix, long_small], axis=0)
    long_stats = long_stats.T.reshape((LONG_COUNT,) + stats.shape[1:])
    own_rank = lax.dynamic_slice_in_dim(rank, first_row, own_rows)
    own_is_long = lax.dynamic_slice_in_dim(is_long, first_row, own_rows)
    rank_hit = own_rank[:, None] == jnp.arange(LONG_COUNT, dtype=jnp.int32)[None, :]
    from_long = jnp.sum(
        jnp.where(rank_hit[:, :, None, None, None, None], long_stats[None], 0.0), axis=1
    )
    cache_stats = jnp.where(own_is_long[:, None, None, None, None], from_long, stats[LONG_COUNT:])
    cache_mix = cache_stats[..., :HEAD_SIZE]
    cache_total = cache_stats[..., HEAD_SIZE]
    cache_top = cache_stats[..., HEAD_SIZE + 1]

    heads = own_query.reshape(own_rows, steps, kv_heads, head_sharing, HEAD_SIZE)
    fresh_keys = keys.reshape(steps, own_rows, kv_heads, HEAD_SIZE).transpose(1, 0, 2, 3)
    fresh_values = values.reshape(steps, own_rows, kv_heads, HEAD_SIZE).transpose(1, 0, 2, 3)
    fresh_scores = (
        jnp.einsum("rtngd,rjnd->rtngj", heads, fresh_keys, preferred_element_type=jnp.float32) * scaling
    )
    allowed = (jnp.arange(steps, dtype=jnp.int32)[None, :] <= jnp.arange(steps, dtype=jnp.int32)[:, None])[
        None, :, None, None, :
    ]
    fresh_top = jnp.max(jnp.where(allowed, fresh_scores, NEGATIVE), axis=-1)
    fresh_weights = jnp.where(
        allowed, jnp.exp(jnp.where(allowed, fresh_scores - fresh_top[..., None], 0.0)), 0.0
    )
    fresh_total = jnp.sum(fresh_weights, axis=-1)
    fresh_mix = jnp.einsum(
        "rtngj,rjnd->rtngd",
        fresh_weights.astype(jnp.bfloat16),
        fresh_values,
        preferred_element_type=jnp.float32,
    )
    overall = jnp.maximum(cache_top, fresh_top)
    retained = jnp.exp(cache_top - overall)
    fresh_scale = jnp.exp(fresh_top - overall)
    denominator = cache_total * retained + fresh_total * fresh_scale
    mixture = cache_mix * retained[..., None] + fresh_mix * fresh_scale[..., None]
    attended = (mixture / denominator[..., None]).astype(jnp.bfloat16)
    attended = attended.transpose(1, 0, 2, 3, 4).reshape(steps * own_rows, q_heads * HEAD_SIZE)
    projected = chunked_matmul(attended, w_out, n_mp)
    summed = reduce_scatter_mp(projected, n_mp).reshape(steps, own_rows, -1)
    hidden = (states.astype(jnp.float32) + summed).astype(jnp.bfloat16)
    return hidden, new_keys, new_values


def solution(mesh):
    n_seq = mesh.shape["seq"]
    n_mp = mesh.shape["mp"]
    placed = (
        P(None, "seq", "mp"),
        P(),
        P(),
        P(),
        P(None, "mp"),
        P(None, "mp"),
        P(None, "mp"),
        P("mp", None),
        P("seq", None, "mp"),
        P("seq", None, "mp"),
        P(),
        P("seq"),
        P("seq"),
        P("seq"),
    )

    def body(*args):
        return shards(*args, n_seq=n_seq, n_mp=n_mp)

    return jax.shard_map(
        body,
        mesh=mesh,
        in_specs=placed,
        out_specs=(P(None, "seq", "mp"), P(None, "seq", "mp"), P(None, "seq", "mp")),
        check_vma=False,
    )
```

```python
import jax
import jax.numpy as jnp
from jax import lax
from jax.experimental import pallas as pl
from jax.experimental.pallas import tpu as pltpu
from jax.sharding import PartitionSpec as P

HEAD_SIZE = 128
LONG_COUNT = 12

ROPE_BASE = 1000000.0
NEGATIVE = -1e30
HIGHEST = lax.Precision.HIGHEST


def scaled_rms(values, gain):
    return values * lax.rsqrt(jnp.mean(values * values, axis=-1, keepdims=True) + 1e-06) * gain


def rotate(values, positions):
    halfway = values.shape[-1] // 2
    frequency = ROPE_BASE ** (-(jnp.arange(halfway, dtype=jnp.float32) * 2.0) / values.shape[-1])
    angles = positions.astype(jnp.float32)[..., None, None] * frequency
    cosine = jnp.cos(angles)
    sine_part = jnp.sin(angles)
    leading = values[..., :halfway]
    trailing = values[..., halfway:]
    return jnp.concatenate(
        [leading * cosine - trailing * sine_part, trailing * cosine + leading * sine_part], axis=-1
    )


def _matmul_kernel(x_ref, *refs):
    count = len(refs) // 2
    x = x_ref[...]
    for w_ref, o_ref in zip(refs[:count], refs[count:]):
        o_ref[...] = jnp.dot(x, w_ref[...], preferred_element_type=jnp.float32)


def _project_kernel(x_ref, g_ref, qg_ref, kg_ref, cos_ref, sin_ref, wq_ref, wk_ref, wv_ref, q_ref, k_ref, v_ref):
    x = x_ref[...].astype(jnp.float32)
    scale = lax.rsqrt(jnp.mean(x * x, axis=-1, keepdims=True) + 1e-06)
    normed = (x * scale * g_ref[...]).astype(jnp.bfloat16)
    cosine = cos_ref[...]
    sine = sin_ref[...]

    def norm_rotate(y, gain):
        y = y * lax.rsqrt(jnp.mean(y * y, axis=-1, keepdims=True) + 1e-06) * gain
        return y * cosine + pltpu.roll(y, HEAD_SIZE // 2, 1) * sine

    for w_ref, o_ref, gain_ref in ((wq_ref, q_ref, qg_ref), (wk_ref, k_ref, kg_ref)):
        product = jnp.dot(normed, w_ref[...], preferred_element_type=jnp.float32)
        gain = gain_ref[...]
        for h in range(product.shape[1] // HEAD_SIZE):
            o_ref[:, h * HEAD_SIZE : (h + 1) * HEAD_SIZE] = norm_rotate(
                product[:, h * HEAD_SIZE : (h + 1) * HEAD_SIZE], gain
            ).astype(o_ref.dtype)
    v_ref[...] = jnp.dot(normed, wv_ref[...], preferred_element_type=jnp.float32).astype(v_ref.dtype)


def project_rows(x, gain, query_gain, key_gain, positions, w_query, key_matrix, value_matrix):
    m, k = x.shape
    halfway = HEAD_SIZE // 2
    frequency = ROPE_BASE ** (-(jnp.arange(halfway, dtype=jnp.float32) * 2.0) / HEAD_SIZE)
    angles = positions.astype(jnp.float32)[:, None] * frequency
    cosine = jnp.cos(angles)
    sine = jnp.sin(angles)
    cos_both = jnp.concatenate([cosine, cosine], axis=-1)
    sin_signed = jnp.concatenate([-sine, sine], axis=-1)
    weights = (w_query, key_matrix, value_matrix)
    widths = [w.shape[1] for w in weights]
    return pl.pallas_call(
        _project_kernel,
        out_shape=[jax.ShapeDtypeStruct((m, n), jnp.bfloat16) for n in widths],
        cost_estimate=pl.CostEstimate(
            flops=2 * m * k * sum(widths),
            bytes_accessed=2 * (m * k + k * sum(widths)) + 2 * m * sum(widths),
            transcendentals=m,
        ),
    )(
        x,
        jnp.broadcast_to(gain[None, :], (m, k)),
        query_gain.reshape(1, HEAD_SIZE),
        key_gain.reshape(1, HEAD_SIZE),
        cos_both,
        sin_signed,
        *weights,
    )


def _vmem():
    return pl.BlockSpec(memory_space=pltpu.VMEM)


def small_matmul(x, *weights):
    m, k = x.shape
    widths = [w.shape[1] for w in weights]
    return pl.pallas_call(
        _matmul_kernel,
        out_shape=[jax.ShapeDtypeStruct((m, n), jnp.float32) for n in widths],
        in_specs=[_vmem() for _ in range(1 + len(weights))],
        out_specs=[_vmem() for _ in widths],
        cost_estimate=pl.CostEstimate(
            flops=2 * m * k * sum(widths),
            bytes_accessed=2 * (m * k + k * sum(widths)) + 4 * m * sum(widths),
            transcendentals=0,
        ),
    )(x, *weights)


def _chunked_kernel(x_ref, w_ref, o_ref):
    chunks, _, width = o_ref.shape
    x = x_ref[...]
    for c in range(chunks):
        o_ref[c] = jnp.dot(x, w_ref[:, c * width : (c + 1) * width], preferred_element_type=jnp.float32)


def chunked_matmul(x, w, chunks):
    m, k = x.shape
    n = w.shape[1]
    return pl.pallas_call(
        _chunked_kernel,
        out_shape=jax.ShapeDtypeStruct((chunks, m, n // chunks), jnp.float32),
        in_specs=[_vmem(), _vmem()],
        out_specs=_vmem(),
        cost_estimate=pl.CostEstimate(
            flops=2 * m * k * n, bytes_accessed=2 * (m * k + k * n) + 4 * m * n, transcendentals=0
        ),
    )(x, w)


def gather_mp(block, n_mp):
    me = lax.axis_index("mp")
    pieces = [block] + [
        lax.ppermute(block, "mp", [(i, (i + s) % n_mp) for i in range(n_mp)]) for s in range(1, n_mp)
    ]
    ordered = []
    for c in range(n_mp):
        shift = (me - c) % n_mp
        chosen = pieces[0]
        for s in range(1, n_mp):
            chosen = jnp.where(shift == s, pieces[s], chosen)
        ordered.append(chosen)
    return jnp.concatenate(ordered, axis=-1)


def reduce_scatter_mp(chunks, n_mp, start):
    me = lax.axis_index("mp")
    total = lax.dynamic_index_in_dim(chunks, me, axis=0, keepdims=False) + start
    for s in range(1, n_mp):
        outgoing = lax.dynamic_index_in_dim(chunks, (me + s) % n_mp, axis=0, keepdims=False)
        total = total + lax.ppermute(outgoing, "mp", [(i, (i + s) % n_mp) for i in range(n_mp)])
    return total


def seq_masks(n_seq):
    if n_seq == 64:
        return [1, 2, 4, 12, 16, 48]
    return [1 << b for b in range(n_seq.bit_length() - 1)]


def butterfly(value, n_seq, combine, extras=None):
    for index, stride in enumerate(seq_masks(n_seq)):
        partner = lax.ppermute(value, "seq", [(i, i ^ stride) for i in range(n_seq)])
        value = combine(value, partner)
        if index == 0 and extras is not None:
            value, extras = lax.optimization_barrier((value, extras))
    return value, extras


def merge_stats(mine, theirs):
    mix_a, stats_a = mine
    mix_b, stats_b = theirs
    top_a = stats_a[1:]
    top_b = stats_b[1:]
    top = jnp.maximum(top_a, top_b)
    scale_a = jnp.exp(top_a - top)
    scale_b = jnp.exp(top_b - top)
    mix = mix_a * scale_a + mix_b.astype(jnp.float32) * scale_b
    total = stats_a[:1] * scale_a + stats_b[:1] * scale_b
    return mix, jnp.concatenate([total, top], axis=0)


def split_exact(x):
    hi = lax.reduce_precision(x, exponent_bits=8, mantissa_bits=7)
    rest = x - hi
    mid = lax.reduce_precision(rest, exponent_bits=8, mantissa_bits=7)
    lo = rest - mid
    return jnp.concatenate([hi, mid, lo], axis=0).astype(jnp.bfloat16)


def join_exact(parts):
    parts = parts.astype(jnp.float32)
    return parts[0:1] + parts[1:2] + parts[2:3]


def stats_butterfly(mix, stats, n_seq):
    width = mix.shape[0]
    for stride in seq_masks(n_seq):
        pairs = [(i, i ^ stride) for i in range(n_seq)]
        packed = jnp.concatenate(
            [mix.astype(jnp.bfloat16), split_exact(stats[:1]), split_exact(stats[1:])], axis=0
        )
        arrived = lax.ppermute(packed, "seq", pairs)
        theirs = (
            arrived[:width],
            jnp.concatenate(
                [join_exact(arrived[width : width + 3]), join_exact(arrived[width + 3 : width + 6])], axis=0
            ),
        )
        mix, stats = merge_stats((mix, stats), theirs)
    return mix, stats


def shards(
    states,
    norm_gain,
    query_gain,
    key_gain,
    w_query,
    key_matrix,
    value_matrix,
    w_out,
    cached_key_blocks,
    cached_value_blocks,
    req_len,
    slot_request,
    slot_block,
    slot_empty,
    n_seq,
    n_mp,
):
    steps, own_rows, _ = states.shape
    me = lax.axis_index("seq")
    first_row = me * own_rows
    kv_heads = key_matrix.shape[1] // HEAD_SIZE
    q_heads = w_query.shape[1] // HEAD_SIZE
    head_sharing = q_heads // kv_heads
    slot_count, block_len, _ = cached_key_blocks.shape
    requests = req_len.shape[0]
    long_len = n_seq * block_len
    scaling = HEAD_SIZE ** (-0.5)

    wide = gather_mp(states, n_mp).reshape(steps * own_rows, -1)
    own_ids = first_row + jnp.arange(own_rows, dtype=jnp.int32)
    own_len = lax.dynamic_slice_in_dim(req_len, first_row, own_rows)
    positions = (own_len[None, :] + jnp.arange(steps, dtype=jnp.int32)[:, None]).reshape(-1)
    rows = steps * own_rows
    query, keys, values = project_rows(
        wide, norm_gain, query_gain, key_gain, positions, w_query, key_matrix, value_matrix
    )
    query = query.reshape(rows, q_heads, HEAD_SIZE)
    keys = keys.reshape(rows, kv_heads, HEAD_SIZE)
    new_keys = keys.reshape(steps, own_rows, kv_heads * HEAD_SIZE)
    new_values = values.reshape(steps, own_rows, kv_heads * HEAD_SIZE)
    own_query = query.reshape(steps, own_rows, q_heads, HEAD_SIZE).transpose(1, 0, 2, 3)

    request_ids = jnp.arange(requests, dtype=jnp.int32)
    is_long = req_len == long_len
    long_count = is_long.astype(jnp.int32)
    rank = jnp.sum(
        jnp.where(request_ids[None, :] < request_ids[:, None], long_count[None, :], 0), axis=1
    )
    long_ids = jnp.sum(
        jnp.where(
            is_long[None, :] & (rank[None, :] == jnp.arange(LONG_COUNT, dtype=jnp.int32)[:, None]),
            request_ids[None, :],
            0,
        ),
        axis=1,
    )
    own_pick = long_ids[:, None] == own_ids[None, :]
    long_table = jnp.sum(
        jnp.where(own_pick[:, :, None, None, None], own_query[None], jnp.zeros((), jnp.bfloat16)), axis=1
    ).astype(jnp.bfloat16)
    long_table, (slot_request, slot_block, slot_empty, slot_lengths) = butterfly(
        long_table, n_seq, lambda a, b: a + b, (slot_request, slot_block, slot_empty, req_len)
    )

    hit = slot_request[:, None] == request_ids[None, :]
    slot_req_long = jnp.any(hit & is_long[None, :], axis=1)
    slot_rank = jnp.sum(jnp.where(hit, rank[None, :], 0), axis=1)
    slot_len = jnp.sum(jnp.where(hit, slot_lengths[None, :], 0), axis=1)
    local_row = slot_request - first_row
    slot_local = (local_row >= 0) & (local_row < own_rows)
    pick = jnp.where(
        slot_req_long, slot_rank, jnp.where(slot_local, LONG_COUNT + local_row, LONG_COUNT + own_rows)
    )
    candidates = jnp.concatenate(
        [long_table, own_query, jnp.zeros((1,) + own_query.shape[1:], jnp.bfloat16)], axis=0
    )
    slot_query = jnp.take(candidates, pick, axis=0).reshape(
        slot_count, steps, kv_heads, head_sharing, HEAD_SIZE
    )
    keys_split = cached_key_blocks.reshape(slot_count, block_len, kv_heads, HEAD_SIZE)
    values_split = cached_value_blocks.reshape(slot_count, block_len, kv_heads, HEAD_SIZE)
    scores = (
        jnp.einsum("stngd,sknd->stngk", slot_query, keys_split, preferred_element_type=jnp.float32)
        * scaling
    )
    kept = slot_empty == 0
    filled = kept[:, None] & (
        slot_block[:, None] * block_len + jnp.arange(block_len, dtype=jnp.int32)[None, :] < slot_len[:, None]
    )
    filled_wide = filled[:, None, None, None, :]
    slot_top = jnp.max(jnp.where(filled_wide, scores, NEGATIVE), axis=-1)
    same = (slot_request[:, None] == slot_request[None, :]) & kept[None, :]
    reference_top = jnp.max(
        jnp.where(same[:, :, None, None, None], slot_top[None], NEGATIVE), axis=1
    )
    weights = jnp.where(
        filled_wide, jnp.exp(jnp.where(filled_wide, scores - reference_top[..., None], 0.0)), 0.0
    )
    slot_total = jnp.sum(weights, axis=-1)
    slot_mix = jnp.einsum(
        "stngk,sknd->stngd", weights.astype(jnp.bfloat16), values_split, preferred_element_type=jnp.float32
    )

    group_ids = jnp.concatenate([long_ids, own_ids])
    member = (group_ids[:, None] == slot_request[None, :]) & kept[None, :]
    member_float = member.astype(jnp.float32)
    group_top = jnp.max(jnp.where(member[:, :, None, None, None], reference_top[None], NEGATIVE), axis=1)
    group_total = jnp.einsum("qs,stng->qtng", member_float, slot_total, precision=HIGHEST)
    group_mix = jnp.einsum("qs,stngd->qtngd", member_float, slot_mix, precision=HIGHEST)
    stats = jnp.concatenate(
        [group_mix, group_total[..., None], group_top[..., None]], axis=-1
    )
    long_stats = stats[:LONG_COUNT].reshape(-1, HEAD_SIZE + 2).T
    long_mix, long_small = stats_butterfly(long_stats[:HEAD_SIZE], long_stats[HEAD_SIZE:], n_seq)
    long_stats = jnp.concatenate([long_mix, long_small], axis=0)
    long_stats = long_stats.T.reshape((LONG_COUNT,) + stats.shape[1:])
    own_rank = lax.dynamic_slice_in_dim(rank, first_row, own_rows)
    own_is_long = lax.dynamic_slice_in_dim(is_long, first_row, own_rows)
    rank_hit = own_rank[:, None] == jnp.arange(LONG_COUNT, dtype=jnp.int32)[None, :]
    from_long = jnp.sum(
        jnp.where(rank_hit[:, :, None, None, None, None], long_stats[None], 0.0), axis=1
    )
    cache_stats = jnp.where(own_is_long[:, None, None, None, None], from_long, stats[LONG_COUNT:])
    cache_mix = cache_stats[..., :HEAD_SIZE]
    cache_total = cache_stats[..., HEAD_SIZE]
    cache_top = cache_stats[..., HEAD_SIZE + 1]

    heads = own_query.reshape(own_rows, steps, kv_heads, head_sharing, HEAD_SIZE)
    fresh_keys = keys.reshape(steps, own_rows, kv_heads, HEAD_SIZE).transpose(1, 0, 2, 3)
    fresh_values = values.reshape(steps, own_rows, kv_heads, HEAD_SIZE).transpose(1, 0, 2, 3)
    fresh_scores = (
        jnp.einsum("rtngd,rjnd->rtngj", heads, fresh_keys, preferred_element_type=jnp.float32) * scaling
    )
    allowed = (jnp.arange(steps, dtype=jnp.int32)[None, :] <= jnp.arange(steps, dtype=jnp.int32)[:, None])[
        None, :, None, None, :
    ]
    fresh_top = jnp.max(jnp.where(allowed, fresh_scores, NEGATIVE), axis=-1)
    fresh_weights = jnp.where(
        allowed, jnp.exp(jnp.where(allowed, fresh_scores - fresh_top[..., None], 0.0)), 0.0
    )
    fresh_total = jnp.sum(fresh_weights, axis=-1)
    fresh_mix = jnp.einsum(
        "rtngj,rjnd->rtngd",
        fresh_weights.astype(jnp.bfloat16),
        fresh_values,
        preferred_element_type=jnp.float32,
    )
    overall = jnp.maximum(cache_top, fresh_top)
    retained = jnp.exp(cache_top - overall)
    fresh_scale = jnp.exp(fresh_top - overall)
    denominator = cache_total * retained + fresh_total * fresh_scale
    mixture = cache_mix * retained[..., None] + fresh_mix * fresh_scale[..., None]
    attended = (mixture / denominator[..., None]).astype(jnp.bfloat16)
    attended = attended.transpose(1, 0, 2, 3, 4).reshape(steps * own_rows, q_heads * HEAD_SIZE)
    projected = chunked_matmul(attended, w_out, n_mp)
    own_states = states.astype(jnp.float32).reshape(steps * own_rows, -1)
    summed = reduce_scatter_mp(projected, n_mp, own_states)
    hidden = summed.astype(jnp.bfloat16).reshape(states.shape)
    return hidden, new_keys, new_values


def solution(mesh):
    n_seq = mesh.shape["seq"]
    n_mp = mesh.shape["mp"]
    placed = (
        P(None, "seq", "mp"),
        P(),
        P(),
        P(),
        P(None, "mp"),
        P(None, "mp"),
        P(None, "mp"),
        P("mp", None),
        P("seq", None, "mp"),
        P("seq", None, "mp"),
        P(),
        P("seq"),
        P("seq"),
        P("seq"),
    )

    def body(*args):
        return shards(*args, n_seq=n_seq, n_mp=n_mp)

    return jax.shard_map(
        body,
        mesh=mesh,
        in_specs=placed,
        out_specs=(P(None, "seq", "mp"), P(None, "seq", "mp"), P(None, "seq", "mp")),
        check_vma=False,
    )
```

```python
import jax
import jax.numpy as jnp
from jax import lax
from jax.experimental import pallas as pl
from jax.experimental.pallas import tpu as pltpu
from jax.sharding import PartitionSpec as P

HEAD_SIZE = 128
LONG_COUNT = 12

ROPE_BASE = 1000000.0
NEGATIVE = -1e30
HIGHEST = lax.Precision.HIGHEST


def scaled_rms(values, gain):
    return values * lax.rsqrt(jnp.mean(values * values, axis=-1, keepdims=True) + 1e-06) * gain


def rotate(values, positions):
    halfway = values.shape[-1] // 2
    frequency = ROPE_BASE ** (-(jnp.arange(halfway, dtype=jnp.float32) * 2.0) / values.shape[-1])
    angles = positions.astype(jnp.float32)[..., None, None] * frequency
    cosine = jnp.cos(angles)
    sine_part = jnp.sin(angles)
    leading = values[..., :halfway]
    trailing = values[..., halfway:]
    return jnp.concatenate(
        [leading * cosine - trailing * sine_part, trailing * cosine + leading * sine_part], axis=-1
    )


def _matmul_kernel(x_ref, *refs):
    count = len(refs) // 2
    x = x_ref[...]
    for w_ref, o_ref in zip(refs[:count], refs[count:]):
        o_ref[...] = jnp.dot(x, w_ref[...], preferred_element_type=jnp.float32)


def _project_kernel(x_ref, g_ref, qg_ref, kg_ref, cos_ref, sin_ref, wq_ref, wk_ref, wv_ref, q_ref, k_ref, v_ref):
    x = x_ref[...].astype(jnp.float32)
    scale = lax.rsqrt(jnp.mean(x * x, axis=-1, keepdims=True) + 1e-06)
    normed = (x * scale * g_ref[...]).astype(jnp.bfloat16)
    cosine = cos_ref[...]
    sine = sin_ref[...]

    def norm_rotate(y, gain):
        y = y * lax.rsqrt(jnp.mean(y * y, axis=-1, keepdims=True) + 1e-06) * gain
        return y * cosine + pltpu.roll(y, HEAD_SIZE // 2, 1) * sine

    for w_ref, o_ref, gain_ref in ((wq_ref, q_ref, qg_ref), (wk_ref, k_ref, kg_ref)):
        product = jnp.dot(normed, w_ref[...], preferred_element_type=jnp.float32)
        gain = gain_ref[...]
        for h in range(product.shape[1] // HEAD_SIZE):
            o_ref[:, h * HEAD_SIZE : (h + 1) * HEAD_SIZE] = norm_rotate(
                product[:, h * HEAD_SIZE : (h + 1) * HEAD_SIZE], gain
            ).astype(o_ref.dtype)
    v_ref[...] = jnp.dot(normed, wv_ref[...], preferred_element_type=jnp.float32).astype(v_ref.dtype)


def project_rows(x, gain, query_gain, key_gain, positions, w_query, key_matrix, value_matrix):
    m, k = x.shape
    halfway = HEAD_SIZE // 2
    frequency = ROPE_BASE ** (-(jnp.arange(halfway, dtype=jnp.float32) * 2.0) / HEAD_SIZE)
    angles = positions.astype(jnp.float32)[:, None] * frequency
    cosine = jnp.cos(angles)
    sine = jnp.sin(angles)
    cos_both = jnp.concatenate([cosine, cosine], axis=-1)
    sin_signed = jnp.concatenate([-sine, sine], axis=-1)
    weights = (w_query, key_matrix, value_matrix)
    widths = [w.shape[1] for w in weights]
    return pl.pallas_call(
        _project_kernel,
        out_shape=[jax.ShapeDtypeStruct((m, n), jnp.bfloat16) for n in widths],
        cost_estimate=pl.CostEstimate(
            flops=2 * m * k * sum(widths),
            bytes_accessed=2 * (m * k + k * sum(widths)) + 2 * m * sum(widths),
            transcendentals=m,
        ),
    )(
        x,
        jnp.broadcast_to(gain[None, :], (m, k)),
        query_gain.reshape(1, HEAD_SIZE),
        key_gain.reshape(1, HEAD_SIZE),
        cos_both,
        sin_signed,
        *weights,
    )


def _vmem():
    return pl.BlockSpec(memory_space=pltpu.VMEM)


def small_matmul(x, *weights):
    m, k = x.shape
    widths = [w.shape[1] for w in weights]
    return pl.pallas_call(
        _matmul_kernel,
        out_shape=[jax.ShapeDtypeStruct((m, n), jnp.float32) for n in widths],
        in_specs=[_vmem() for _ in range(1 + len(weights))],
        out_specs=[_vmem() for _ in widths],
        cost_estimate=pl.CostEstimate(
            flops=2 * m * k * sum(widths),
            bytes_accessed=2 * (m * k + k * sum(widths)) + 4 * m * sum(widths),
            transcendentals=0,
        ),
    )(x, *weights)


def _chunked_kernel(x_ref, w_ref, o_ref):
    chunks, _, width = o_ref.shape
    me = lax.axis_index("mp")
    x = x_ref[...]
    products = [
        jnp.dot(x, w_ref[:, c * width : (c + 1) * width], preferred_element_type=jnp.float32)
        for c in range(chunks)
    ]
    for s in range(chunks):
        index = (me + s) % chunks
        chosen = products[0]
        for c in range(1, chunks):
            chosen = jnp.where(index == c, products[c], chosen)
        o_ref[s] = chosen


def chunked_matmul(x, w, chunks):
    m, k = x.shape
    n = w.shape[1]
    return pl.pallas_call(
        _chunked_kernel,
        out_shape=jax.ShapeDtypeStruct((chunks, m, n // chunks), jnp.float32),
        in_specs=[_vmem(), _vmem()],
        out_specs=_vmem(),
        cost_estimate=pl.CostEstimate(
            flops=2 * m * k * n, bytes_accessed=2 * (m * k + k * n) + 4 * m * n, transcendentals=0
        ),
    )(x, w)


def gather_mp(block, n_mp):
    me = lax.axis_index("mp")
    pieces = [block] + [
        lax.ppermute(block, "mp", [(i, (i + s) % n_mp) for i in range(n_mp)]) for s in range(1, n_mp)
    ]
    ordered = []
    for c in range(n_mp):
        shift = (me - c) % n_mp
        chosen = pieces[0]
        for s in range(1, n_mp):
            chosen = jnp.where(shift == s, pieces[s], chosen)
        ordered.append(chosen)
    return jnp.concatenate(ordered, axis=-1)


def reduce_scatter_mp(chunks, n_mp, start):
    total = chunks[0] + start
    for s in range(1, n_mp):
        total = total + lax.ppermute(chunks[s], "mp", [(i, (i + s) % n_mp) for i in range(n_mp)])
    return total


def seq_masks(n_seq):
    if n_seq == 64:
        return [1, 2, 4, 12, 16, 48]
    return [1 << b for b in range(n_seq.bit_length() - 1)]


def butterfly(value, n_seq, combine, extras=None):
    for index, stride in enumerate(seq_masks(n_seq)):
        partner = lax.ppermute(value, "seq", [(i, i ^ stride) for i in range(n_seq)])
        value = combine(value, partner)
        if index == 0 and extras is not None:
            value, extras = lax.optimization_barrier((value, extras))
    return value, extras


def merge_stats(mine, theirs):
    mix_a, stats_a = mine
    mix_b, stats_b = theirs
    top_a = stats_a[1:]
    top_b = stats_b[1:]
    top = jnp.maximum(top_a, top_b)
    scale_a = jnp.exp(top_a - top)
    scale_b = jnp.exp(top_b - top)
    mix = mix_a * scale_a + mix_b.astype(jnp.float32) * scale_b
    total = stats_a[:1] * scale_a + stats_b[:1] * scale_b
    return mix, jnp.concatenate([total, top], axis=0)


def split_exact(x):
    hi = lax.reduce_precision(x, exponent_bits=8, mantissa_bits=7)
    rest = x - hi
    mid = lax.reduce_precision(rest, exponent_bits=8, mantissa_bits=7)
    lo = rest - mid
    return jnp.concatenate([hi, mid, lo], axis=0).astype(jnp.bfloat16)


def join_exact(parts):
    parts = parts.astype(jnp.float32)
    return parts[0:1] + parts[1:2] + parts[2:3]


def stats_butterfly(mix, stats, n_seq):
    width = mix.shape[0]
    for stride in seq_masks(n_seq):
        pairs = [(i, i ^ stride) for i in range(n_seq)]
        packed = jnp.concatenate(
            [mix.astype(jnp.bfloat16), split_exact(stats[:1]), split_exact(stats[1:])], axis=0
        )
        arrived = lax.ppermute(packed, "seq", pairs)
        theirs = (
            arrived[:width],
            jnp.concatenate(
                [join_exact(arrived[width : width + 3]), join_exact(arrived[width + 3 : width + 6])], axis=0
            ),
        )
        mix, stats = merge_stats((mix, stats), theirs)
    return mix, stats


def shards(
    states,
    norm_gain,
    query_gain,
    key_gain,
    w_query,
    key_matrix,
    value_matrix,
    w_out,
    cached_key_blocks,
    cached_value_blocks,
    req_len,
    slot_request,
    slot_block,
    slot_empty,
    n_seq,
    n_mp,
):
    steps, own_rows, _ = states.shape
    me = lax.axis_index("seq")
    first_row = me * own_rows
    kv_heads = key_matrix.shape[1] // HEAD_SIZE
    q_heads = w_query.shape[1] // HEAD_SIZE
    head_sharing = q_heads // kv_heads
    slot_count, block_len, _ = cached_key_blocks.shape
    requests = req_len.shape[0]
    long_len = n_seq * block_len
    scaling = HEAD_SIZE ** (-0.5)

    wide = gather_mp(states, n_mp).reshape(steps * own_rows, -1)
    own_ids = first_row + jnp.arange(own_rows, dtype=jnp.int32)
    own_len = lax.dynamic_slice_in_dim(req_len, first_row, own_rows)
    positions = (own_len[None, :] + jnp.arange(steps, dtype=jnp.int32)[:, None]).reshape(-1)
    rows = steps * own_rows
    query, keys, values = project_rows(
        wide, norm_gain, query_gain, key_gain, positions, w_query, key_matrix, value_matrix
    )
    query = query.reshape(rows, q_heads, HEAD_SIZE)
    keys = keys.reshape(rows, kv_heads, HEAD_SIZE)
    new_keys = keys.reshape(steps, own_rows, kv_heads * HEAD_SIZE)
    new_values = values.reshape(steps, own_rows, kv_heads * HEAD_SIZE)
    own_query = query.reshape(steps, own_rows, q_heads, HEAD_SIZE).transpose(1, 0, 2, 3)

    request_ids = jnp.arange(requests, dtype=jnp.int32)
    is_long = req_len == long_len
    long_count = is_long.astype(jnp.int32)
    rank = jnp.sum(
        jnp.where(request_ids[None, :] < request_ids[:, None], long_count[None, :], 0), axis=1
    )
    long_ids = jnp.sum(
        jnp.where(
            is_long[None, :] & (rank[None, :] == jnp.arange(LONG_COUNT, dtype=jnp.int32)[:, None]),
            request_ids[None, :],
            0,
        ),
        axis=1,
    )
    own_pick = long_ids[:, None] == own_ids[None, :]
    long_table = jnp.sum(
        jnp.where(own_pick[:, :, None, None, None], own_query[None], jnp.zeros((), jnp.bfloat16)), axis=1
    ).astype(jnp.bfloat16)
    long_table, (slot_request, slot_block, slot_empty, slot_lengths) = butterfly(
        long_table, n_seq, lambda a, b: a + b, (slot_request, slot_block, slot_empty, req_len)
    )

    hit = slot_request[:, None] == request_ids[None, :]
    slot_req_long = jnp.any(hit & is_long[None, :], axis=1)
    slot_rank = jnp.sum(jnp.where(hit, rank[None, :], 0), axis=1)
    slot_len = jnp.sum(jnp.where(hit, slot_lengths[None, :], 0), axis=1)
    local_row = slot_request - first_row
    slot_local = (local_row >= 0) & (local_row < own_rows)
    pick = jnp.where(
        slot_req_long, slot_rank, jnp.where(slot_local, LONG_COUNT + local_row, LONG_COUNT + own_rows)
    )
    candidates = jnp.concatenate(
        [long_table, own_query, jnp.zeros((1,) + own_query.shape[1:], jnp.bfloat16)], axis=0
    )
    slot_query = jnp.take(candidates, pick, axis=0).reshape(
        slot_count, steps, kv_heads, head_sharing, HEAD_SIZE
    )
    keys_split = cached_key_blocks.reshape(slot_count, block_len, kv_heads, HEAD_SIZE)
    values_split = cached_value_blocks.reshape(slot_count, block_len, kv_heads, HEAD_SIZE)
    scores = (
        jnp.einsum("stngd,sknd->stngk", slot_query, keys_split, preferred_element_type=jnp.float32)
        * scaling
    )
    kept = slot_empty == 0
    filled = kept[:, None] & (
        slot_block[:, None] * block_len + jnp.arange(block_len, dtype=jnp.int32)[None, :] < slot_len[:, None]
    )
    filled_wide = filled[:, None, None, None, :]
    slot_top = jnp.max(jnp.where(filled_wide, scores, NEGATIVE), axis=-1)
    same = (slot_request[:, None] == slot_request[None, :]) & kept[None, :]
    reference_top = jnp.max(
        jnp.where(same[:, :, None, None, None], slot_top[None], NEGATIVE), axis=1
    )
    weights = jnp.where(
        filled_wide, jnp.exp(jnp.where(filled_wide, scores - reference_top[..., None], 0.0)), 0.0
    )
    slot_total = jnp.sum(weights, axis=-1)
    slot_mix = jnp.einsum(
        "stngk,sknd->stngd", weights.astype(jnp.bfloat16), values_split, preferred_element_type=jnp.float32
    )

    group_ids = jnp.concatenate([long_ids, own_ids])
    member = (group_ids[:, None] == slot_request[None, :]) & kept[None, :]
    member_float = member.astype(jnp.float32)
    group_top = jnp.max(jnp.where(member[:, :, None, None, None], reference_top[None], NEGATIVE), axis=1)
    group_total = jnp.einsum("qs,stng->qtng", member_float, slot_total, precision=HIGHEST)
    group_mix = jnp.einsum("qs,stngd->qtngd", member_float, slot_mix, precision=HIGHEST)
    stats = jnp.concatenate(
        [group_mix, group_total[..., None], group_top[..., None]], axis=-1
    )
    long_stats = stats[:LONG_COUNT].reshape(-1, HEAD_SIZE + 2).T
    long_mix, long_small = stats_butterfly(long_stats[:HEAD_SIZE], long_stats[HEAD_SIZE:], n_seq)
    long_stats = jnp.concatenate([long_mix, long_small], axis=0)
    long_stats = long_stats.T.reshape((LONG_COUNT,) + stats.shape[1:])
    own_rank = lax.dynamic_slice_in_dim(rank, first_row, own_rows)
    own_is_long = lax.dynamic_slice_in_dim(is_long, first_row, own_rows)
    rank_hit = own_rank[:, None] == jnp.arange(LONG_COUNT, dtype=jnp.int32)[None, :]
    from_long = jnp.sum(
        jnp.where(rank_hit[:, :, None, None, None, None], long_stats[None], 0.0), axis=1
    )
    cache_stats = jnp.where(own_is_long[:, None, None, None, None], from_long, stats[LONG_COUNT:])
    cache_mix = cache_stats[..., :HEAD_SIZE]
    cache_total = cache_stats[..., HEAD_SIZE]
    cache_top = cache_stats[..., HEAD_SIZE + 1]

    heads = own_query.reshape(own_rows, steps, kv_heads, head_sharing, HEAD_SIZE)
    fresh_keys = keys.reshape(steps, own_rows, kv_heads, HEAD_SIZE).transpose(1, 0, 2, 3)
    fresh_values = values.reshape(steps, own_rows, kv_heads, HEAD_SIZE).transpose(1, 0, 2, 3)
    fresh_scores = (
        jnp.einsum("rtngd,rjnd->rtngj", heads, fresh_keys, preferred_element_type=jnp.float32) * scaling
    )
    allowed = (jnp.arange(steps, dtype=jnp.int32)[None, :] <= jnp.arange(steps, dtype=jnp.int32)[:, None])[
        None, :, None, None, :
    ]
    fresh_top = jnp.max(jnp.where(allowed, fresh_scores, NEGATIVE), axis=-1)
    fresh_weights = jnp.where(
        allowed, jnp.exp(jnp.where(allowed, fresh_scores - fresh_top[..., None], 0.0)), 0.0
    )
    fresh_total = jnp.sum(fresh_weights, axis=-1)
    fresh_mix = jnp.einsum(
        "rtngj,rjnd->rtngd",
        fresh_weights.astype(jnp.bfloat16),
        fresh_values,
        preferred_element_type=jnp.float32,
    )
    overall = jnp.maximum(cache_top, fresh_top)
    retained = jnp.exp(cache_top - overall)
    fresh_scale = jnp.exp(fresh_top - overall)
    denominator = cache_total * retained + fresh_total * fresh_scale
    mixture = cache_mix * retained[..., None] + fresh_mix * fresh_scale[..., None]
    attended = (mixture / denominator[..., None]).astype(jnp.bfloat16)
    attended = attended.transpose(1, 0, 2, 3, 4).reshape(steps * own_rows, q_heads * HEAD_SIZE)
    projected = chunked_matmul(attended, w_out, n_mp)
    own_states = states.astype(jnp.float32).reshape(steps * own_rows, -1)
    summed = reduce_scatter_mp(projected, n_mp, own_states)
    hidden = summed.astype(jnp.bfloat16).reshape(states.shape)
    return hidden, new_keys, new_values


def solution(mesh):
    n_seq = mesh.shape["seq"]
    n_mp = mesh.shape["mp"]
    placed = (
        P(None, "seq", "mp"),
        P(),
        P(),
        P(),
        P(None, "mp"),
        P(None, "mp"),
        P(None, "mp"),
        P("mp", None),
        P("seq", None, "mp"),
        P("seq", None, "mp"),
        P(),
        P("seq"),
        P("seq"),
        P("seq"),
    )

    def body(*args):
        return shards(*args, n_seq=n_seq, n_mp=n_mp)

    return jax.shard_map(
        body,
        mesh=mesh,
        in_specs=placed,
        out_specs=(P(None, "seq", "mp"), P(None, "seq", "mp"), P(None, "seq", "mp")),
        check_vma=False,
    )
```

```python
import jax
import jax.numpy as jnp
from jax import lax
from jax.experimental import pallas as pl
from jax.experimental.pallas import tpu as pltpu
from jax.sharding import PartitionSpec as P

HEAD_SIZE = 128
LONG_COUNT = 12

ROPE_BASE = 1000000.0
NEGATIVE = -1e30
HIGHEST = lax.Precision.HIGHEST


def scaled_rms(values, gain):
    return values * lax.rsqrt(jnp.mean(values * values, axis=-1, keepdims=True) + 1e-06) * gain


def rotate(values, positions):
    halfway = values.shape[-1] // 2
    frequency = ROPE_BASE ** (-(jnp.arange(halfway, dtype=jnp.float32) * 2.0) / values.shape[-1])
    angles = positions.astype(jnp.float32)[..., None, None] * frequency
    cosine = jnp.cos(angles)
    sine_part = jnp.sin(angles)
    leading = values[..., :halfway]
    trailing = values[..., halfway:]
    return jnp.concatenate(
        [leading * cosine - trailing * sine_part, trailing * cosine + leading * sine_part], axis=-1
    )


def _matmul_kernel(x_ref, *refs):
    count = len(refs) // 2
    x = x_ref[...]
    for w_ref, o_ref in zip(refs[:count], refs[count:]):
        o_ref[...] = jnp.dot(x, w_ref[...], preferred_element_type=jnp.float32)


def _project_kernel(x_ref, g_ref, qg_ref, kg_ref, cos_ref, sin_ref, wq_ref, wk_ref, wv_ref, q_ref, k_ref, v_ref):
    x = x_ref[...].astype(jnp.float32)
    scale = lax.rsqrt(jnp.mean(x * x, axis=-1, keepdims=True) + 1e-06)
    normed = (x * scale * g_ref[...]).astype(jnp.bfloat16)
    cosine = cos_ref[...]
    sine = sin_ref[...]

    def norm_rotate(y, gain):
        y = y * lax.rsqrt(jnp.mean(y * y, axis=-1, keepdims=True) + 1e-06) * gain
        return y * cosine + pltpu.roll(y, HEAD_SIZE // 2, 1) * sine

    for w_ref, o_ref, gain_ref in ((wq_ref, q_ref, qg_ref), (wk_ref, k_ref, kg_ref)):
        product = jnp.dot(normed, w_ref[...], preferred_element_type=jnp.float32)
        gain = gain_ref[...]
        for h in range(product.shape[1] // HEAD_SIZE):
            o_ref[:, h * HEAD_SIZE : (h + 1) * HEAD_SIZE] = norm_rotate(
                product[:, h * HEAD_SIZE : (h + 1) * HEAD_SIZE], gain
            ).astype(o_ref.dtype)
    v_ref[...] = jnp.dot(normed, wv_ref[...], preferred_element_type=jnp.float32).astype(v_ref.dtype)


def project_rows(x, gain, query_gain, key_gain, positions, w_query, key_matrix, value_matrix):
    m, k = x.shape
    halfway = HEAD_SIZE // 2
    frequency = ROPE_BASE ** (-(jnp.arange(halfway, dtype=jnp.float32) * 2.0) / HEAD_SIZE)
    angles = positions.astype(jnp.float32)[:, None] * frequency
    cosine = jnp.cos(angles)
    sine = jnp.sin(angles)
    cos_both = jnp.concatenate([cosine, cosine], axis=-1)
    sin_signed = jnp.concatenate([-sine, sine], axis=-1)
    weights = (w_query, key_matrix, value_matrix)
    widths = [w.shape[1] for w in weights]
    return pl.pallas_call(
        _project_kernel,
        out_shape=[jax.ShapeDtypeStruct((m, n), jnp.bfloat16) for n in widths],
        cost_estimate=pl.CostEstimate(
            flops=2 * m * k * sum(widths),
            bytes_accessed=2 * (m * k + k * sum(widths)) + 2 * m * sum(widths),
            transcendentals=m,
        ),
    )(
        x,
        jnp.broadcast_to(gain[None, :], (m, k)),
        jnp.broadcast_to(query_gain[None, :], (m, HEAD_SIZE)),
        jnp.broadcast_to(key_gain[None, :], (m, HEAD_SIZE)),
        cos_both,
        sin_signed,
        *weights,
    )


def _vmem():
    return pl.BlockSpec(memory_space=pltpu.VMEM)


def small_matmul(x, *weights):
    m, k = x.shape
    widths = [w.shape[1] for w in weights]
    return pl.pallas_call(
        _matmul_kernel,
        out_shape=[jax.ShapeDtypeStruct((m, n), jnp.float32) for n in widths],
        in_specs=[_vmem() for _ in range(1 + len(weights))],
        out_specs=[_vmem() for _ in widths],
        cost_estimate=pl.CostEstimate(
            flops=2 * m * k * sum(widths),
            bytes_accessed=2 * (m * k + k * sum(widths)) + 4 * m * sum(widths),
            transcendentals=0,
        ),
    )(x, *weights)


def _chunked_kernel(x_ref, w_ref, o_ref):
    chunks, _, width = o_ref.shape
    me = lax.axis_index("mp")
    x = x_ref[...]
    products = [
        jnp.dot(x, w_ref[:, c * width : (c + 1) * width], preferred_element_type=jnp.float32)
        for c in range(chunks)
    ]
    for s in range(chunks):
        index = (me + s) % chunks
        chosen = products[0]
        for c in range(1, chunks):
            chosen = jnp.where(index == c, products[c], chosen)
        o_ref[s] = chosen


def chunked_matmul(x, w, chunks):
    m, k = x.shape
    n = w.shape[1]
    return pl.pallas_call(
        _chunked_kernel,
        out_shape=jax.ShapeDtypeStruct((chunks, m, n // chunks), jnp.float32),
        in_specs=[_vmem(), _vmem()],
        out_specs=_vmem(),
        cost_estimate=pl.CostEstimate(
            flops=2 * m * k * n, bytes_accessed=2 * (m * k + k * n) + 4 * m * n, transcendentals=0
        ),
    )(x, w)


def gather_mp(block, n_mp):
    me = lax.axis_index("mp")
    pieces = [block] + [
        lax.ppermute(block, "mp", [(i, (i + s) % n_mp) for i in range(n_mp)]) for s in range(1, n_mp)
    ]
    ordered = []
    for c in range(n_mp):
        shift = (me - c) % n_mp
        chosen = pieces[0]
        for s in range(1, n_mp):
            chosen = jnp.where(shift == s, pieces[s], chosen)
        ordered.append(chosen)
    return jnp.concatenate(ordered, axis=-1)


def reduce_scatter_mp(chunks, n_mp, start):
    total = chunks[0] + start
    for s in range(1, n_mp):
        total = total + lax.ppermute(chunks[s], "mp", [(i, (i + s) % n_mp) for i in range(n_mp)])
    return total


def seq_masks(n_seq):
    if n_seq == 64:
        return [1, 2, 4, 12, 16, 48]
    return [1 << b for b in range(n_seq.bit_length() - 1)]


def butterfly(value, n_seq, combine, extras=None):
    for index, stride in enumerate(seq_masks(n_seq)):
        partner = lax.ppermute(value, "seq", [(i, i ^ stride) for i in range(n_seq)])
        value = combine(value, partner)
        if index == 0 and extras is not None:
            value, extras = lax.optimization_barrier((value, extras))
    return value, extras


def merge_stats(mine, theirs):
    mix_a, stats_a = mine
    mix_b, stats_b = theirs
    top_a = stats_a[1:]
    top_b = stats_b[1:]
    top = jnp.maximum(top_a, top_b)
    scale_a = jnp.exp(top_a - top)
    scale_b = jnp.exp(top_b - top)
    mix = mix_a * scale_a + mix_b.astype(jnp.float32) * scale_b
    total = stats_a[:1] * scale_a + stats_b[:1] * scale_b
    return mix, jnp.concatenate([total, top], axis=0)


def split_exact(x):
    hi = lax.reduce_precision(x, exponent_bits=8, mantissa_bits=7)
    rest = x - hi
    mid = lax.reduce_precision(rest, exponent_bits=8, mantissa_bits=7)
    lo = rest - mid
    return jnp.concatenate([hi, mid, lo], axis=0).astype(jnp.bfloat16)


def join_exact(parts):
    parts = parts.astype(jnp.float32)
    return parts[0:1] + parts[1:2] + parts[2:3]


def stats_butterfly(mix, stats, n_seq):
    width = mix.shape[0]
    for stride in seq_masks(n_seq):
        pairs = [(i, i ^ stride) for i in range(n_seq)]
        packed = jnp.concatenate(
            [mix.astype(jnp.bfloat16), split_exact(stats[:1]), split_exact(stats[1:])], axis=0
        )
        arrived = lax.ppermute(packed, "seq", pairs)
        theirs = (
            arrived[:width],
            jnp.concatenate(
                [join_exact(arrived[width : width + 3]), join_exact(arrived[width + 3 : width + 6])], axis=0
            ),
        )
        mix, stats = merge_stats((mix, stats), theirs)
    return mix, stats


def shards(
    states,
    norm_gain,
    query_gain,
    key_gain,
    w_query,
    key_matrix,
    value_matrix,
    w_out,
    cached_key_blocks,
    cached_value_blocks,
    req_len,
    slot_request,
    slot_block,
    slot_empty,
    n_seq,
    n_mp,
):
    steps, own_rows, _ = states.shape
    me = lax.axis_index("seq")
    first_row = me * own_rows
    kv_heads = key_matrix.shape[1] // HEAD_SIZE
    q_heads = w_query.shape[1] // HEAD_SIZE
    head_sharing = q_heads // kv_heads
    slot_count, block_len, _ = cached_key_blocks.shape
    requests = req_len.shape[0]
    long_len = n_seq * block_len
    scaling = HEAD_SIZE ** (-0.5)

    wide = gather_mp(states, n_mp).reshape(steps * own_rows, -1)
    own_ids = first_row + jnp.arange(own_rows, dtype=jnp.int32)
    own_len = lax.dynamic_slice_in_dim(req_len, first_row, own_rows)
    positions = (own_len[None, :] + jnp.arange(steps, dtype=jnp.int32)[:, None]).reshape(-1)
    rows = steps * own_rows
    query, keys, values = project_rows(
        wide, norm_gain, query_gain, key_gain, positions, w_query, key_matrix, value_matrix
    )
    query = query.reshape(rows, q_heads, HEAD_SIZE)
    keys = keys.reshape(rows, kv_heads, HEAD_SIZE)
    new_keys = keys.reshape(steps, own_rows, kv_heads * HEAD_SIZE)
    new_values = values.reshape(steps, own_rows, kv_heads * HEAD_SIZE)
    own_query = query.reshape(steps, own_rows, q_heads, HEAD_SIZE).transpose(1, 0, 2, 3)

    request_ids = jnp.arange(requests, dtype=jnp.int32)
    is_long = req_len == long_len
    long_count = is_long.astype(jnp.int32)
    rank = jnp.sum(
        jnp.where(request_ids[None, :] < request_ids[:, None], long_count[None, :], 0), axis=1
    )
    long_ids = jnp.sum(
        jnp.where(
            is_long[None, :] & (rank[None, :] == jnp.arange(LONG_COUNT, dtype=jnp.int32)[:, None]),
            request_ids[None, :],
            0,
        ),
        axis=1,
    )
    own_pick = long_ids[:, None] == own_ids[None, :]
    long_table = jnp.sum(
        jnp.where(own_pick[:, :, None, None, None], own_query[None], jnp.zeros((), jnp.bfloat16)), axis=1
    ).astype(jnp.bfloat16)
    long_table, (slot_request, slot_block, slot_empty, slot_lengths) = butterfly(
        long_table, n_seq, lambda a, b: a + b, (slot_request, slot_block, slot_empty, req_len)
    )

    hit = slot_request[:, None] == request_ids[None, :]
    slot_req_long = jnp.any(hit & is_long[None, :], axis=1)
    slot_rank = jnp.sum(jnp.where(hit, rank[None, :], 0), axis=1)
    slot_len = jnp.sum(jnp.where(hit, slot_lengths[None, :], 0), axis=1)
    local_row = slot_request - first_row
    slot_local = (local_row >= 0) & (local_row < own_rows)
    pick = jnp.where(
        slot_req_long, slot_rank, jnp.where(slot_local, LONG_COUNT + local_row, LONG_COUNT + own_rows)
    )
    candidates = jnp.concatenate(
        [long_table, own_query, jnp.zeros((1,) + own_query.shape[1:], jnp.bfloat16)], axis=0
    )
    slot_query = jnp.take(candidates, pick, axis=0).reshape(
        slot_count, steps, kv_heads, head_sharing, HEAD_SIZE
    )
    keys_split = cached_key_blocks.reshape(slot_count, block_len, kv_heads, HEAD_SIZE)
    values_split = cached_value_blocks.reshape(slot_count, block_len, kv_heads, HEAD_SIZE)
    scores = (
        jnp.einsum("stngd,sknd->stngk", slot_query, keys_split, preferred_element_type=jnp.float32)
        * scaling
    )
    kept = slot_empty == 0
    filled = kept[:, None] & (
        slot_block[:, None] * block_len + jnp.arange(block_len, dtype=jnp.int32)[None, :] < slot_len[:, None]
    )
    filled_wide = filled[:, None, None, None, :]
    slot_top = jnp.max(jnp.where(filled_wide, scores, NEGATIVE), axis=-1)
    same = (slot_request[:, None] == slot_request[None, :]) & kept[None, :]
    reference_top = jnp.max(
        jnp.where(same[:, :, None, None, None], slot_top[None], NEGATIVE), axis=1
    )
    weights = jnp.where(
        filled_wide, jnp.exp(jnp.where(filled_wide, scores - reference_top[..., None], 0.0)), 0.0
    )
    slot_total = jnp.sum(weights, axis=-1)
    slot_mix = jnp.einsum(
        "stngk,sknd->stngd", weights.astype(jnp.bfloat16), values_split, preferred_element_type=jnp.float32
    )

    group_ids = jnp.concatenate([long_ids, own_ids])
    member = (group_ids[:, None] == slot_request[None, :]) & kept[None, :]
    member_float = member.astype(jnp.float32)
    group_top = jnp.max(jnp.where(member[:, :, None, None, None], reference_top[None], NEGATIVE), axis=1)
    group_total = jnp.einsum("qs,stng->qtng", member_float, slot_total, precision=HIGHEST)
    group_mix = jnp.einsum("qs,stngd->qtngd", member_float, slot_mix, precision=HIGHEST)
    stats = jnp.concatenate(
        [group_mix, group_total[..., None], group_top[..., None]], axis=-1
    )
    long_stats = stats[:LONG_COUNT].reshape(-1, HEAD_SIZE + 2).T
    long_mix, long_small = stats_butterfly(long_stats[:HEAD_SIZE], long_stats[HEAD_SIZE:], n_seq)
    long_stats = jnp.concatenate([long_mix, long_small], axis=0)
    long_stats = long_stats.T.reshape((LONG_COUNT,) + stats.shape[1:])
    own_rank = lax.dynamic_slice_in_dim(rank, first_row, own_rows)
    own_is_long = lax.dynamic_slice_in_dim(is_long, first_row, own_rows)
    rank_hit = own_rank[:, None] == jnp.arange(LONG_COUNT, dtype=jnp.int32)[None, :]
    from_long = jnp.sum(
        jnp.where(rank_hit[:, :, None, None, None, None], long_stats[None], 0.0), axis=1
    )
    cache_stats = jnp.where(own_is_long[:, None, None, None, None], from_long, stats[LONG_COUNT:])
    cache_mix = cache_stats[..., :HEAD_SIZE]
    cache_total = cache_stats[..., HEAD_SIZE]
    cache_top = cache_stats[..., HEAD_SIZE + 1]

    heads = own_query.reshape(own_rows, steps, kv_heads, head_sharing, HEAD_SIZE)
    fresh_keys = keys.reshape(steps, own_rows, kv_heads, HEAD_SIZE).transpose(1, 0, 2, 3)
    fresh_values = values.reshape(steps, own_rows, kv_heads, HEAD_SIZE).transpose(1, 0, 2, 3)
    fresh_scores = (
        jnp.einsum("rtngd,rjnd->rtngj", heads, fresh_keys, preferred_element_type=jnp.float32) * scaling
    )
    allowed = (jnp.arange(steps, dtype=jnp.int32)[None, :] <= jnp.arange(steps, dtype=jnp.int32)[:, None])[
        None, :, None, None, :
    ]
    fresh_top = jnp.max(jnp.where(allowed, fresh_scores, NEGATIVE), axis=-1)
    fresh_weights = jnp.where(
        allowed, jnp.exp(jnp.where(allowed, fresh_scores - fresh_top[..., None], 0.0)), 0.0
    )
    fresh_total = jnp.sum(fresh_weights, axis=-1)
    fresh_mix = jnp.einsum(
        "rtngj,rjnd->rtngd",
        fresh_weights.astype(jnp.bfloat16),
        fresh_values,
        preferred_element_type=jnp.float32,
    )
    overall = jnp.maximum(cache_top, fresh_top)
    retained = jnp.exp(cache_top - overall)
    fresh_scale = jnp.exp(fresh_top - overall)
    denominator = cache_total * retained + fresh_total * fresh_scale
    mixture = cache_mix * retained[..., None] + fresh_mix * fresh_scale[..., None]
    attended = (mixture / denominator[..., None]).astype(jnp.bfloat16)
    attended = attended.transpose(1, 0, 2, 3, 4).reshape(steps * own_rows, q_heads * HEAD_SIZE)
    projected = chunked_matmul(attended, w_out, n_mp)
    own_states = states.astype(jnp.float32).reshape(steps * own_rows, -1)
    summed = reduce_scatter_mp(projected, n_mp, own_states)
    hidden = summed.astype(jnp.bfloat16).reshape(states.shape)
    return hidden, new_keys, new_values


def solution(mesh):
    n_seq = mesh.shape["seq"]
    n_mp = mesh.shape["mp"]
    placed = (
        P(None, "seq", "mp"),
        P(),
        P(),
        P(),
        P(None, "mp"),
        P(None, "mp"),
        P(None, "mp"),
        P("mp", None),
        P("seq", None, "mp"),
        P("seq", None, "mp"),
        P(),
        P("seq"),
        P("seq"),
        P("seq"),
    )

    def body(*args):
        return shards(*args, n_seq=n_seq, n_mp=n_mp)

    return jax.shard_map(
        body,
        mesh=mesh,
        in_specs=placed,
        out_specs=(P(None, "seq", "mp"), P(None, "seq", "mp"), P(None, "seq", "mp")),
        check_vma=False,
    )
```
